256 devices in a mesh: wall: 8 (over y_lo, x), stream: 32 (over z, y_hi, core).
Axes of the slice: x: 4, y: 4 (y_hi: 2, y_lo: 2; y = y_hi * 2 + y_lo), z: 8, core: 2. Of those that a mesh axis runs over, the one named last changes fastest.
Arguments:
- velocity: float32 [3, 64, 512, 128], P(None, 'wall', 'stream'), may hold values from -6 to 6
- sample_block: int32 [8, 256], P('wall', 'stream'), may hold values from 0 to 127
- sample_member: int32 [8, 256, 1], P('wall', 'stream'), may hold values from 0 to 7; in each aligned block of 8 rows (0 to 7, 8 to 15, ..., all dimensions but the last counted through in order) at most 2 rows name the same one
- k_first: bfloat16 [8, 54, 64], P('wall'), may hold values from -6 to 6
- k_second: bfloat16 [8, 27, 64, 64], P('wall'), may hold values from -6 to 6
- w_hidden: bfloat16 [8, 2048, 2048], P('wall'), may hold values from -6 to 6
- w_out: bfloat16 [8, 2048, 2], P('wall'), may hold values from -6 to 6
Outputs:
- new_field: float32 [3, 64, 512, 128], P(None, 'wall', 'stream')
- stress: float32 [2, 8, 256], P(None, 'wall', 'stream')
- new_k_first: float32 [8, 54, 64], P('wall')
- new_k_second: float32 [8, 27, 64, 64], P('wall')
- new_w_hidden: float32 [8, 2048, 2048], P('wall', 'stream')
- new_w_out: float32 [8, 2048, 2], P('wall')
The draws below stay inside these ranges and needn't reach their ends.
Inputs may be any that keep to these rules, and one draw needn't show every extreme that they name: `sample_block`: A block of the slab's own points, numbered as in the reference program. `sample_member`: in the list of one slab at most 2 samples name the same member; in every draw some slab names some member exactly 2 times.
All inputs are finite; a program needn't handle non-finite values.
Results may differ from the reference program's by a relative error of at most 0.0064.
Values may be sent and summed in bfloat16 or wider, within the bound.
No kernel may reach another device: no remote copies, remote signals or barrier semaphores. Data moves between devices by JAX's collectives and lax.ppermute only.
A program may use at most 128 MiB of HBM per device.

```python
import math
import jax
import jax.numpy as jnp
import numpy as np
from jax import lax

P_SIZE = 8
EY = 1
EX = 2
PY = 4
PX = 4
PZ = 8
CH = 64
HID = 2048
CAP = 2
SAMPLES = 8
NBLK = 128
FEAT_IN = 256
FEATS = 2048
NY = 64
NX = 512
NZ = 128
MEMBERS = 8
N_WALL = 8
N_STREAM = 32


def place_ends(values, key, smallest, largest):
    spot = [jax.random.randint(jax.random.fold_in(key, axis), (), 0, length) for axis, length in enumerate(values.shape)]
    widest = values.shape.index(max(values.shape))
    beside = spot[:widest] + [(spot[widest] + 1) % values.shape[widest]] + spot[widest + 1:]
    return values.at[tuple(spot)].set(smallest).at[tuple(beside)].set(largest)


def levels(own_key, extent, shards, low, top_value):
    def one(dim, blocks):
        heights = jax.random.uniform(jax.random.fold_in(jax.random.fold_in(own_key, 6), dim), (blocks,), jnp.float32, low / len(shards), top_value / len(shards))
        return jnp.repeat(jnp.exp(heights), extent[dim] // blocks).reshape((-1,) + (1,) * (len(extent) - dim - 1))

    level = one(*shards[0])
    for cut in shards[1:]:
        level = level * one(*cut)
    return level


def shared_out(rng, own, number, rows, count, top, reach, skew):
    order = jax.random.permutation(rng, count)
    packed, usual = shares(count, rows * top, reach, skew, True), shares(count, rows * top, reach, skew, False)
    places = jnp.arange(count)

    def named(lengths, turn):
        used = int((lengths > 0).sum())
        fixed = max(1, used // 4)
        moved = fixed + (places - fixed + turn * (used - fixed)) % max(1, count - fixed)
        return jnp.zeros((count,), jnp.int32).at[order[jnp.where(places < fixed, places, moved)]].set(jnp.asarray(lengths, jnp.int32))

    lengths = jnp.where(number % 4 == 0, named(packed, number // 4), named(usual, number - number // 4 - 1))
    mixed = jax.random.permutation(jax.random.fold_in(own, 3), count)
    source_of, receiver = mixed[0:count // 2 * 2:2], mixed[1:count // 2 * 2:2]
    room = jnp.minimum(lengths[source_of] - 1, reach - lengths[receiver]) // 2
    room = jnp.where((source_of == order[0]) | (receiver == order[0]) | (lengths[receiver] == 0), 0, jnp.maximum(room, 0))
    moved = jax.random.randint(jax.random.fold_in(own, 4), (count // 2,), 0, 1 << 20) % (room + 1)
    lengths = lengths.at[source_of].add(-moved).at[receiver].add(moved)
    items = jnp.searchsorted(jnp.cumsum(lengths), jnp.arange(rows * top), side="right").astype(jnp.int32)
    table = items.reshape(top, rows).T
    table = table[jax.random.permutation(jax.random.fold_in(own, 1), rows)]
    turn = jax.random.randint(jax.random.fold_in(own, 2), (rows, 1), 0, top)
    return jnp.take_along_axis(table, (jnp.arange(top)[None, :] + turn) % top, axis=1)


def shares(number_of, total, bound, skew, full):
    portions = [(1 << 20) // math.isqrt(standing ** skew) + 1 for standing in range(1, number_of + 1)]
    largest = bound if full else min(bound, max(-(-total // number_of), total * portions[0] // sum(portions)))
    least = 1 if total - largest >= number_of - 1 else 0
    counts, spare = [largest] + [least] * (number_of - 1), total - largest - least * (number_of - 1)
    while spare > 0:
        candidates = [i for i in range(1, number_of) if counts[i] < largest] or [i for i in range(1, number_of) if counts[i] < bound]
        mass, remaining = sum([portions[i] for i in candidates]), spare
        for i in candidates:
            extra = min(bound - counts[i], max(1, remaining * portions[i] // mass), spare)
            counts[i] = counts[i] + extra
            spare = spare - extra
    return np.array(counts)


def scatter_about(stream_key, shape, deviation, reach, pieces=(), held_as=jnp.bfloat16):
    drawn = deviation * jax.random.normal(stream_key, shape, jnp.float32)
    if pieces:
        drawn = drawn * levels(stream_key, shape, pieces, -0.22, 0.18)
    return jnp.clip(drawn, -reach, reach).astype(held_as)


def setup_inputs(seed: int = 0) -> dict:
    key_list = jax.random.split(jax.random.key(seed), 8)
    velocity = scatter_about(key_list[0], (3, NY, NX, NZ), 1.0, 6.0, ((1, 8), (2, 32)), jnp.float32)
    sample_block = place_ends(jax.random.randint(key_list[1], (N_WALL, N_STREAM * SAMPLES), 0, NBLK), jax.random.fold_in(key_list[1], 1), 0, NBLK - 1).astype(jnp.int32)
    sample_member_keys = jax.random.split(jax.random.fold_in(key_list[2], 1), N_WALL * (N_STREAM * SAMPLES) // SAMPLES)
    sample_member_turns = jax.random.permutation(jax.random.fold_in(key_list[2], 3), N_WALL * (N_STREAM * SAMPLES) // SAMPLES)
    sample_member = jax.vmap(lambda own, number: shared_out(jax.random.fold_in(key_list[2], 2), own, number, SAMPLES, N_WALL, 1, CAP, 2))(sample_member_keys, sample_member_turns).reshape((N_WALL, N_STREAM * SAMPLES, 1))
    k_first = scatter_about(key_list[3], (MEMBERS, 54, CH), 1.0, 6.0, ((0, 8),))
    k_second = scatter_about(key_list[4], (MEMBERS, 27, CH, CH), 1.0, 6.0, ((0, 8),))
    w_hidden = scatter_about(key_list[5], (MEMBERS, FEATS, HID), 1.0, 6.0, ((0, 8),))
    w_out = scatter_about(key_list[6], (MEMBERS, HID, 2), 1.0, 6.0, ((0, 8),))
    return {"velocity": velocity, "sample_block": sample_block, "sample_member": sample_member, "k_first": k_first, "k_second": k_second, "w_hidden": w_hidden, "w_out": w_out}


highest = lax.Precision.HIGHEST
time_step = 0.005
relax_rate = 20.0
viscosity = 0.3
learn_rate = 0.5
rms_eps = 1e-06
tap_offsets = [(first_off, second_off, third_off) for first_off in (-1, 0, 1) for second_off in (-1, 0, 1) for third_off in (-1, 0, 1)]

def cheb_tables(points):
    order = points - 1
    node_index = np.arange(points)
    nodes = -np.cos(np.pi * node_index / order)
    end_weight = np.where((node_index == 0) | (node_index == order), 2.0, 1.0)
    parity = (-1.0) ** (node_index[:, None] + node_index[None, :])
    offdiag = 1.0 - np.eye(points)
    spread = nodes[:, None] - nodes[None, :] + np.eye(points)
    deriv = end_weight[:, None] / end_weight[None, :] * parity / spread * offdiag
    deriv = deriv - np.eye(points) * deriv.sum(axis=1)[:, None]
    highpass = parity / (order * end_weight[None, :])
    return (deriv, highpass, 0.5 * order * order)

def along_axis(values, axis, periodic):
    deriv, highpass, lift_half = cheb_tables(P_SIZE)
    moved = jnp.moveaxis(values, axis, -1)
    leading = moved.shape[:-1]
    count = moved.shape[-1] // P_SIZE
    blocks = moved.reshape(leading + (count, P_SIZE))
    slope = jnp.einsum('...ep,qp->...eq', blocks, jnp.asarray(deriv, jnp.float32), precision=highest)
    upper = jnp.einsum('...ep,qp->...eq', blocks, jnp.asarray(highpass, jnp.float32), precision=highest)
    first = blocks[..., 0]
    last = blocks[..., P_SIZE - 1]
    if periodic:
        from_left = jnp.roll(last, 1, axis=-1)
        from_right = jnp.roll(first, -1, axis=-1)
    else:
        zeros_edge = jnp.zeros(leading + (1,), jnp.float32)
        from_left = jnp.concatenate([zeros_edge, last[..., :-1]], axis=-1)
        from_right = jnp.concatenate([first[..., 1:], zeros_edge], axis=-1)
    slope = slope.at[..., 0].add(-lift_half * (from_left - first))
    slope = slope.at[..., P_SIZE - 1].add(lift_half * (from_right - last))
    return (jnp.moveaxis(slope.reshape(moved.shape), -1, axis), jnp.moveaxis(upper.reshape(moved.shape), -1, axis))

def slot_matrix(members, member_count):
    member_hot = (members[..., None] == jnp.arange(member_count, dtype=jnp.int32)).astype(jnp.int32)
    before = jnp.cumsum(member_hot, axis=-2) - member_hot
    ranks = lax.optimization_barrier(jnp.sum(before * member_hot, axis=-1))
    slots = members * CAP + ranks
    return (slots[..., None, :] == jnp.arange(member_count * CAP, dtype=jnp.int32)[:, None]).astype(jnp.float32)

def shifted(grid, offset):
    padded = jnp.pad(grid, ((0, 0), (1, 1), (1, 1), (1, 1), (0, 0)))
    size_y, size_x, size_z = (grid.shape[1], grid.shape[2], grid.shape[3])
    return padded[:, 1 + offset[0]:1 + offset[0] + size_y, 1 + offset[1]:1 + offset[1] + size_x, 1 + offset[2]:1 + offset[2] + size_z, :]

def silu_slope(value):
    gate = jax.nn.sigmoid(value)
    return gate * (1.0 + value * (1.0 - gate))

def forward_back(patches, aim_rows, valid, k_first, k_second, w_hidden, w_out):
    batch = patches.shape[0]
    channels = k_second.shape[-1]
    inputs = patches.reshape(batch, 2, PY, PX, PZ).transpose(0, 2, 3, 4, 1)
    columns = jnp.concatenate([shifted(inputs, offset) for offset in tap_offsets], axis=-1).reshape(-1, 54)
    scale_one = 1.0 / math.sqrt(54.0)
    scale_two = 1.0 / math.sqrt(27.0 * channels)
    scale_three = 1.0 / math.sqrt(1.0 * w_hidden.shape[0])
    scale_four = 1.0 / math.sqrt(1.0 * w_hidden.shape[1])
    pre_one = jnp.dot(columns, k_first, preferred_element_type=jnp.float32) * scale_one
    hidden_one = jax.nn.silu(pre_one).astype(jnp.bfloat16).reshape(batch, PY, PX, PZ, channels)
    pre_two = jnp.zeros((batch * PY * PX * PZ, channels), jnp.float32)
    for tap_index in range(27):
        moved = shifted(hidden_one, tap_offsets[tap_index]).reshape(-1, channels)
        pre_two = pre_two + jnp.dot(moved, k_second[tap_index], preferred_element_type=jnp.float32)
    pre_two = pre_two * scale_two
    pooled = jax.nn.silu(pre_two).reshape(batch, PY // 2, 2, PX // 2, 2, PZ, channels).mean(axis=(2, 4))
    features = pooled.reshape(batch, -1).astype(jnp.bfloat16)
    pre_three = jnp.dot(features, w_hidden, preferred_element_type=jnp.float32) * scale_three
    hidden_three = jax.nn.silu(pre_three).astype(jnp.bfloat16)
    pred = jnp.dot(hidden_three, w_out, preferred_element_type=jnp.float32) * scale_four
    error = valid.astype(jnp.float32)[:, None] * (pred - aim_rows.astype(jnp.float32))
    grad_out = jnp.dot(hidden_three.astype(jnp.float32).T, error, precision=highest) * scale_four
    delta_three = (jnp.dot(error, w_out.astype(jnp.float32).T, precision=highest) * scale_four * silu_slope(pre_three)).astype(jnp.bfloat16)
    back_feat = jnp.dot(delta_three, w_hidden.T, preferred_element_type=jnp.float32) * scale_three
    back_grid = back_feat.reshape(batch, PY // 2, 1, PX // 2, 1, PZ, channels)
    spread_back = jnp.broadcast_to(back_grid, (batch, PY // 2, 2, PX // 2, 2, PZ, channels)).reshape(-1, channels) * 0.25
    delta_two = (spread_back * silu_slope(pre_two)).astype(jnp.bfloat16)
    delta_grid = delta_two.reshape(batch, PY, PX, PZ, channels)
    grad_two = []
    back_one = jnp.zeros((batch * PY * PX * PZ, channels), jnp.float32)
    for tap_index in range(27):
        offset = tap_offsets[tap_index]
        moved = shifted(hidden_one, offset).reshape(-1, channels)
        grad_two.append(jnp.dot(moved.T, delta_two, preferred_element_type=jnp.float32) * scale_two)
        mirror = (-offset[0], -offset[1], -offset[2])
        back_one = back_one + jnp.dot(shifted(delta_grid, mirror).reshape(-1, channels), k_second[tap_index].T, preferred_element_type=jnp.float32)
    delta_one = (back_one * scale_two * silu_slope(pre_one)).astype(jnp.bfloat16)
    grad_one = jnp.dot(columns.T, delta_one, preferred_element_type=jnp.float32) * scale_one
    return (pred, grad_one, jnp.stack(grad_two), grad_out, features, delta_three)

def row_update(weight, grad):
    scale = jnp.sqrt(lax.optimization_barrier(jnp.mean(grad * grad, axis=-1, keepdims=True)) + rms_eps)
    return weight.astype(jnp.float32) - learn_rate * grad / scale

def whole_update(weight, grad):
    scale = jnp.sqrt(jnp.mean(grad * grad) + rms_eps)
    return weight.astype(jnp.float32) - learn_rate * grad / scale

def to_members(values):
    rest = values.shape[3:]
    grid = values.reshape((N_WALL, N_STREAM, N_WALL, CAP) + rest)
    grid = jnp.swapaxes(grid, 0, 2)
    return grid.reshape((N_WALL, N_STREAM * N_WALL * CAP) + rest)

def reference(velocity, sample_block, sample_member, k_first, k_second, w_hidden, w_out):
    grad_x, high_x = along_axis(velocity, 2, True)
    grad_y, high_y = along_axis(velocity, 1, False)
    grad_z, high_z = along_axis(velocity, 3, True)
    advect = velocity[0][None] * grad_x + velocity[1][None] * grad_y + velocity[2][None] * grad_z
    new_field = velocity + time_step * (-advect - relax_rate * (high_x + high_y + high_z))
    rows_y, rows_x, rows_z = (EY * P_SIZE // PY, EX * P_SIZE // PX, NZ // PZ)
    tangent = jnp.stack([velocity[0], velocity[2]]).reshape(2, N_WALL, rows_y, PY, N_STREAM, rows_x, PX, rows_z, PZ)
    blocks = tangent.transpose(1, 4, 2, 5, 7, 0, 3, 6, 8).reshape(N_WALL, N_STREAM, NBLK, FEAT_IN)
    slope_wall = jnp.stack([grad_y[0], grad_y[2]]).reshape(2, N_WALL, rows_y, PY, N_STREAM, rows_x, PX, rows_z, PZ)
    stress_true = (viscosity * lax.optimization_barrier(jnp.mean(slope_wall, axis=(3, 6, 8)))).transpose(1, 3, 2, 4, 5, 0).reshape(N_WALL, N_STREAM, NBLK, 2)
    picked = sample_block.reshape(N_WALL, N_STREAM, SAMPLES)
    members = sample_member.reshape(N_WALL, N_STREAM, SAMPLES)
    take_rows = jax.vmap(jax.vmap(lambda lookup_table, row_index: jnp.take(lookup_table, row_index, axis=0)))
    patch_rows = take_rows(blocks, picked).astype(jnp.bfloat16)
    aim_rows = take_rows(stress_true, picked).astype(jnp.bfloat16)
    select = slot_matrix(members, N_WALL)
    send_rows = jnp.einsum('wtls,wtsf->wtlf', select, patch_rows.astype(jnp.float32), precision=highest).astype(jnp.bfloat16)
    send_aims = jnp.einsum('wtls,wtsf->wtlf', select, aim_rows.astype(jnp.float32), precision=highest).astype(jnp.bfloat16)
    send_valid = lax.optimization_barrier(jnp.sum(select, axis=-1)).astype(jnp.bfloat16)
    bundles = (to_members(send_rows), to_members(send_aims), to_members(send_valid), k_first, k_second, w_hidden, w_out)

    def per_member(bundle):
        pred, grad_one, grad_two, grad_out, features, delta_three = forward_back(bundle[0], bundle[1], bundle[2], bundle[3], bundle[4], bundle[5], bundle[6])
        grad_hidden = jnp.dot(features.T, delta_three, preferred_element_type=jnp.float32) * (1.0 / math.sqrt(1.0 * FEATS))
        return (pred, row_update(bundle[3], grad_one), row_update(bundle[4], grad_two), row_update(bundle[5], grad_hidden), whole_update(bundle[6], grad_out))
    preds, new_k_first, new_k_second, new_w_hidden, new_w_out = lax.map(per_member, bundles)
    back = jnp.swapaxes(preds.reshape(N_WALL, N_STREAM, N_WALL, CAP, 2), 0, 2).reshape(N_WALL, N_STREAM, N_WALL * CAP, 2)
    stress = jnp.einsum('wtls,wtlk->kwts', select, back, precision=highest).reshape(2, N_WALL, N_STREAM * SAMPLES)
    return (new_field, stress, new_k_first, new_k_second, new_w_hidden, new_w_out)
```

```python
import math

import jax
import jax.numpy as jnp
import numpy as np
from jax import lax
from jax.sharding import Mesh
from jax.sharding import PartitionSpec as P

P_SIZE = 8
PY = 4
PX = 4
PZ = 8
CH = 64
CAP = 2
FEATS = 2048
STREAM = ("stream_0", "stream_1", "stream_2")


highest = lax.Precision.HIGHEST
time_step = 0.005
relax_rate = 20.0
viscosity = 0.3
learn_rate = 0.5
rms_eps = 1e-06
def extended(shard, sides, width):
    edges = {}
    for axis, dim in sides:
        size, length = (lax.axis_size(axis), shard.shape[dim])
        up = [(i, (i + 1) % size) for i in range(size)]
        last = lax.slice_in_dim(shard, length - width, length, axis=dim)
        first = lax.slice_in_dim(shard, 0, width, axis=dim)
        edges[dim] = (
            lax.ppermute(last, axis, up),
            lax.ppermute(first, axis, [(b, a) for a, b in up]),
        )
    done = []
    for _, dim in sides:
        low, high = edges[dim]
        around = [(width, width) if d in done else (0, 0) for d in range(shard.ndim)]
        shard = jnp.concatenate([jnp.pad(low, around), shard, jnp.pad(high, around)], axis=dim)
        done.append(dim)
    return shard


def in_one_piece(arrays, axis, split_dim, concat_dim, along):
    widths = [math.prod(a.shape[along:]) for a in arrays]
    both = jnp.concatenate(
        [a.reshape(*a.shape[:along], w) for a, w in zip(arrays, widths)], axis=along
    )
    whole = lax.all_to_all(both, axis, split_axis=split_dim, concat_axis=concat_dim, tiled=True)
    tiles = jnp.split(whole, [sum(widths[:k]) for k in range(1, len(widths))], axis=along)
    return tuple((b.reshape(*whole.shape[:along], *a.shape[along:]) for a, b in zip(arrays, tiles)))


def joined_along(tiles, dim):
    lengths = list(tiles.shape[1:])
    lengths[dim] *= tiles.shape[0]
    return jnp.moveaxis(tiles, 0, dim).reshape(lengths)


def gather_in_order(shard, axes, order):
    tiles = shard
    for k in order:
        tiles = lax.all_gather(tiles, axes[k])
    done = order[::-1]
    back = [done.index(k) for k in range(len(axes))]
    tiles = tiles.transpose(*back, *range(len(axes), tiles.ndim))
    return tiles.reshape(-1, *shard.shape)


def gathered_by_axis(shard, axes, order, dim):
    return joined_along(gather_in_order(shard, axes, order), dim)


def cheb_tables(points):
    order = points - 1
    node_index = np.arange(points)
    nodes = -np.cos(np.pi * node_index / order)
    end_weight = np.where((node_index == 0) | (node_index == order), 2.0, 1.0)
    parity = (-1.0) ** (node_index[:, None] + node_index[None, :])
    offdiag = 1.0 - np.eye(points)
    spread = nodes[:, None] - nodes[None, :] + np.eye(points)
    deriv = end_weight[:, None] / end_weight[None, :] * parity / spread * offdiag
    deriv = deriv - np.eye(points) * deriv.sum(axis=1)[:, None]
    highpass = parity / (order * end_weight[None, :])
    return (deriv, highpass, 0.5 * order * order)


def axis_matrices(count, periodic):
    deriv, highpass, lift_half = cheb_tables(P_SIZE)
    length = count * P_SIZE
    slope = np.kron(np.eye(count), deriv)
    upper = np.kron(np.eye(count), highpass)
    faces = count if periodic else count - 1
    for element in range(faces):
        last_node = element * P_SIZE + P_SIZE - 1
        next_node = (element + 1) % count * P_SIZE
        slope[last_node, next_node] += lift_half
        slope[last_node, last_node] -= lift_half
        slope[next_node, last_node] -= lift_half
        slope[next_node, next_node] += lift_half
    if not periodic:
        slope[0, 0] += lift_half
        slope[length - 1, length - 1] -= lift_half
    paired = jnp.asarray(np.concatenate([slope, upper], axis=0), jnp.float32)
    return (paired, lift_half)


def slot_matrix(members, member_count):
    member_hot = (members[..., None] == jnp.arange(member_count, dtype=jnp.int32)).astype(jnp.int32)
    before = jnp.cumsum(member_hot, axis=-2) - member_hot
    ranks = jnp.sum(before * member_hot, axis=-1)
    slots = members * CAP + ranks
    return (slots[..., None, :] == jnp.arange(member_count * CAP, dtype=jnp.int32)[:, None]).astype(
        jnp.float32
    )


DIMS = ("NDHWC", "DHWIO", "NDHWC")
FILTER_DIMS = ("CDHWN", "IDHWO", "NDHWC")
SAME = ((1, 1), (1, 1), (1, 1))


def silu_slope(value):
    gate = jax.nn.sigmoid(value)
    return gate * (1.0 + value * (1.0 - gate))


def conv_taps(grid, kernel):
    return lax.conv_general_dilated(
        grid, kernel, (1, 1, 1), SAME, dimension_numbers=DIMS,
        preferred_element_type=jnp.float32,
    )


def conv_filter(grid, delta):
    taps = lax.conv_general_dilated(
        grid, delta, (1, 1, 1), SAME, dimension_numbers=FILTER_DIMS,
        preferred_element_type=jnp.float32,
    )
    return jnp.moveaxis(taps, 0, 3)


def forward_back(patches, aim_rows, valid, k_first, k_second, w_hidden, w_out):
    batch = patches.shape[0]
    channels = k_second.shape[-1]
    inputs = patches.reshape(batch, 2, PY, PX, PZ).transpose(0, 2, 3, 4, 1)
    first_taps = k_first.reshape(3, 3, 3, 2, channels)
    second_taps = k_second.reshape(3, 3, 3, channels, channels)
    scale_one = 1.0 / math.sqrt(54.0)
    scale_two = 1.0 / math.sqrt(27.0 * channels)
    scale_three = 1.0 / math.sqrt(1.0 * w_hidden.shape[0])
    scale_four = 1.0 / math.sqrt(1.0 * w_hidden.shape[1])
    pre_one = conv_taps(inputs, first_taps) * scale_one
    hidden_one = jax.nn.silu(pre_one).astype(jnp.bfloat16)
    pre_two = conv_taps(hidden_one, second_taps) * scale_two
    pooled = jax.nn.silu(pre_two).reshape(batch, PY // 2, 2, PX // 2, 2, PZ, channels).mean(axis=(2, 4))
    features = pooled.reshape(batch, -1).astype(jnp.bfloat16)
    pre_three = jnp.dot(features, w_hidden, preferred_element_type=jnp.float32) * scale_three
    hidden_three = jax.nn.silu(pre_three).astype(jnp.bfloat16)
    pred = jnp.dot(hidden_three, w_out, preferred_element_type=jnp.float32) * scale_four
    error = valid.astype(jnp.float32)[:, None] * (pred - aim_rows.astype(jnp.float32))
    grad_out = jnp.dot(hidden_three.astype(jnp.float32).T, error, precision=highest) * scale_four
    delta_three = (
        jnp.dot(error, w_out.astype(jnp.float32).T, precision=highest) * scale_four * silu_slope(pre_three)
    ).astype(jnp.bfloat16)
    back_feat = jnp.dot(delta_three, w_hidden.T, preferred_element_type=jnp.float32) * scale_three
    back_grid = back_feat.reshape(batch, PY // 2, 1, PX // 2, 1, PZ, channels)
    spread_back = jnp.broadcast_to(back_grid, (batch, PY // 2, 2, PX // 2, 2, PZ, channels)).reshape(pre_two.shape) * 0.25
    delta_two = (spread_back * silu_slope(pre_two)).astype(jnp.bfloat16)
    grad_two = (conv_filter(hidden_one, delta_two) * scale_two).reshape(27, channels, channels)
    mirrored = jnp.flip(second_taps, axis=(0, 1, 2)).swapaxes(3, 4)
    back_one = conv_taps(delta_two, mirrored)
    delta_one = (back_one * scale_two * silu_slope(pre_one)).astype(jnp.bfloat16)
    grad_one = (conv_filter(inputs, delta_one) * scale_one).reshape(54, channels)
    return (pred, grad_one, grad_two, grad_out, features, delta_three)


def row_update(weight, grad):
    scale = jnp.sqrt(jnp.mean(grad * grad, axis=-1, keepdims=True) + rms_eps)
    return weight.astype(jnp.float32) - learn_rate * grad / scale


def whole_update(weight, grad):
    scale = jnp.sqrt(jnp.mean(grad * grad) + rms_eps)
    return weight.astype(jnp.float32) - learn_rate * grad / scale


def body(velocity, sample_block, sample_member, k_first, k_second, w_hidden, w_out):
    wall_count = lax.axis_size("wall")
    wall_place = lax.axis_index("wall")
    flow_count = lax.axis_size(STREAM)
    flow_place = lax.axis_index(STREAM)
    padded = extended(velocity, (("wall", 1), (STREAM, 2)), 1)
    keep_low = (wall_place > 0).astype(jnp.float32)
    keep_high = (wall_place < wall_count - 1).astype(jnp.float32)
    below = padded[:, 0, 1:-1, :] * keep_low
    above = padded[:, -1, 1:-1, :] * keep_high
    left_face = padded[:, 1:-1, 0, :]
    right_face = padded[:, 1:-1, -1, :]
    size_y, size_x, size_z = (velocity.shape[1], velocity.shape[2], velocity.shape[3])
    pair_y, lift_half = axis_matrices(size_y // P_SIZE, False)
    pair_x, lift_same = axis_matrices(size_x // P_SIZE, False)
    pair_z, lift_again = axis_matrices(size_z // P_SIZE, True)
    along_y = jnp.einsum("cyxz,wy->cwxz", velocity, pair_y, precision=highest)
    grad_y = (
        along_y[:, :size_y]
        .at[:, 0]
        .add(-lift_half * below)
        .at[:, size_y - 1]
        .add(lift_half * above)
    )
    high_y = along_y[:, size_y:]
    along_x = jnp.einsum("cyxz,wx->cywz", velocity, pair_x, precision=highest)
    grad_x = (
        along_x[:, :, :size_x]
        .at[:, :, 0]
        .add(-lift_half * left_face)
        .at[:, :, size_x - 1]
        .add(lift_half * right_face)
    )
    high_x = along_x[:, :, size_x:]
    along_z = jnp.einsum("cyxz,wz->cyxw", velocity, pair_z, precision=highest)
    grad_z = along_z[..., :size_z]
    high_z = along_z[..., size_z:]
    advect = velocity[0][None] * grad_x + velocity[1][None] * grad_y + velocity[2][None] * grad_z
    new_field = velocity + time_step * (-advect - relax_rate * (high_x + high_y + high_z))
    rows_y, rows_x, rows_z = (size_y // PY, size_x // PX, size_z // PZ)
    tangent = jnp.stack([velocity[0], velocity[2]]).reshape(2, rows_y, PY, rows_x, PX, rows_z, PZ)
    blocks = tangent.transpose(1, 3, 5, 0, 2, 4, 6).reshape(-1, 2 * PY * PX * PZ)
    slope_wall = jnp.stack([grad_y[0], grad_y[2]]).reshape(2, rows_y, PY, rows_x, PX, rows_z, PZ)
    stress_true = (
        (viscosity * jnp.mean(slope_wall, axis=(2, 4, 6))).transpose(1, 2, 3, 0).reshape(-1, 2)
    )
    picked = sample_block.reshape(-1)
    members = sample_member.reshape(-1)
    patch_rows = jnp.take(blocks, picked, axis=0).astype(jnp.bfloat16)
    aim_rows = jnp.take(stress_true, picked, axis=0).astype(jnp.bfloat16)
    select = slot_matrix(members, wall_count)
    select_half = select.astype(jnp.bfloat16)
    send_rows = jnp.dot(select_half, patch_rows, preferred_element_type=jnp.float32).astype(
        jnp.bfloat16
    )
    send_aims = jnp.dot(select_half, aim_rows, preferred_element_type=jnp.float32).astype(
        jnp.bfloat16
    )
    send_valid = jnp.sum(select, axis=1).astype(jnp.bfloat16)
    recv_rows, recv_aims, recv_valid = in_one_piece(
        (send_rows, send_aims, send_valid), "wall", 0, 0, 1
    )
    pred, grad_one, grad_two, grad_out, features, delta_three = forward_back(
        recv_rows, recv_aims, recv_valid, k_first[0], k_second[0], w_hidden[0], w_out[0]
    )
    back = lax.all_to_all(pred, "wall", split_axis=0, concat_axis=0, tiled=True)
    stress_local = jnp.dot(select.T, back, precision=highest)
    stress = stress_local.T[:, None, :]
    share_rows = FEATS // flow_count
    dense_scale = 1.0 / math.sqrt(1.0 * FEATS)
    columns_here = lax.all_to_all(features, STREAM, split_axis=1, concat_axis=0, tiled=True)
    grad_hidden = (
        jnp.dot(
            columns_here.T,
            gathered_by_axis(delta_three, STREAM, (1, 0, 2), 0),
            preferred_element_type=jnp.float32,
        )
        * dense_scale
    )
    own_rows = lax.dynamic_slice_in_dim(w_hidden[0], flow_place * share_rows, share_rows, 0)
    new_w_hidden = row_update(own_rows, grad_hidden)[None]
    grad_one, grad_two, grad_out = lax.psum((grad_one, grad_two, grad_out), STREAM)
    new_k_second = row_update(k_second[0], grad_two)
    new_k_first = row_update(k_first[0], grad_one)
    new_w_out = whole_update(w_out[0], grad_out)
    return (new_field, stress, new_k_first[None], new_k_second[None], new_w_hidden, new_w_out[None])


def solution(mesh):
    torus = Mesh(
        mesh.devices.reshape(mesh.shape["wall"], 8, 2, 2),
        ("wall", "stream_0", "stream_1", "stream_2"),
    )
    in_specs = (
        P(None, "wall", STREAM, None),
        P("wall", STREAM),
        P("wall", STREAM, None),
        P("wall", None, None),
        P("wall", None, None, None),
        P("wall", None, None),
        P("wall", None, None),
    )
    out_specs = (
        P(None, "wall", STREAM, None),
        P(None, "wall", STREAM),
        P("wall", None, None),
        P("wall", None, None, None),
        P("wall", STREAM, None),
        P("wall", None, None),
    )
    return jax.shard_map(body, mesh=torus, in_specs=in_specs, out_specs=out_specs, check_vma=False)
```

```python
import math

import jax
import jax.numpy as jnp
import numpy as np
from jax import lax
from jax.sharding import Mesh
from jax.sharding import PartitionSpec as P

P_SIZE = 8
PY = 4
PX = 4
PZ = 8
CH = 64
CAP = 2
FEATS = 2048
STREAM = ("stream_0", "stream_1", "stream_2")


highest = lax.Precision.HIGHEST
time_step = 0.005
relax_rate = 20.0
viscosity = 0.3
learn_rate = 0.5
rms_eps = 1e-06
def extended(shard, sides, width):
    edges = {}
    for axis, dim in sides:
        size, length = (lax.axis_size(axis), shard.shape[dim])
        up = [(i, (i + 1) % size) for i in range(size)]
        last = lax.slice_in_dim(shard, length - width, length, axis=dim)
        first = lax.slice_in_dim(shard, 0, width, axis=dim)
        edges[dim] = (
            lax.ppermute(last, axis, up),
            lax.ppermute(first, axis, [(b, a) for a, b in up]),
        )
    done = []
    for _, dim in sides:
        low, high = edges[dim]
        around = [(width, width) if d in done else (0, 0) for d in range(shard.ndim)]
        shard = jnp.concatenate([jnp.pad(low, around), shard, jnp.pad(high, around)], axis=dim)
        done.append(dim)
    return shard


def in_one_piece(arrays, axis, split_dim, concat_dim, along):
    widths = [math.prod(a.shape[along:]) for a in arrays]
    both = jnp.concatenate(
        [a.reshape(*a.shape[:along], w) for a, w in zip(arrays, widths)], axis=along
    )
    whole = lax.all_to_all(both, axis, split_axis=split_dim, concat_axis=concat_dim, tiled=True)
    tiles = jnp.split(whole, [sum(widths[:k]) for k in range(1, len(widths))], axis=along)
    return tuple((b.reshape(*whole.shape[:along], *a.shape[along:]) for a, b in zip(arrays, tiles)))


def joined_along(tiles, dim):
    lengths = list(tiles.shape[1:])
    lengths[dim] *= tiles.shape[0]
    return jnp.moveaxis(tiles, 0, dim).reshape(lengths)


def gather_in_order(shard, axes, order):
    tiles = shard
    for k in order:
        tiles = lax.all_gather(tiles, axes[k])
    done = order[::-1]
    back = [done.index(k) for k in range(len(axes))]
    tiles = tiles.transpose(*back, *range(len(axes), tiles.ndim))
    return tiles.reshape(-1, *shard.shape)


def gathered_by_axis(shard, axes, order, dim):
    return joined_along(gather_in_order(shard, axes, order), dim)


def from_everyone(shard, axis):
    copies = jnp.broadcast_to(shard, (lax.axis_size(axis), *shard.shape))
    return lax.all_to_all(copies, axis, split_axis=0, concat_axis=0, tiled=True)


def collect(shard, axis, dim):
    return joined_along(from_everyone(shard, axis), dim)


def summed_and_owned(whole, shared, axis):
    count = lax.axis_size(axis)
    copies = jnp.broadcast_to(whole.ravel(), (count, whole.size))
    tiles = shared.reshape(count, -1)
    both = jnp.concatenate([copies, tiles], axis=1)
    arrived = lax.all_to_all(both, axis, split_axis=0, concat_axis=0, tiled=True).sum(axis=0)
    return arrived[: whole.size].reshape(whole.shape), arrived[whole.size :].reshape(-1, shared.shape[-1])


def cheb_tables(points):
    order = points - 1
    node_index = np.arange(points)
    nodes = -np.cos(np.pi * node_index / order)
    end_weight = np.where((node_index == 0) | (node_index == order), 2.0, 1.0)
    parity = (-1.0) ** (node_index[:, None] + node_index[None, :])
    offdiag = 1.0 - np.eye(points)
    spread = nodes[:, None] - nodes[None, :] + np.eye(points)
    deriv = end_weight[:, None] / end_weight[None, :] * parity / spread * offdiag
    deriv = deriv - np.eye(points) * deriv.sum(axis=1)[:, None]
    highpass = parity / (order * end_weight[None, :])
    return (deriv, highpass, 0.5 * order * order)


def axis_matrices(count, periodic):
    deriv, highpass, lift_half = cheb_tables(P_SIZE)
    length = count * P_SIZE
    slope = np.kron(np.eye(count), deriv)
    upper = np.kron(np.eye(count), highpass)
    faces = count if periodic else count - 1
    for element in range(faces):
        last_node = element * P_SIZE + P_SIZE - 1
        next_node = (element + 1) % count * P_SIZE
        slope[last_node, next_node] += lift_half
        slope[last_node, last_node] -= lift_half
        slope[next_node, last_node] -= lift_half
        slope[next_node, next_node] += lift_half
    if not periodic:
        slope[0, 0] += lift_half
        slope[length - 1, length - 1] -= lift_half
    paired = jnp.asarray(np.concatenate([slope, upper], axis=0), jnp.float32)
    return (paired, lift_half)


def slot_matrix(members, member_count):
    member_hot = (members[..., None] == jnp.arange(member_count, dtype=jnp.int32)).astype(jnp.int32)
    before = jnp.cumsum(member_hot, axis=-2) - member_hot
    ranks = jnp.sum(before * member_hot, axis=-1)
    slots = members * CAP + ranks
    return (slots[..., None, :] == jnp.arange(member_count * CAP, dtype=jnp.int32)[:, None]).astype(
        jnp.float32
    )


DIMS = ("NDHWC", "DHWIO", "NDHWC")
FILTER_DIMS = ("CDHWN", "IDHWO", "NDHWC")
SAME = ((1, 1), (1, 1), (1, 1))


def silu_slope(value):
    gate = jax.nn.sigmoid(value)
    return gate * (1.0 + value * (1.0 - gate))


def conv_taps(grid, kernel):
    return lax.conv_general_dilated(
        grid, kernel, (1, 1, 1), SAME, dimension_numbers=DIMS,
        preferred_element_type=jnp.float32,
    )


def conv_filter(grid, delta):
    taps = lax.conv_general_dilated(
        grid, delta, (1, 1, 1), SAME, dimension_numbers=FILTER_DIMS,
        preferred_element_type=jnp.float32,
    )
    return jnp.moveaxis(taps, 0, 3)


def forward_back(patches, aim_rows, valid, k_first, k_second, w_hidden, w_out):
    batch = patches.shape[0]
    channels = k_second.shape[-1]
    inputs = patches.reshape(batch, 2, PY, PX, PZ).transpose(0, 2, 3, 4, 1)
    first_taps = k_first.reshape(3, 3, 3, 2, channels)
    second_taps = k_second.reshape(3, 3, 3, channels, channels)
    scale_one = 1.0 / math.sqrt(54.0)
    scale_two = 1.0 / math.sqrt(27.0 * channels)
    scale_three = 1.0 / math.sqrt(1.0 * w_hidden.shape[0])
    scale_four = 1.0 / math.sqrt(1.0 * w_hidden.shape[1])
    pre_one = conv_taps(inputs, first_taps) * scale_one
    hidden_one = jax.nn.silu(pre_one).astype(jnp.bfloat16)
    pre_two = conv_taps(hidden_one, second_taps) * scale_two
    pooled = jax.nn.silu(pre_two).reshape(batch, PY // 2, 2, PX // 2, 2, PZ, channels).mean(axis=(2, 4))
    features = pooled.reshape(batch, -1).astype(jnp.bfloat16)
    pre_three = jnp.dot(features, w_hidden, preferred_element_type=jnp.float32) * scale_three
    hidden_three = jax.nn.silu(pre_three).astype(jnp.bfloat16)
    pred = jnp.dot(hidden_three, w_out, preferred_element_type=jnp.float32) * scale_four
    error = valid.astype(jnp.float32)[:, None] * (pred - aim_rows.astype(jnp.float32))
    grad_out = jnp.dot(hidden_three.astype(jnp.float32).T, error, precision=highest) * scale_four
    delta_three = (
        jnp.dot(error, w_out.astype(jnp.float32).T, precision=highest) * scale_four * silu_slope(pre_three)
    ).astype(jnp.bfloat16)
    back_feat = jnp.dot(delta_three, w_hidden.T, preferred_element_type=jnp.float32) * scale_three
    back_grid = back_feat.reshape(batch, PY // 2, 1, PX // 2, 1, PZ, channels)
    spread_back = jnp.broadcast_to(back_grid, (batch, PY // 2, 2, PX // 2, 2, PZ, channels)).reshape(pre_two.shape) * 0.25
    delta_two = (spread_back * silu_slope(pre_two)).astype(jnp.bfloat16)
    grad_two = (conv_filter(hidden_one, delta_two) * scale_two).reshape(27, channels, channels)
    mirrored = jnp.flip(second_taps, axis=(0, 1, 2)).swapaxes(3, 4)
    back_one = conv_taps(delta_two, mirrored)
    delta_one = (back_one * scale_two * silu_slope(pre_one)).astype(jnp.bfloat16)
    grad_one = (conv_filter(inputs, delta_one) * scale_one).reshape(54, channels)
    return (pred, grad_one, grad_two, grad_out, features, delta_three)


def row_update(weight, grad):
    scale = jnp.sqrt(jnp.mean(grad * grad, axis=-1, keepdims=True) + rms_eps)
    return weight.astype(jnp.float32) - learn_rate * grad / scale


def whole_update(weight, grad):
    scale = jnp.sqrt(jnp.mean(grad * grad) + rms_eps)
    return weight.astype(jnp.float32) - learn_rate * grad / scale


def body(velocity, sample_block, sample_member, k_first, k_second, w_hidden, w_out):
    wall_count = lax.axis_size("wall")
    wall_place = lax.axis_index("wall")
    flow_count = lax.axis_size(STREAM)
    flow_place = lax.axis_index(STREAM)
    padded = extended(velocity, (("wall", 1), (STREAM, 2)), 1)
    keep_low = (wall_place > 0).astype(jnp.float32)
    keep_high = (wall_place < wall_count - 1).astype(jnp.float32)
    below = padded[:, 0, 1:-1, :] * keep_low
    above = padded[:, -1, 1:-1, :] * keep_high
    left_face = padded[:, 1:-1, 0, :]
    right_face = padded[:, 1:-1, -1, :]
    size_y, size_x, size_z = (velocity.shape[1], velocity.shape[2], velocity.shape[3])
    pair_y, lift_half = axis_matrices(size_y // P_SIZE, False)
    pair_x, lift_same = axis_matrices(size_x // P_SIZE, False)
    pair_z, lift_again = axis_matrices(size_z // P_SIZE, True)
    along_y = jnp.einsum("cyxz,wy->cwxz", velocity, pair_y, precision=highest)
    grad_y = (
        along_y[:, :size_y]
        .at[:, 0]
        .add(-lift_half * below)
        .at[:, size_y - 1]
        .add(lift_half * above)
    )
    high_y = along_y[:, size_y:]
    along_x = jnp.einsum("cyxz,wx->cywz", velocity, pair_x, precision=highest)
    grad_x = (
        along_x[:, :, :size_x]
        .at[:, :, 0]
        .add(-lift_half * left_face)
        .at[:, :, size_x - 1]
        .add(lift_half * right_face)
    )
    high_x = along_x[:, :, size_x:]
    along_z = jnp.einsum("cyxz,wz->cyxw", velocity, pair_z, precision=highest)
    grad_z = along_z[..., :size_z]
    high_z = along_z[..., size_z:]
    advect = velocity[0][None] * grad_x + velocity[1][None] * grad_y + velocity[2][None] * grad_z
    new_field = velocity + time_step * (-advect - relax_rate * (high_x + high_y + high_z))
    rows_y, rows_x, rows_z = (size_y // PY, size_x // PX, size_z // PZ)
    tangent = jnp.stack([velocity[0], velocity[2]]).reshape(2, rows_y, PY, rows_x, PX, rows_z, PZ)
    blocks = tangent.transpose(1, 3, 5, 0, 2, 4, 6).reshape(-1, 2 * PY * PX * PZ)
    slope_wall = jnp.stack([grad_y[0], grad_y[2]]).reshape(2, rows_y, PY, rows_x, PX, rows_z, PZ)
    stress_true = (
        (viscosity * jnp.mean(slope_wall, axis=(2, 4, 6))).transpose(1, 2, 3, 0).reshape(-1, 2)
    )
    picked = sample_block.reshape(-1)
    members = sample_member.reshape(-1)
    patch_rows = jnp.take(blocks, picked, axis=0).astype(jnp.bfloat16)
    aim_rows = jnp.take(stress_true, picked, axis=0).astype(jnp.bfloat16)
    select = slot_matrix(members, wall_count)
    select_half = select.astype(jnp.bfloat16)
    send_rows = jnp.dot(select_half, patch_rows, preferred_element_type=jnp.float32).astype(
        jnp.bfloat16
    )
    send_aims = jnp.dot(select_half, aim_rows, preferred_element_type=jnp.float32).astype(
        jnp.bfloat16
    )
    send_valid = jnp.sum(select, axis=1).astype(jnp.bfloat16)
    recv_rows, recv_aims, recv_valid = in_one_piece(
        (send_rows, send_aims, send_valid), "wall", 0, 0, 1
    )
    pred, grad_one, grad_two, grad_out, features, delta_three = forward_back(
        recv_rows, recv_aims, recv_valid, k_first[0], k_second[0], w_hidden[0], w_out[0]
    )
    back = lax.all_to_all(pred, "wall", split_axis=0, concat_axis=0, tiled=True)
    stress_local = jnp.dot(select.T, back, precision=highest)
    stress = stress_local.T[:, None, :]
    share_rows = FEATS // flow_count
    dense_scale = 1.0 / math.sqrt(1.0 * FEATS)
    columns_here = lax.all_to_all(features, STREAM, split_axis=1, concat_axis=0, tiled=True)
    grad_hidden = (
        jnp.dot(
            columns_here.T,
            gathered_by_axis(delta_three, STREAM, (1, 0, 2), 0),
            preferred_element_type=jnp.float32,
        )
        * dense_scale
    )
    own_rows = lax.dynamic_slice_in_dim(w_hidden[0], flow_place * share_rows, share_rows, 0)
    new_w_hidden = row_update(own_rows, grad_hidden)[None]
    small = jnp.concatenate([grad_one.ravel(), grad_out.ravel()])
    small, grad_share = summed_and_owned(small, grad_two.reshape(-1, CH), STREAM)
    grad_one = small[: grad_one.size].reshape(grad_one.shape)
    grad_out = small[grad_one.size :].reshape(grad_out.shape)
    share_count = grad_share.shape[0]
    kernel_own = lax.dynamic_slice_in_dim(
        k_second[0].reshape(-1, CH), flow_place * share_count, share_count, 0
    )
    updated_rows = row_update(kernel_own, grad_share)
    new_k_second = collect(updated_rows, STREAM, 0).reshape(k_second.shape[1:])
    new_k_first = row_update(k_first[0], grad_one)
    new_w_out = whole_update(w_out[0], grad_out)
    return (new_field, stress, new_k_first[None], new_k_second[None], new_w_hidden, new_w_out[None])


def solution(mesh):
    torus = Mesh(
        mesh.devices.reshape(mesh.shape["wall"], 8, 2, 2),
        ("wall", "stream_0", "stream_1", "stream_2"),
    )
    in_specs = (
        P(None, "wall", STREAM, None),
        P("wall", STREAM),
        P("wall", STREAM, None),
        P("wall", None, None),
        P("wall", None, None, None),
        P("wall", None, None),
        P("wall", None, None),
    )
    out_specs = (
        P(None, "wall", STREAM, None),
        P(None, "wall", STREAM),
        P("wall", None, None),
        P("wall", None, None, None),
        P("wall", STREAM, None),
        P("wall", None, None),
    )
    return jax.shard_map(body, mesh=torus, in_specs=in_specs, out_specs=out_specs, check_vma=False)
```

```python
import math

import jax
import jax.numpy as jnp
import numpy as np
from jax import lax
from jax.sharding import Mesh
from jax.sharding import PartitionSpec as P

P_SIZE = 8
PY = 4
PX = 4
PZ = 8
CH = 64
CAP = 2
FEATS = 2048
STREAM = ("stream_0", "stream_1", "stream_2")


highest = lax.Precision.HIGHEST
time_step = 0.005
relax_rate = 20.0
viscosity = 0.3
learn_rate = 0.5
rms_eps = 1e-06
def extended(shard, sides, width):
    edges = {}
    for axis, dim in sides:
        size, length = (lax.axis_size(axis), shard.shape[dim])
        up = [(i, (i + 1) % size) for i in range(size)]
        last = lax.slice_in_dim(shard, length - width, length, axis=dim)
        first = lax.slice_in_dim(shard, 0, width, axis=dim)
        edges[dim] = (
            lax.ppermute(last, axis, up),
            lax.ppermute(first, axis, [(b, a) for a, b in up]),
        )
    done = []
    for _, dim in sides:
        low, high = edges[dim]
        around = [(width, width) if d in done else (0, 0) for d in range(shard.ndim)]
        shard = jnp.concatenate([jnp.pad(low, around), shard, jnp.pad(high, around)], axis=dim)
        done.append(dim)
    return shard


def in_one_piece(arrays, axis, split_dim, concat_dim, along):
    widths = [math.prod(a.shape[along:]) for a in arrays]
    both = jnp.concatenate(
        [a.reshape(*a.shape[:along], w) for a, w in zip(arrays, widths)], axis=along
    )
    whole = lax.all_to_all(both, axis, split_axis=split_dim, concat_axis=concat_dim, tiled=True)
    tiles = jnp.split(whole, [sum(widths[:k]) for k in range(1, len(widths))], axis=along)
    return tuple((b.reshape(*whole.shape[:along], *a.shape[along:]) for a, b in zip(arrays, tiles)))


def joined_along(tiles, dim):
    lengths = list(tiles.shape[1:])
    lengths[dim] *= tiles.shape[0]
    return jnp.moveaxis(tiles, 0, dim).reshape(lengths)


def from_everyone(shard, axis):
    copies = jnp.broadcast_to(shard, (lax.axis_size(axis), *shard.shape))
    return lax.all_to_all(copies, axis, split_axis=0, concat_axis=0, tiled=True)


def collect(shard, axis, dim):
    return joined_along(from_everyone(shard, axis), dim)


def summed_and_owned(whole, shared, axis):
    count = lax.axis_size(axis)
    copies = jnp.broadcast_to(whole.ravel(), (count, whole.size))
    tiles = shared.reshape(count, -1)
    both = jnp.concatenate([copies, tiles], axis=1)
    arrived = lax.all_to_all(both, axis, split_axis=0, concat_axis=0, tiled=True).sum(axis=0)
    return arrived[: whole.size].reshape(whole.shape), arrived[whole.size :].reshape(-1, shared.shape[-1])


def dense_inputs(features, delta, axis):
    count = lax.axis_size(axis)
    batch, width = features.shape
    tiles = features.reshape(batch, count, width // count).transpose(1, 0, 2)
    copies = jnp.broadcast_to(delta, (count, *delta.shape))
    both = jnp.concatenate([tiles, copies], axis=2)
    arrived = lax.all_to_all(both, axis, split_axis=0, concat_axis=0, tiled=True)
    arrived = arrived.reshape(count * batch, -1)
    return arrived[:, : width // count], arrived[:, width // count :]


def cheb_tables(points):
    order = points - 1
    node_index = np.arange(points)
    nodes = -np.cos(np.pi * node_index / order)
    end_weight = np.where((node_index == 0) | (node_index == order), 2.0, 1.0)
    parity = (-1.0) ** (node_index[:, None] + node_index[None, :])
    offdiag = 1.0 - np.eye(points)
    spread = nodes[:, None] - nodes[None, :] + np.eye(points)
    deriv = end_weight[:, None] / end_weight[None, :] * parity / spread * offdiag
    deriv = deriv - np.eye(points) * deriv.sum(axis=1)[:, None]
    highpass = parity / (order * end_weight[None, :])
    return (deriv, highpass, 0.5 * order * order)


def axis_matrices(count, periodic):
    deriv, highpass, lift_half = cheb_tables(P_SIZE)
    length = count * P_SIZE
    slope = np.kron(np.eye(count), deriv)
    upper = np.kron(np.eye(count), highpass)
    faces = count if periodic else count - 1
    for element in range(faces):
        last_node = element * P_SIZE + P_SIZE - 1
        next_node = (element + 1) % count * P_SIZE
        slope[last_node, next_node] += lift_half
        slope[last_node, last_node] -= lift_half
        slope[next_node, last_node] -= lift_half
        slope[next_node, next_node] += lift_half
    if not periodic:
        slope[0, 0] += lift_half
        slope[length - 1, length - 1] -= lift_half
    paired = jnp.asarray(np.concatenate([slope, upper], axis=0), jnp.float32)
    return (paired, lift_half)


def slot_matrix(members, member_count):
    member_hot = (members[..., None] == jnp.arange(member_count, dtype=jnp.int32)).astype(jnp.int32)
    before = jnp.cumsum(member_hot, axis=-2) - member_hot
    ranks = jnp.sum(before * member_hot, axis=-1)
    slots = members * CAP + ranks
    return (slots[..., None, :] == jnp.arange(member_count * CAP, dtype=jnp.int32)[:, None]).astype(
        jnp.float32
    )


DIMS = ("NDHWC", "DHWIO", "NDHWC")
FILTER_DIMS = ("CDHWN", "IDHWO", "NDHWC")
SAME = ((1, 1), (1, 1), (1, 1))


def silu_slope(value):
    gate = jax.nn.sigmoid(value)
    return gate * (1.0 + value * (1.0 - gate))


def conv_taps(grid, kernel):
    return lax.conv_general_dilated(
        grid, kernel, (1, 1, 1), SAME, dimension_numbers=DIMS,
        preferred_element_type=jnp.float32,
    )


def conv_filter(grid, delta):
    taps = lax.conv_general_dilated(
        grid, delta, (1, 1, 1), SAME, dimension_numbers=FILTER_DIMS,
        preferred_element_type=jnp.float32,
    )
    return jnp.moveaxis(taps, 0, 3)


def forward_back(patches, aim_rows, valid, k_first, k_second, w_hidden, w_out):
    batch = patches.shape[0]
    channels = k_second.shape[-1]
    inputs = patches.reshape(batch, 2, PY, PX, PZ).transpose(0, 2, 3, 4, 1)
    first_taps = k_first.reshape(3, 3, 3, 2, channels)
    second_taps = k_second.reshape(3, 3, 3, channels, channels)
    scale_one = 1.0 / math.sqrt(54.0)
    scale_two = 1.0 / math.sqrt(27.0 * channels)
    scale_three = 1.0 / math.sqrt(1.0 * w_hidden.shape[0])
    scale_four = 1.0 / math.sqrt(1.0 * w_hidden.shape[1])
    pre_one = conv_taps(inputs, first_taps) * scale_one
    hidden_one = jax.nn.silu(pre_one).astype(jnp.bfloat16)
    pre_two = conv_taps(hidden_one, second_taps) * scale_two
    pooled = jax.nn.silu(pre_two).reshape(batch, PY // 2, 2, PX // 2, 2, PZ, channels).mean(axis=(2, 4))
    features = pooled.reshape(batch, -1).astype(jnp.bfloat16)
    pre_three = jnp.dot(features, w_hidden, preferred_element_type=jnp.float32) * scale_three
    hidden_three = jax.nn.silu(pre_three).astype(jnp.bfloat16)
    pred = jnp.dot(hidden_three, w_out, preferred_element_type=jnp.float32) * scale_four
    error = valid.astype(jnp.float32)[:, None] * (pred - aim_rows.astype(jnp.float32))
    grad_out = jnp.dot(hidden_three.astype(jnp.float32).T, error, precision=highest) * scale_four
    delta_three = (
        jnp.dot(error, w_out.astype(jnp.float32).T, precision=highest) * scale_four * silu_slope(pre_three)
    ).astype(jnp.bfloat16)
    back_feat = jnp.dot(delta_three, w_hidden.T, preferred_element_type=jnp.float32) * scale_three
    back_grid = back_feat.reshape(batch, PY // 2, 1, PX // 2, 1, PZ, channels)
    spread_back = jnp.broadcast_to(back_grid, (batch, PY // 2, 2, PX // 2, 2, PZ, channels)).reshape(pre_two.shape) * 0.25
    delta_two = (spread_back * silu_slope(pre_two)).astype(jnp.bfloat16)
    grad_two = (conv_filter(hidden_one, delta_two) * scale_two).reshape(27, channels, channels)
    mirrored = jnp.flip(second_taps, axis=(0, 1, 2)).swapaxes(3, 4)
    back_one = conv_taps(delta_two, mirrored)
    delta_one = (back_one * scale_two * silu_slope(pre_one)).astype(jnp.bfloat16)
    grad_one = (conv_filter(inputs, delta_one) * scale_one).reshape(54, channels)
    return (pred, grad_one, grad_two, grad_out, features, delta_three)


def row_update(weight, grad):
    scale = jnp.sqrt(jnp.mean(grad * grad, axis=-1, keepdims=True) + rms_eps)
    return weight.astype(jnp.float32) - learn_rate * grad / scale


def whole_update(weight, grad):
    scale = jnp.sqrt(jnp.mean(grad * grad) + rms_eps)
    return weight.astype(jnp.float32) - learn_rate * grad / scale


def body(velocity, sample_block, sample_member, k_first, k_second, w_hidden, w_out):
    wall_count = lax.axis_size("wall")
    wall_place = lax.axis_index("wall")
    flow_count = lax.axis_size(STREAM)
    flow_place = lax.axis_index(STREAM)
    padded = extended(velocity, (("wall", 1), (STREAM, 2)), 1)
    keep_low = (wall_place > 0).astype(jnp.float32)
    keep_high = (wall_place < wall_count - 1).astype(jnp.float32)
    below = padded[:, 0, 1:-1, :] * keep_low
    above = padded[:, -1, 1:-1, :] * keep_high
    left_face = padded[:, 1:-1, 0, :]
    right_face = padded[:, 1:-1, -1, :]
    size_y, size_x, size_z = (velocity.shape[1], velocity.shape[2], velocity.shape[3])
    pair_y, lift_half = axis_matrices(size_y // P_SIZE, False)
    pair_x, lift_same = axis_matrices(size_x // P_SIZE, False)
    pair_z, lift_again = axis_matrices(size_z // P_SIZE, True)
    along_y = jnp.einsum("cyxz,wy->cwxz", velocity, pair_y, precision=highest)
    grad_y = (
        along_y[:, :size_y]
        .at[:, 0]
        .add(-lift_half * below)
        .at[:, size_y - 1]
        .add(lift_half * above)
    )
    high_y = along_y[:, size_y:]
    along_x = jnp.einsum("cyxz,wx->cywz", velocity, pair_x, precision=highest)
    grad_x = (
        along_x[:, :, :size_x]
        .at[:, :, 0]
        .add(-lift_half * left_face)
        .at[:, :, size_x - 1]
        .add(lift_half * right_face)
    )
    high_x = along_x[:, :, size_x:]
    along_z = jnp.einsum("cyxz,wz->cyxw", velocity, pair_z, precision=highest)
    grad_z = along_z[..., :size_z]
    high_z = along_z[..., size_z:]
    advect = velocity[0][None] * grad_x + velocity[1][None] * grad_y + velocity[2][None] * grad_z
    new_field = velocity + time_step * (-advect - relax_rate * (high_x + high_y + high_z))
    rows_y, rows_x, rows_z = (size_y // PY, size_x // PX, size_z // PZ)
    tangent = jnp.stack([velocity[0], velocity[2]]).reshape(2, rows_y, PY, rows_x, PX, rows_z, PZ)
    blocks = tangent.transpose(1, 3, 5, 0, 2, 4, 6).reshape(-1, 2 * PY * PX * PZ)
    slope_wall = jnp.stack([grad_y[0], grad_y[2]]).reshape(2, rows_y, PY, rows_x, PX, rows_z, PZ)
    stress_true = (
        (viscosity * jnp.mean(slope_wall, axis=(2, 4, 6))).transpose(1, 2, 3, 0).reshape(-1, 2)
    )
    picked = sample_block.reshape(-1)
    members = sample_member.reshape(-1)
    patch_rows = jnp.take(blocks, picked, axis=0).astype(jnp.bfloat16)
    aim_rows = jnp.take(stress_true, picked, axis=0).astype(jnp.bfloat16)
    select = slot_matrix(members, wall_count)
    select_half = select.astype(jnp.bfloat16)
    send_rows = jnp.dot(select_half, patch_rows, preferred_element_type=jnp.float32).astype(
        jnp.bfloat16
    )
    send_aims = jnp.dot(select_half, aim_rows, preferred_element_type=jnp.float32).astype(
        jnp.bfloat16
    )
    send_valid = jnp.sum(select, axis=1).astype(jnp.bfloat16)
    recv_rows, recv_aims, recv_valid = in_one_piece(
        (send_rows, send_aims, send_valid), "wall", 0, 0, 1
    )
    pred, grad_one, grad_two, grad_out, features, delta_three = forward_back(
        recv_rows, recv_aims, recv_valid, k_first[0], k_second[0], w_hidden[0], w_out[0]
    )
    back = lax.all_to_all(pred, "wall", split_axis=0, concat_axis=0, tiled=True)
    stress_local = jnp.dot(select.T, back, precision=highest)
    stress = stress_local.T[:, None, :]
    share_rows = FEATS // flow_count
    dense_scale = 1.0 / math.sqrt(1.0 * FEATS)
    columns_here, delta_all = dense_inputs(features, delta_three, STREAM)
    grad_hidden = (
        jnp.dot(columns_here.T, delta_all, preferred_element_type=jnp.float32) * dense_scale
    )
    own_rows = lax.dynamic_slice_in_dim(w_hidden[0], flow_place * share_rows, share_rows, 0)
    new_w_hidden = row_update(own_rows, grad_hidden)[None]
    small = jnp.concatenate([grad_one.ravel(), grad_out.ravel()])
    small, grad_share = summed_and_owned(small, grad_two.reshape(-1, CH), STREAM)
    grad_one = small[: grad_one.size].reshape(grad_one.shape)
    grad_out = small[grad_one.size :].reshape(grad_out.shape)
    share_count = grad_share.shape[0]
    kernel_own = lax.dynamic_slice_in_dim(
        k_second[0].reshape(-1, CH), flow_place * share_count, share_count, 0
    )
    updated_rows = row_update(kernel_own, grad_share)
    new_k_second = collect(updated_rows, STREAM, 0).reshape(k_second.shape[1:])
    new_k_first = row_update(k_first[0], grad_one)
    new_w_out = whole_update(w_out[0], grad_out)
    return (new_field, stress, new_k_first[None], new_k_second[None], new_w_hidden, new_w_out[None])


def solution(mesh):
    torus = Mesh(
        mesh.devices.reshape(mesh.shape["wall"], 8, 2, 2),
        ("wall", "stream_0", "stream_1", "stream_2"),
    )
    in_specs = (
        P(None, "wall", STREAM, None),
        P("wall", STREAM),
        P("wall", STREAM, None),
        P("wall", None, None),
        P("wall", None, None, None),
        P("wall", None, None),
        P("wall", None, None),
    )
    out_specs = (
        P(None, "wall", STREAM, None),
        P(None, "wall", STREAM),
        P("wall", None, None),
        P("wall", None, None, None),
        P("wall", STREAM, None),
        P("wall", None, None),
    )
    return jax.shard_map(body, mesh=torus, in_specs=in_specs, out_specs=out_specs, check_vma=False)
```

```python
import math

import jax
import jax.numpy as jnp
import numpy as np
from jax import lax
from jax.sharding import Mesh
from jax.sharding import PartitionSpec as P

P_SIZE = 8
PY = 4
PX = 4
PZ = 8
CH = 64
CAP = 2
FEATS = 2048
STREAM = ("stream_0", "stream_1", "stream_2")


highest = lax.Precision.HIGHEST
time_step = 0.005
relax_rate = 20.0
viscosity = 0.3
learn_rate = 0.5
rms_eps = 1e-06
def extended(shard, sides, width):
    edges = {}
    for axis, dim in sides:
        size, length = (lax.axis_size(axis), shard.shape[dim])
        up = [(i, (i + 1) % size) for i in range(size)]
        last = lax.slice_in_dim(shard, length - width, length, axis=dim)
        first = lax.slice_in_dim(shard, 0, width, axis=dim)
        edges[dim] = (
            lax.ppermute(last, axis, up),
            lax.ppermute(first, axis, [(b, a) for a, b in up]),
        )
    done = []
    for _, dim in sides:
        low, high = edges[dim]
        around = [(width, width) if d in done else (0, 0) for d in range(shard.ndim)]
        shard = jnp.concatenate([jnp.pad(low, around), shard, jnp.pad(high, around)], axis=dim)
        done.append(dim)
    return shard


def in_one_piece(arrays, axis, split_dim, concat_dim, along):
    widths = [math.prod(a.shape[along:]) for a in arrays]
    both = jnp.concatenate(
        [a.reshape(*a.shape[:along], w) for a, w in zip(arrays, widths)], axis=along
    )
    whole = lax.all_to_all(both, axis, split_axis=split_dim, concat_axis=concat_dim, tiled=True)
    tiles = jnp.split(whole, [sum(widths[:k]) for k in range(1, len(widths))], axis=along)
    return tuple((b.reshape(*whole.shape[:along], *a.shape[along:]) for a, b in zip(arrays, tiles)))


def joined_along(tiles, dim):
    lengths = list(tiles.shape[1:])
    lengths[dim] *= tiles.shape[0]
    return jnp.moveaxis(tiles, 0, dim).reshape(lengths)


def gather_in_order(shard, axes, order):
    tiles = shard
    for k in order:
        tiles = lax.all_gather(tiles, axes[k])
    done = order[::-1]
    back = [done.index(k) for k in range(len(axes))]
    tiles = tiles.transpose(*back, *range(len(axes), tiles.ndim))
    return tiles.reshape(-1, *shard.shape)


def gathered_by_axis(shard, axes, order, dim):
    return joined_along(gather_in_order(shard, axes, order), dim)


def from_everyone(shard, axis):
    copies = jnp.broadcast_to(shard, (lax.axis_size(axis), *shard.shape))
    return lax.all_to_all(copies, axis, split_axis=0, concat_axis=0, tiled=True)


def owner_sums(rows, small, axis):
    count = lax.axis_size(axis)
    spare = -small.size % count
    small = jnp.pad(small, (0, spare))
    both = jnp.concatenate([rows.reshape(count, -1), small.reshape(count, -1)], axis=1)
    arrived = lax.all_to_all(both, axis, split_axis=0, concat_axis=0, tiled=True).sum(axis=0)
    part = rows.size // count
    return arrived[:part].reshape(-1, rows.shape[-1]), arrived[part:]


def shared_back(rows, chunk, axis):
    everything = from_everyone(jnp.concatenate([rows.ravel(), chunk]), axis)
    whole_rows = everything[:, : rows.size].reshape(-1, rows.shape[-1])
    return whole_rows, everything[:, rows.size :].reshape(-1)


def cheb_tables(points):
    order = points - 1
    node_index = np.arange(points)
    nodes = -np.cos(np.pi * node_index / order)
    end_weight = np.where((node_index == 0) | (node_index == order), 2.0, 1.0)
    parity = (-1.0) ** (node_index[:, None] + node_index[None, :])
    offdiag = 1.0 - np.eye(points)
    spread = nodes[:, None] - nodes[None, :] + np.eye(points)
    deriv = end_weight[:, None] / end_weight[None, :] * parity / spread * offdiag
    deriv = deriv - np.eye(points) * deriv.sum(axis=1)[:, None]
    highpass = parity / (order * end_weight[None, :])
    return (deriv, highpass, 0.5 * order * order)


def axis_matrices(count, periodic):
    deriv, highpass, lift_half = cheb_tables(P_SIZE)
    length = count * P_SIZE
    slope = np.kron(np.eye(count), deriv)
    upper = np.kron(np.eye(count), highpass)
    faces = count if periodic else count - 1
    for element in range(faces):
        last_node = element * P_SIZE + P_SIZE - 1
        next_node = (element + 1) % count * P_SIZE
        slope[last_node, next_node] += lift_half
        slope[last_node, last_node] -= lift_half
        slope[next_node, last_node] -= lift_half
        slope[next_node, next_node] += lift_half
    if not periodic:
        slope[0, 0] += lift_half
        slope[length - 1, length - 1] -= lift_half
    paired = jnp.asarray(np.concatenate([slope, upper], axis=0), jnp.float32)
    return (paired, lift_half)


def slot_matrix(members, member_count):
    member_hot = (members[..., None] == jnp.arange(member_count, dtype=jnp.int32)).astype(jnp.int32)
    before = jnp.cumsum(member_hot, axis=-2) - member_hot
    ranks = jnp.sum(before * member_hot, axis=-1)
    slots = members * CAP + ranks
    return (slots[..., None, :] == jnp.arange(member_count * CAP, dtype=jnp.int32)[:, None]).astype(
        jnp.float32
    )


DIMS = ("NDHWC", "DHWIO", "NDHWC")
FILTER_DIMS = ("CDHWN", "IDHWO", "NDHWC")
SAME = ((1, 1), (1, 1), (1, 1))


def silu_slope(value):
    gate = jax.nn.sigmoid(value)
    return gate * (1.0 + value * (1.0 - gate))


def conv_taps(grid, kernel):
    return lax.conv_general_dilated(
        grid, kernel, (1, 1, 1), SAME, dimension_numbers=DIMS,
        preferred_element_type=jnp.float32,
    )


def conv_filter(grid, delta):
    taps = lax.conv_general_dilated(
        grid, delta, (1, 1, 1), SAME, dimension_numbers=FILTER_DIMS,
        preferred_element_type=jnp.float32,
    )
    return jnp.moveaxis(taps, 0, 3)


def forward_back(patches, aim_rows, valid, k_first, k_second, w_hidden, w_out):
    batch = patches.shape[0]
    channels = k_second.shape[-1]
    inputs = patches.reshape(batch, 2, PY, PX, PZ).transpose(0, 2, 3, 4, 1)
    first_taps = k_first.reshape(3, 3, 3, 2, channels)
    second_taps = k_second.reshape(3, 3, 3, channels, channels)
    scale_one = 1.0 / math.sqrt(54.0)
    scale_two = 1.0 / math.sqrt(27.0 * channels)
    scale_three = 1.0 / math.sqrt(1.0 * w_hidden.shape[0])
    scale_four = 1.0 / math.sqrt(1.0 * w_hidden.shape[1])
    pre_one = conv_taps(inputs, first_taps) * scale_one
    hidden_one = jax.nn.silu(pre_one).astype(jnp.bfloat16)
    pre_two = conv_taps(hidden_one, second_taps) * scale_two
    pooled = jax.nn.silu(pre_two).reshape(batch, PY // 2, 2, PX // 2, 2, PZ, channels).mean(axis=(2, 4))
    features = pooled.reshape(batch, -1).astype(jnp.bfloat16)
    pre_three = jnp.dot(features, w_hidden, preferred_element_type=jnp.float32) * scale_three
    hidden_three = jax.nn.silu(pre_three).astype(jnp.bfloat16)
    pred = jnp.dot(hidden_three, w_out, preferred_element_type=jnp.float32) * scale_four
    error = valid.astype(jnp.float32)[:, None] * (pred - aim_rows.astype(jnp.float32))
    grad_out = jnp.dot(hidden_three.astype(jnp.float32).T, error, precision=highest) * scale_four
    delta_three = (
        jnp.dot(error, w_out.astype(jnp.float32).T, precision=highest) * scale_four * silu_slope(pre_three)
    ).astype(jnp.bfloat16)
    back_feat = jnp.dot(delta_three, w_hidden.T, preferred_element_type=jnp.float32) * scale_three
    back_grid = back_feat.reshape(batch, PY // 2, 1, PX // 2, 1, PZ, channels)
    spread_back = jnp.broadcast_to(back_grid, (batch, PY // 2, 2, PX // 2, 2, PZ, channels)).reshape(pre_two.shape) * 0.25
    delta_two = (spread_back * silu_slope(pre_two)).astype(jnp.bfloat16)
    grad_two = (conv_filter(hidden_one, delta_two) * scale_two).reshape(27, channels, channels)
    mirrored = jnp.flip(second_taps, axis=(0, 1, 2)).swapaxes(3, 4)
    back_one = conv_taps(delta_two, mirrored)
    delta_one = (back_one * scale_two * silu_slope(pre_one)).astype(jnp.bfloat16)
    grad_one = (conv_filter(inputs, delta_one) * scale_one).reshape(54, channels)
    return (pred, grad_one, grad_two, grad_out, features, delta_three)


def row_update(weight, grad):
    scale = jnp.sqrt(jnp.mean(grad * grad, axis=-1, keepdims=True) + rms_eps)
    return weight.astype(jnp.float32) - learn_rate * grad / scale


def whole_update(weight, grad):
    scale = jnp.sqrt(jnp.mean(grad * grad) + rms_eps)
    return weight.astype(jnp.float32) - learn_rate * grad / scale


def body(velocity, sample_block, sample_member, k_first, k_second, w_hidden, w_out):
    wall_count = lax.axis_size("wall")
    wall_place = lax.axis_index("wall")
    flow_count = lax.axis_size(STREAM)
    flow_place = lax.axis_index(STREAM)
    padded = extended(velocity, (("wall", 1), (STREAM, 2)), 1)
    keep_low = (wall_place > 0).astype(jnp.float32)
    keep_high = (wall_place < wall_count - 1).astype(jnp.float32)
    below = padded[:, 0, 1:-1, :] * keep_low
    above = padded[:, -1, 1:-1, :] * keep_high
    left_face = padded[:, 1:-1, 0, :]
    right_face = padded[:, 1:-1, -1, :]
    size_y, size_x, size_z = (velocity.shape[1], velocity.shape[2], velocity.shape[3])
    pair_y, lift_half = axis_matrices(size_y // P_SIZE, False)
    pair_x, lift_same = axis_matrices(size_x // P_SIZE, False)
    pair_z, lift_again = axis_matrices(size_z // P_SIZE, True)
    along_y = jnp.einsum("cyxz,wy->cwxz", velocity, pair_y, precision=highest)
    grad_y = (
        along_y[:, :size_y]
        .at[:, 0]
        .add(-lift_half * below)
        .at[:, size_y - 1]
        .add(lift_half * above)
    )
    high_y = along_y[:, size_y:]
    along_x = jnp.einsum("cyxz,wx->cywz", velocity, pair_x, precision=highest)
    grad_x = (
        along_x[:, :, :size_x]
        .at[:, :, 0]
        .add(-lift_half * left_face)
        .at[:, :, size_x - 1]
        .add(lift_half * right_face)
    )
    high_x = along_x[:, :, size_x:]
    along_z = jnp.einsum("cyxz,wz->cyxw", velocity, pair_z, precision=highest)
    grad_z = along_z[..., :size_z]
    high_z = along_z[..., size_z:]
    advect = velocity[0][None] * grad_x + velocity[1][None] * grad_y + velocity[2][None] * grad_z
    new_field = velocity + time_step * (-advect - relax_rate * (high_x + high_y + high_z))
    rows_y, rows_x, rows_z = (size_y // PY, size_x // PX, size_z // PZ)
    tangent = jnp.stack([velocity[0], velocity[2]]).reshape(2, rows_y, PY, rows_x, PX, rows_z, PZ)
    blocks = tangent.transpose(1, 3, 5, 0, 2, 4, 6).reshape(-1, 2 * PY * PX * PZ)
    slope_wall = jnp.stack([grad_y[0], grad_y[2]]).reshape(2, rows_y, PY, rows_x, PX, rows_z, PZ)
    stress_true = (
        (viscosity * jnp.mean(slope_wall, axis=(2, 4, 6))).transpose(1, 2, 3, 0).reshape(-1, 2)
    )
    picked = sample_block.reshape(-1)
    members = sample_member.reshape(-1)
    patch_rows = jnp.take(blocks, picked, axis=0).astype(jnp.bfloat16)
    aim_rows = jnp.take(stress_true, picked, axis=0).astype(jnp.bfloat16)
    select = slot_matrix(members, wall_count)
    select_half = select.astype(jnp.bfloat16)
    send_rows = jnp.dot(select_half, patch_rows, preferred_element_type=jnp.float32).astype(
        jnp.bfloat16
    )
    send_aims = jnp.dot(select_half, aim_rows, preferred_element_type=jnp.float32).astype(
        jnp.bfloat16
    )
    send_valid = jnp.sum(select, axis=1).astype(jnp.bfloat16)
    new_field, send_rows, send_aims, send_valid = lax.optimization_barrier(
        (new_field, send_rows, send_aims, send_valid)
    )
    recv_rows, recv_aims, recv_valid = in_one_piece(
        (send_rows, send_aims, send_valid), "wall", 0, 0, 1
    )
    pred, grad_one, grad_two, grad_out, features, delta_three = forward_back(
        recv_rows, recv_aims, recv_valid, k_first[0], k_second[0], w_hidden[0], w_out[0]
    )
    back = lax.all_to_all(pred, "wall", split_axis=0, concat_axis=0, tiled=True)
    stress_local = jnp.dot(select.T, back, precision=highest)
    stress = stress_local.T[:, None, :]
    share_rows = FEATS // flow_count
    dense_scale = 1.0 / math.sqrt(1.0 * FEATS)
    columns_here = lax.all_to_all(features, STREAM, split_axis=1, concat_axis=0, tiled=True)
    grad_hidden = (
        jnp.dot(
            columns_here.T,
            gathered_by_axis(delta_three, STREAM, (1, 0, 2), 0),
            preferred_element_type=jnp.float32,
        )
        * dense_scale
    )
    own_rows = lax.dynamic_slice_in_dim(w_hidden[0], flow_place * share_rows, share_rows, 0)
    new_w_hidden = row_update(own_rows, grad_hidden)[None]
    small = jnp.concatenate([grad_one.ravel(), grad_out.ravel()])
    grad_share, small_part = owner_sums(grad_two.reshape(-1, CH), small, STREAM)
    share_count = grad_share.shape[0]
    kernel_own = lax.dynamic_slice_in_dim(
        k_second[0].reshape(-1, CH), flow_place * share_count, share_count, 0
    )
    updated_rows = row_update(kernel_own, grad_share)
    kernel_rows, small = shared_back(updated_rows, small_part, STREAM)
    new_k_second = kernel_rows.reshape(k_second.shape[1:])
    grad_one = small[: grad_one.size].reshape(grad_one.shape)
    grad_out = small[grad_one.size : grad_one.size + grad_out.size].reshape(grad_out.shape)
    new_k_first = row_update(k_first[0], grad_one)
    new_w_out = whole_update(w_out[0], grad_out)
    return (new_field, stress, new_k_first[None], new_k_second[None], new_w_hidden, new_w_out[None])


def solution(mesh):
    torus = Mesh(
        mesh.devices.reshape(mesh.shape["wall"], 8, 2, 2),
        ("wall", "stream_0", "stream_1", "stream_2"),
    )
    in_specs = (
        P(None, "wall", STREAM, None),
        P("wall", STREAM),
        P("wall", STREAM, None),
        P("wall", None, None),
        P("wall", None, None, None),
        P("wall", None, None),
        P("wall", None, None),
    )
    out_specs = (
        P(None, "wall", STREAM, None),
        P(None, "wall", STREAM),
        P("wall", None, None),
        P("wall", None, None, None),
        P("wall", STREAM, None),
        P("wall", None, None),
    )
    return jax.shard_map(body, mesh=torus, in_specs=in_specs, out_specs=out_specs, check_vma=False)
```

```python
import math

import jax
import jax.numpy as jnp
import numpy as np
from jax import lax
from jax.sharding import Mesh
from jax.sharding import PartitionSpec as P

P_SIZE = 8
PY = 4
PX = 4
PZ = 8
CH = 64
CAP = 2
FEATS = 2048
STREAM = ("stream_0", "stream_1", "stream_2")


highest = lax.Precision.HIGHEST
time_step = 0.005
relax_rate = 20.0
viscosity = 0.3
learn_rate = 0.5
rms_eps = 1e-06
def extended(shard, sides, width):
    edges = {}
    for axis, dim in sides:
        size, length = (lax.axis_size(axis), shard.shape[dim])
        up = [(i, (i + 1) % size) for i in range(size)]
        last = lax.slice_in_dim(shard, length - width, length, axis=dim)
        first = lax.slice_in_dim(shard, 0, width, axis=dim)
        edges[dim] = (
            lax.ppermute(last, axis, up),
            lax.ppermute(first, axis, [(b, a) for a, b in up]),
        )
    done = []
    for _, dim in sides:
        low, high = edges[dim]
        around = [(width, width) if d in done else (0, 0) for d in range(shard.ndim)]
        shard = jnp.concatenate([jnp.pad(low, around), shard, jnp.pad(high, around)], axis=dim)
        done.append(dim)
    return shard


def in_one_piece(arrays, axis, split_dim, concat_dim, along):
    widths = [math.prod(a.shape[along:]) for a in arrays]
    both = jnp.concatenate(
        [a.reshape(*a.shape[:along], w) for a, w in zip(arrays, widths)], axis=along
    )
    whole = lax.all_to_all(both, axis, split_axis=split_dim, concat_axis=concat_dim, tiled=True)
    tiles = jnp.split(whole, [sum(widths[:k]) for k in range(1, len(widths))], axis=along)
    return tuple((b.reshape(*whole.shape[:along], *a.shape[along:]) for a, b in zip(arrays, tiles)))


def from_everyone(shard, axis):
    copies = jnp.broadcast_to(shard, (lax.axis_size(axis), *shard.shape))
    return lax.all_to_all(copies, axis, split_axis=0, concat_axis=0, tiled=True)


def owner_sums(rows, small, tiles, axis):
    count = lax.axis_size(axis)
    spare = -small.size % count
    small = jnp.pad(small, (0, spare))
    summed = [rows.reshape(count, -1), small.reshape(count, -1)]
    width = sum(part.shape[1] for part in summed)
    both = jnp.concatenate(summed + [tiles.reshape(count, -1).astype(jnp.float32)], axis=1)
    arrived = lax.all_to_all(both, axis, split_axis=0, concat_axis=0, tiled=True)
    total = arrived[:, :width].sum(axis=0)
    part = rows.size // count
    moved = arrived[:, width:].astype(tiles.dtype).reshape(-1, *tiles.shape[2:])
    return total[:part].reshape(-1, rows.shape[-1]), total[part:], moved


def shared_back(rows, chunk, axis):
    everything = from_everyone(jnp.concatenate([rows.ravel(), chunk]), axis)
    whole_rows = everything[:, : rows.size].reshape(-1, rows.shape[-1])
    return whole_rows, everything[:, rows.size :].reshape(-1)


def cheb_tables(points):
    order = points - 1
    node_index = np.arange(points)
    nodes = -np.cos(np.pi * node_index / order)
    end_weight = np.where((node_index == 0) | (node_index == order), 2.0, 1.0)
    parity = (-1.0) ** (node_index[:, None] + node_index[None, :])
    offdiag = 1.0 - np.eye(points)
    spread = nodes[:, None] - nodes[None, :] + np.eye(points)
    deriv = end_weight[:, None] / end_weight[None, :] * parity / spread * offdiag
    deriv = deriv - np.eye(points) * deriv.sum(axis=1)[:, None]
    highpass = parity / (order * end_weight[None, :])
    return (deriv, highpass, 0.5 * order * order)


def axis_matrices(count, periodic):
    deriv, highpass, lift_half = cheb_tables(P_SIZE)
    length = count * P_SIZE
    slope = np.kron(np.eye(count), deriv)
    upper = np.kron(np.eye(count), highpass)
    faces = count if periodic else count - 1
    for element in range(faces):
        last_node = element * P_SIZE + P_SIZE - 1
        next_node = (element + 1) % count * P_SIZE
        slope[last_node, next_node] += lift_half
        slope[last_node, last_node] -= lift_half
        slope[next_node, last_node] -= lift_half
        slope[next_node, next_node] += lift_half
    if not periodic:
        slope[0, 0] += lift_half
        slope[length - 1, length - 1] -= lift_half
    paired = jnp.asarray(np.concatenate([slope, upper], axis=0), jnp.float32)
    return (paired, lift_half)


def slot_matrix(members, member_count):
    member_hot = (members[..., None] == jnp.arange(member_count, dtype=jnp.int32)).astype(jnp.int32)
    before = jnp.cumsum(member_hot, axis=-2) - member_hot
    ranks = jnp.sum(before * member_hot, axis=-1)
    slots = members * CAP + ranks
    return (slots[..., None, :] == jnp.arange(member_count * CAP, dtype=jnp.int32)[:, None]).astype(
        jnp.float32
    )


DIMS = ("NDHWC", "DHWIO", "NDHWC")
FILTER_DIMS = ("CDHWN", "IDHWO", "NDHWC")
SAME = ((1, 1), (1, 1), (1, 1))


def silu_slope(value):
    gate = jax.nn.sigmoid(value)
    return gate * (1.0 + value * (1.0 - gate))


def conv_taps(grid, kernel):
    return lax.conv_general_dilated(
        grid, kernel, (1, 1, 1), SAME, dimension_numbers=DIMS,
        preferred_element_type=jnp.float32,
    )


def conv_filter(grid, delta):
    taps = lax.conv_general_dilated(
        grid, delta, (1, 1, 1), SAME, dimension_numbers=FILTER_DIMS,
        preferred_element_type=jnp.float32,
    )
    return jnp.moveaxis(taps, 0, 3)


def forward_back(patches, aim_rows, valid, k_first, k_second, w_hidden, w_out):
    batch = patches.shape[0]
    channels = k_second.shape[-1]
    inputs = patches.reshape(batch, 2, PY, PX, PZ).transpose(0, 2, 3, 4, 1)
    first_taps = k_first.reshape(3, 3, 3, 2, channels)
    second_taps = k_second.reshape(3, 3, 3, channels, channels)
    scale_one = 1.0 / math.sqrt(54.0)
    scale_two = 1.0 / math.sqrt(27.0 * channels)
    scale_three = 1.0 / math.sqrt(1.0 * w_hidden.shape[0])
    scale_four = 1.0 / math.sqrt(1.0 * w_hidden.shape[1])
    pre_one = conv_taps(inputs, first_taps) * scale_one
    hidden_one = jax.nn.silu(pre_one).astype(jnp.bfloat16)
    pre_two = conv_taps(hidden_one, second_taps) * scale_two
    pooled = jax.nn.silu(pre_two).reshape(batch, PY // 2, 2, PX // 2, 2, PZ, channels).mean(axis=(2, 4))
    features = pooled.reshape(batch, -1).astype(jnp.bfloat16)
    pre_three = jnp.dot(features, w_hidden, preferred_element_type=jnp.float32) * scale_three
    hidden_three = jax.nn.silu(pre_three).astype(jnp.bfloat16)
    pred = jnp.dot(hidden_three, w_out, preferred_element_type=jnp.float32) * scale_four
    error = valid.astype(jnp.float32)[:, None] * (pred - aim_rows.astype(jnp.float32))
    grad_out = jnp.dot(hidden_three.astype(jnp.float32).T, error, precision=highest) * scale_four
    delta_three = (
        jnp.dot(error, w_out.astype(jnp.float32).T, precision=highest) * scale_four * silu_slope(pre_three)
    ).astype(jnp.bfloat16)
    back_feat = jnp.dot(delta_three, w_hidden.T, preferred_element_type=jnp.float32) * scale_three
    back_grid = back_feat.reshape(batch, PY // 2, 1, PX // 2, 1, PZ, channels)
    spread_back = jnp.broadcast_to(back_grid, (batch, PY // 2, 2, PX // 2, 2, PZ, channels)).reshape(pre_two.shape) * 0.25
    delta_two = (spread_back * silu_slope(pre_two)).astype(jnp.bfloat16)
    grad_two = (conv_filter(hidden_one, delta_two) * scale_two).reshape(27, channels, channels)
    mirrored = jnp.flip(second_taps, axis=(0, 1, 2)).swapaxes(3, 4)
    back_one = conv_taps(delta_two, mirrored)
    delta_one = (back_one * scale_two * silu_slope(pre_one)).astype(jnp.bfloat16)
    grad_one = (conv_filter(inputs, delta_one) * scale_one).reshape(54, channels)
    return (pred, grad_one, grad_two, grad_out, features, delta_three)


def row_update(weight, grad):
    scale = jnp.sqrt(jnp.mean(grad * grad, axis=-1, keepdims=True) + rms_eps)
    return weight.astype(jnp.float32) - learn_rate * grad / scale


def whole_update(weight, grad):
    scale = jnp.sqrt(jnp.mean(grad * grad) + rms_eps)
    return weight.astype(jnp.float32) - learn_rate * grad / scale


def body(velocity, sample_block, sample_member, k_first, k_second, w_hidden, w_out):
    wall_count = lax.axis_size("wall")
    wall_place = lax.axis_index("wall")
    flow_count = lax.axis_size(STREAM)
    flow_place = lax.axis_index(STREAM)
    padded = extended(velocity, (("wall", 1), (STREAM, 2)), 1)
    keep_low = (wall_place > 0).astype(jnp.float32)
    keep_high = (wall_place < wall_count - 1).astype(jnp.float32)
    below = padded[:, 0, 1:-1, :] * keep_low
    above = padded[:, -1, 1:-1, :] * keep_high
    left_face = padded[:, 1:-1, 0, :]
    right_face = padded[:, 1:-1, -1, :]
    size_y, size_x, size_z = (velocity.shape[1], velocity.shape[2], velocity.shape[3])
    pair_y, lift_half = axis_matrices(size_y // P_SIZE, False)
    pair_x, lift_same = axis_matrices(size_x // P_SIZE, False)
    pair_z, lift_again = axis_matrices(size_z // P_SIZE, True)
    along_y = jnp.einsum("cyxz,wy->cwxz", velocity, pair_y, precision=highest)
    grad_y = (
        along_y[:, :size_y]
        .at[:, 0]
        .add(-lift_half * below)
        .at[:, size_y - 1]
        .add(lift_half * above)
    )
    high_y = along_y[:, size_y:]
    along_x = jnp.einsum("cyxz,wx->cywz", velocity, pair_x, precision=highest)
    grad_x = (
        along_x[:, :, :size_x]
        .at[:, :, 0]
        .add(-lift_half * left_face)
        .at[:, :, size_x - 1]
        .add(lift_half * right_face)
    )
    high_x = along_x[:, :, size_x:]
    along_z = jnp.einsum("cyxz,wz->cyxw", velocity, pair_z, precision=highest)
    grad_z = along_z[..., :size_z]
    high_z = along_z[..., size_z:]
    advect = velocity[0][None] * grad_x + velocity[1][None] * grad_y + velocity[2][None] * grad_z
    new_field = velocity + time_step * (-advect - relax_rate * (high_x + high_y + high_z))
    rows_y, rows_x, rows_z = (size_y // PY, size_x // PX, size_z // PZ)
    tangent = jnp.stack([velocity[0], velocity[2]]).reshape(2, rows_y, PY, rows_x, PX, rows_z, PZ)
    blocks = tangent.transpose(1, 3, 5, 0, 2, 4, 6).reshape(-1, 2 * PY * PX * PZ)
    slope_wall = jnp.stack([grad_y[0], grad_y[2]]).reshape(2, rows_y, PY, rows_x, PX, rows_z, PZ)
    stress_true = (
        (viscosity * jnp.mean(slope_wall, axis=(2, 4, 6))).transpose(1, 2, 3, 0).reshape(-1, 2)
    )
    picked = sample_block.reshape(-1)
    members = sample_member.reshape(-1)
    patch_rows = jnp.take(blocks, picked, axis=0).astype(jnp.bfloat16)
    aim_rows = jnp.take(stress_true, picked, axis=0).astype(jnp.bfloat16)
    select = slot_matrix(members, wall_count)
    select_half = select.astype(jnp.bfloat16)
    send_rows = jnp.dot(select_half, patch_rows, preferred_element_type=jnp.float32).astype(
        jnp.bfloat16
    )
    send_aims = jnp.dot(select_half, aim_rows, preferred_element_type=jnp.float32).astype(
        jnp.bfloat16
    )
    send_valid = jnp.sum(select, axis=1).astype(jnp.bfloat16)
    new_field, send_rows, send_aims, send_valid = lax.optimization_barrier(
        (new_field, send_rows, send_aims, send_valid)
    )
    recv_rows, recv_aims, recv_valid = in_one_piece(
        (send_rows, send_aims, send_valid), "wall", 0, 0, 1
    )
    pred, grad_one, grad_two, grad_out, features, delta_three = forward_back(
        recv_rows, recv_aims, recv_valid, k_first[0], k_second[0], w_hidden[0], w_out[0]
    )
    back = lax.all_to_all(pred, "wall", split_axis=0, concat_axis=0, tiled=True)
    stress_local = jnp.dot(select.T, back, precision=highest)
    stress = stress_local.T[:, None, :]
    share_rows = FEATS // flow_count
    dense_scale = 1.0 / math.sqrt(1.0 * FEATS)
    small = jnp.concatenate([grad_one.ravel(), grad_out.ravel()])
    tiles = features.reshape(features.shape[0], flow_count, -1).transpose(1, 0, 2)
    grad_share, small_part, columns_here = owner_sums(grad_two.reshape(-1, CH), small, tiles, STREAM)
    grad_hidden = (
        jnp.dot(
            columns_here.T,
            lax.all_gather(delta_three, STREAM, axis=0, tiled=True),
            preferred_element_type=jnp.float32,
        )
        * dense_scale
    )
    own_rows = lax.dynamic_slice_in_dim(w_hidden[0], flow_place * share_rows, share_rows, 0)
    new_w_hidden = row_update(own_rows, grad_hidden)[None]
    share_count = grad_share.shape[0]
    kernel_own = lax.dynamic_slice_in_dim(
        k_second[0].reshape(-1, CH), flow_place * share_count, share_count, 0
    )
    updated_rows = row_update(kernel_own, grad_share)
    kernel_rows, small = shared_back(updated_rows, small_part, STREAM)
    new_k_second = kernel_rows.reshape(k_second.shape[1:])
    grad_one = small[: grad_one.size].reshape(grad_one.shape)
    grad_out = small[grad_one.size : grad_one.size + grad_out.size].reshape(grad_out.shape)
    new_k_first = row_update(k_first[0], grad_one)
    new_w_out = whole_update(w_out[0], grad_out)
    return (new_field, stress, new_k_first[None], new_k_second[None], new_w_hidden, new_w_out[None])


def solution(mesh):
    torus = Mesh(
        mesh.devices.reshape(mesh.shape["wall"], 8, 2, 2),
        ("wall", "stream_0", "stream_1", "stream_2"),
    )
    in_specs = (
        P(None, "wall", STREAM, None),
        P("wall", STREAM),
        P("wall", STREAM, None),
        P("wall", None, None),
        P("wall", None, None, None),
        P("wall", None, None),
        P("wall", None, None),
    )
    out_specs = (
        P(None, "wall", STREAM, None),
        P(None, "wall", STREAM),
        P("wall", None, None),
        P("wall", None, None, None),
        P("wall", STREAM, None),
        P("wall", None, None),
    )
    return jax.shard_map(body, mesh=torus, in_specs=in_specs, out_specs=out_specs, check_vma=False)
```

```python
import math

import jax
import jax.numpy as jnp
import numpy as np
from jax import lax
from jax.sharding import Mesh
from jax.sharding import PartitionSpec as P

P_SIZE = 8
PY = 4
PX = 4
PZ = 8
CH = 64
CAP = 2
FEATS = 2048
STREAM = ("stream_0", "stream_1", "stream_2")


highest = lax.Precision.HIGHEST
time_step = 0.005
relax_rate = 20.0
viscosity = 0.3
learn_rate = 0.5
rms_eps = 1e-06
def extended(shard, sides, width):
    edges = {}
    for axis, dim in sides:
        size, length = (lax.axis_size(axis), shard.shape[dim])
        up = [(i, (i + 1) % size) for i in range(size)]
        last = lax.slice_in_dim(shard, length - width, length, axis=dim)
        first = lax.slice_in_dim(shard, 0, width, axis=dim)
        edges[dim] = (
            lax.ppermute(last, axis, up),
            lax.ppermute(first, axis, [(b, a) for a, b in up]),
        )
    done = []
    for _, dim in sides:
        low, high = edges[dim]
        around = [(width, width) if d in done else (0, 0) for d in range(shard.ndim)]
        shard = jnp.concatenate([jnp.pad(low, around), shard, jnp.pad(high, around)], axis=dim)
        done.append(dim)
    return shard


def in_one_piece(arrays, axis, split_dim, concat_dim, along):
    widths = [math.prod(a.shape[along:]) for a in arrays]
    both = jnp.concatenate(
        [a.reshape(*a.shape[:along], w) for a, w in zip(arrays, widths)], axis=along
    )
    whole = lax.all_to_all(both, axis, split_axis=split_dim, concat_axis=concat_dim, tiled=True)
    tiles = jnp.split(whole, [sum(widths[:k]) for k in range(1, len(widths))], axis=along)
    return tuple((b.reshape(*whole.shape[:along], *a.shape[along:]) for a, b in zip(arrays, tiles)))


def joined_along(tiles, dim):
    lengths = list(tiles.shape[1:])
    lengths[dim] *= tiles.shape[0]
    return jnp.moveaxis(tiles, 0, dim).reshape(lengths)


def gather_in_order(shard, axes, order):
    tiles = shard
    for k in order:
        tiles = lax.all_gather(tiles, axes[k])
    done = order[::-1]
    back = [done.index(k) for k in range(len(axes))]
    tiles = tiles.transpose(*back, *range(len(axes), tiles.ndim))
    return tiles.reshape(-1, *shard.shape)


def gathered_by_axis(shard, axes, order, dim):
    return joined_along(gather_in_order(shard, axes, order), dim)


def from_everyone(shard, axis):
    copies = jnp.broadcast_to(shard, (lax.axis_size(axis), *shard.shape))
    return lax.all_to_all(copies, axis, split_axis=0, concat_axis=0, tiled=True)


def owner_sums(rows, small, tiles, axis):
    count = lax.axis_size(axis)
    spare = -small.size % count
    small = jnp.pad(small, (0, spare))
    summed = [rows.reshape(count, -1), small.reshape(count, -1)]
    width = sum(part.shape[1] for part in summed)
    both = jnp.concatenate(summed + [tiles.reshape(count, -1).astype(jnp.float32)], axis=1)
    arrived = lax.all_to_all(both, axis, split_axis=0, concat_axis=0, tiled=True)
    total = arrived[:, :width].sum(axis=0)
    part = rows.size // count
    moved = arrived[:, width:].astype(tiles.dtype).reshape(-1, *tiles.shape[2:])
    return total[:part].reshape(-1, rows.shape[-1]), total[part:], moved


def shared_back(rows, chunk, axis):
    everything = from_everyone(jnp.concatenate([rows.ravel(), chunk]), axis)
    whole_rows = everything[:, : rows.size].reshape(-1, rows.shape[-1])
    return whole_rows, everything[:, rows.size :].reshape(-1)


def cheb_tables(points):
    order = points - 1
    node_index = np.arange(points)
    nodes = -np.cos(np.pi * node_index / order)
    end_weight = np.where((node_index == 0) | (node_index == order), 2.0, 1.0)
    parity = (-1.0) ** (node_index[:, None] + node_index[None, :])
    offdiag = 1.0 - np.eye(points)
    spread = nodes[:, None] - nodes[None, :] + np.eye(points)
    deriv = end_weight[:, None] / end_weight[None, :] * parity / spread * offdiag
    deriv = deriv - np.eye(points) * deriv.sum(axis=1)[:, None]
    highpass = parity / (order * end_weight[None, :])
    return (deriv, highpass, 0.5 * order * order)


def axis_matrices(count, periodic):
    deriv, highpass, lift_half = cheb_tables(P_SIZE)
    length = count * P_SIZE
    slope = np.kron(np.eye(count), deriv)
    upper = np.kron(np.eye(count), highpass)
    faces = count if periodic else count - 1
    for element in range(faces):
        last_node = element * P_SIZE + P_SIZE - 1
        next_node = (element + 1) % count * P_SIZE
        slope[last_node, next_node] += lift_half
        slope[last_node, last_node] -= lift_half
        slope[next_node, last_node] -= lift_half
        slope[next_node, next_node] += lift_half
    if not periodic:
        slope[0, 0] += lift_half
        slope[length - 1, length - 1] -= lift_half
    paired = jnp.asarray(np.concatenate([slope, upper], axis=0), jnp.float32)
    return (paired, lift_half)


def slot_matrix(members, member_count):
    member_hot = (members[..., None] == jnp.arange(member_count, dtype=jnp.int32)).astype(jnp.int32)
    before = jnp.cumsum(member_hot, axis=-2) - member_hot
    ranks = jnp.sum(before * member_hot, axis=-1)
    slots = members * CAP + ranks
    return (slots[..., None, :] == jnp.arange(member_count * CAP, dtype=jnp.int32)[:, None]).astype(
        jnp.float32
    )


DIMS = ("NDHWC", "DHWIO", "NDHWC")
FILTER_DIMS = ("CDHWN", "IDHWO", "NDHWC")
SAME = ((1, 1), (1, 1), (1, 1))


def silu_slope(value):
    gate = jax.nn.sigmoid(value)
    return gate * (1.0 + value * (1.0 - gate))


def conv_taps(grid, kernel):
    return lax.conv_general_dilated(
        grid, kernel, (1, 1, 1), SAME, dimension_numbers=DIMS,
        preferred_element_type=jnp.float32,
    )


def conv_filter(grid, delta):
    taps = lax.conv_general_dilated(
        grid, delta, (1, 1, 1), SAME, dimension_numbers=FILTER_DIMS,
        preferred_element_type=jnp.float32,
    )
    return jnp.moveaxis(taps, 0, 3)


def forward_back(patches, aim_rows, valid, k_first, k_second, w_hidden, w_out):
    batch = patches.shape[0]
    channels = k_second.shape[-1]
    inputs = patches.reshape(batch, 2, PY, PX, PZ).transpose(0, 2, 3, 4, 1)
    first_taps = k_first.reshape(3, 3, 3, 2, channels)
    second_taps = k_second.reshape(3, 3, 3, channels, channels)
    scale_one = 1.0 / math.sqrt(54.0)
    scale_two = 1.0 / math.sqrt(27.0 * channels)
    scale_three = 1.0 / math.sqrt(1.0 * w_hidden.shape[0])
    scale_four = 1.0 / math.sqrt(1.0 * w_hidden.shape[1])
    pre_one = conv_taps(inputs, first_taps) * scale_one
    hidden_one = jax.nn.silu(pre_one).astype(jnp.bfloat16)
    pre_two = conv_taps(hidden_one, second_taps) * scale_two
    pooled = jax.nn.silu(pre_two).reshape(batch, PY // 2, 2, PX // 2, 2, PZ, channels).mean(axis=(2, 4))
    features = pooled.reshape(batch, -1).astype(jnp.bfloat16)
    pre_three = jnp.dot(features, w_hidden, preferred_element_type=jnp.float32) * scale_three
    hidden_three = jax.nn.silu(pre_three).astype(jnp.bfloat16)
    pred = jnp.dot(hidden_three, w_out, preferred_element_type=jnp.float32) * scale_four
    error = valid.astype(jnp.float32)[:, None] * (pred - aim_rows.astype(jnp.float32))
    grad_out = jnp.dot(hidden_three.astype(jnp.float32).T, error, precision=highest) * scale_four
    delta_three = (
        jnp.dot(error, w_out.astype(jnp.float32).T, precision=highest) * scale_four * silu_slope(pre_three)
    ).astype(jnp.bfloat16)
    back_feat = jnp.dot(delta_three, w_hidden.T, preferred_element_type=jnp.float32) * scale_three
    back_grid = back_feat.reshape(batch, PY // 2, 1, PX // 2, 1, PZ, channels)
    spread_back = jnp.broadcast_to(back_grid, (batch, PY // 2, 2, PX // 2, 2, PZ, channels)).reshape(pre_two.shape) * 0.25
    delta_two = (spread_back * silu_slope(pre_two)).astype(jnp.bfloat16)
    grad_two = (conv_filter(hidden_one, delta_two) * scale_two).reshape(27, channels, channels)
    mirrored = jnp.flip(second_taps, axis=(0, 1, 2)).swapaxes(3, 4)
    back_one = conv_taps(delta_two, mirrored)
    delta_one = (back_one * scale_two * silu_slope(pre_one)).astype(jnp.bfloat16)
    grad_one = (conv_filter(inputs, delta_one) * scale_one).reshape(54, channels)
    return (pred, grad_one, grad_two, grad_out, features, delta_three)


def row_update(weight, grad):
    scale = jnp.sqrt(jnp.mean(grad * grad, axis=-1, keepdims=True) + rms_eps)
    return weight.astype(jnp.float32) - learn_rate * grad / scale


def whole_update(weight, grad):
    scale = jnp.sqrt(jnp.mean(grad * grad) + rms_eps)
    return weight.astype(jnp.float32) - learn_rate * grad / scale


def body(velocity, sample_block, sample_member, k_first, k_second, w_hidden, w_out):
    wall_count = lax.axis_size("wall")
    wall_place = lax.axis_index("wall")
    flow_count = lax.axis_size(STREAM)
    flow_place = lax.axis_index(STREAM)
    padded = extended(velocity, (("wall", 1), (STREAM, 2)), 1)
    keep_low = (wall_place > 0).astype(jnp.float32)
    keep_high = (wall_place < wall_count - 1).astype(jnp.float32)
    below = padded[:, 0, 1:-1, :] * keep_low
    above = padded[:, -1, 1:-1, :] * keep_high
    left_face = padded[:, 1:-1, 0, :]
    right_face = padded[:, 1:-1, -1, :]
    size_y, size_x, size_z = (velocity.shape[1], velocity.shape[2], velocity.shape[3])
    pair_y, lift_half = axis_matrices(size_y // P_SIZE, False)
    pair_x, lift_same = axis_matrices(size_x // P_SIZE, False)
    pair_z, lift_again = axis_matrices(size_z // P_SIZE, True)
    along_y = jnp.einsum("cyxz,wy->cwxz", velocity, pair_y, precision=highest)
    grad_y = (
        along_y[:, :size_y]
        .at[:, 0]
        .add(-lift_half * below)
        .at[:, size_y - 1]
        .add(lift_half * above)
    )
    high_y = along_y[:, size_y:]
    along_x = jnp.einsum("cyxz,wx->cywz", velocity, pair_x, precision=highest)
    grad_x = (
        along_x[:, :, :size_x]
        .at[:, :, 0]
        .add(-lift_half * left_face)
        .at[:, :, size_x - 1]
        .add(lift_half * right_face)
    )
    high_x = along_x[:, :, size_x:]
    along_z = jnp.einsum("cyxz,wz->cyxw", velocity, pair_z, precision=highest)
    grad_z = along_z[..., :size_z]
    high_z = along_z[..., size_z:]
    advect = velocity[0][None] * grad_x + velocity[1][None] * grad_y + velocity[2][None] * grad_z
    new_field = velocity + time_step * (-advect - relax_rate * (high_x + high_y + high_z))
    rows_y, rows_x, rows_z = (size_y // PY, size_x // PX, size_z // PZ)
    tangent = jnp.stack([velocity[0], velocity[2]]).reshape(2, rows_y, PY, rows_x, PX, rows_z, PZ)
    blocks = tangent.transpose(1, 3, 5, 0, 2, 4, 6).reshape(-1, 2 * PY * PX * PZ)
    slope_wall = jnp.stack([grad_y[0], grad_y[2]]).reshape(2, rows_y, PY, rows_x, PX, rows_z, PZ)
    stress_true = (
        (viscosity * jnp.mean(slope_wall, axis=(2, 4, 6))).transpose(1, 2, 3, 0).reshape(-1, 2)
    )
    picked = sample_block.reshape(-1)
    members = sample_member.reshape(-1)
    patch_rows = jnp.take(blocks, picked, axis=0).astype(jnp.bfloat16)
    aim_rows = jnp.take(stress_true, picked, axis=0).astype(jnp.bfloat16)
    select = slot_matrix(members, wall_count)
    select_half = select.astype(jnp.bfloat16)
    send_rows = jnp.dot(select_half, patch_rows, preferred_element_type=jnp.float32).astype(
        jnp.bfloat16
    )
    send_aims = jnp.dot(select_half, aim_rows, preferred_element_type=jnp.float32).astype(
        jnp.bfloat16
    )
    send_valid = jnp.sum(select, axis=1).astype(jnp.bfloat16)
    new_field, send_rows, send_aims, send_valid = lax.optimization_barrier(
        (new_field, send_rows, send_aims, send_valid)
    )
    recv_rows, recv_aims, recv_valid = in_one_piece(
        (send_rows, send_aims, send_valid), "wall", 0, 0, 1
    )
    pred, grad_one, grad_two, grad_out, features, delta_three = forward_back(
        recv_rows, recv_aims, recv_valid, k_first[0], k_second[0], w_hidden[0], w_out[0]
    )
    back = lax.all_to_all(pred, "wall", split_axis=0, concat_axis=0, tiled=True)
    stress_local = jnp.dot(select.T, back, precision=highest)
    stress = stress_local.T[:, None, :]
    share_rows = FEATS // flow_count
    dense_scale = 1.0 / math.sqrt(1.0 * FEATS)
    small = jnp.concatenate([grad_one.ravel(), grad_out.ravel()])
    tiles = features.reshape(features.shape[0], flow_count, -1).transpose(1, 0, 2)
    grad_share, small_part, columns_here = owner_sums(grad_two.reshape(-1, CH), small, tiles, STREAM)
    grad_hidden = (
        jnp.dot(
            columns_here.T,
            gathered_by_axis(delta_three, STREAM, (1, 0, 2), 0),
            preferred_element_type=jnp.float32,
        )
        * dense_scale
    )
    own_rows = lax.dynamic_slice_in_dim(w_hidden[0], flow_place * share_rows, share_rows, 0)
    new_w_hidden = row_update(own_rows, grad_hidden)[None]
    share_count = grad_share.shape[0]
    kernel_own = lax.dynamic_slice_in_dim(
        k_second[0].reshape(-1, CH), flow_place * share_count, share_count, 0
    )
    updated_rows = row_update(kernel_own, grad_share)
    kernel_rows, small = shared_back(updated_rows, small_part, STREAM)
    new_k_second = kernel_rows.reshape(k_second.shape[1:])
    grad_one = small[: grad_one.size].reshape(grad_one.shape)
    grad_out = small[grad_one.size : grad_one.size + grad_out.size].reshape(grad_out.shape)
    new_k_first = row_update(k_first[0], grad_one)
    new_w_out = whole_update(w_out[0], grad_out)
    return (new_field, stress, new_k_first[None], new_k_second[None], new_w_hidden, new_w_out[None])


def solution(mesh):
    torus = Mesh(
        mesh.devices.reshape(mesh.shape["wall"], 8, 2, 2),
        ("wall", "stream_0", "stream_1", "stream_2"),
    )
    in_specs = (
        P(None, "wall", STREAM, None),
        P("wall", STREAM),
        P("wall", STREAM, None),
        P("wall", None, None),
        P("wall", None, None, None),
        P("wall", None, None),
        P("wall", None, None),
    )
    out_specs = (
        P(None, "wall", STREAM, None),
        P(None, "wall", STREAM),
        P("wall", None, None),
        P("wall", None, None, None),
        P("wall", STREAM, None),
        P("wall", None, None),
    )
    return jax.shard_map(body, mesh=torus, in_specs=in_specs, out_specs=out_specs, check_vma=False)
```

```python
import math

import jax
import jax.numpy as jnp
import numpy as np
from jax import lax
from jax.sharding import Mesh
from jax.sharding import PartitionSpec as P

P_SIZE = 8
PY = 4
PX = 4
PZ = 8
CH = 64
CAP = 2
FEATS = 2048
STREAM = ("stream_0", "stream_1", "stream_2")


highest = lax.Precision.HIGHEST
time_step = 0.005
relax_rate = 20.0
viscosity = 0.3
learn_rate = 0.5
rms_eps = 1e-06
def extended(shard, sides, width):
    edges = {}
    for axis, dim in sides:
        size, length = (lax.axis_size(axis), shard.shape[dim])
        up = [(i, (i + 1) % size) for i in range(size)]
        last = lax.slice_in_dim(shard, length - width, length, axis=dim)
        first = lax.slice_in_dim(shard, 0, width, axis=dim)
        edges[dim] = (
            lax.ppermute(last, axis, up),
            lax.ppermute(first, axis, [(b, a) for a, b in up]),
        )
    done = []
    for _, dim in sides:
        low, high = edges[dim]
        around = [(width, width) if d in done else (0, 0) for d in range(shard.ndim)]
        shard = jnp.concatenate([jnp.pad(low, around), shard, jnp.pad(high, around)], axis=dim)
        done.append(dim)
    return shard


def in_one_piece(arrays, axis, split_dim, concat_dim, along):
    widths = [math.prod(a.shape[along:]) for a in arrays]
    both = jnp.concatenate(
        [a.reshape(*a.shape[:along], w) for a, w in zip(arrays, widths)], axis=along
    )
    whole = lax.all_to_all(both, axis, split_axis=split_dim, concat_axis=concat_dim, tiled=True)
    tiles = jnp.split(whole, [sum(widths[:k]) for k in range(1, len(widths))], axis=along)
    return tuple((b.reshape(*whole.shape[:along], *a.shape[along:]) for a, b in zip(arrays, tiles)))


def joined_along(tiles, dim):
    lengths = list(tiles.shape[1:])
    lengths[dim] *= tiles.shape[0]
    return jnp.moveaxis(tiles, 0, dim).reshape(lengths)


def gather_in_order(shard, axes, order, started=None, stages=0):
    tiles = shard if started is None else started
    for k in order[stages:]:
        tiles = lax.all_gather(tiles, axes[k])
    done = order[::-1]
    back = [done.index(k) for k in range(len(axes))]
    tiles = tiles.transpose(*back, *range(len(axes), tiles.ndim))
    return tiles.reshape(-1, *shard.shape)


def gathered_by_axis(shard, axes, order, dim, started=None, stages=0):
    return joined_along(gather_in_order(shard, axes, order, started, stages), dim)


def from_everyone(shard, axis):
    copies = jnp.broadcast_to(shard, (lax.axis_size(axis), *shard.shape))
    return lax.all_to_all(copies, axis, split_axis=0, concat_axis=0, tiled=True)


def owner_sums(rows, small, tiles, axis):
    count = lax.axis_size(axis)
    spare = -small.size % count
    small = jnp.pad(small, (0, spare))
    summed = [rows.reshape(count, -1), small.reshape(count, -1)]
    width = sum(part.shape[1] for part in summed)
    both = jnp.concatenate(summed + [tiles.reshape(count, -1).astype(jnp.float32)], axis=1)
    arrived = lax.all_to_all(both, axis, split_axis=0, concat_axis=0, tiled=True)
    total = arrived[:, :width].sum(axis=0)
    part = rows.size // count
    moved = arrived[:, width:].astype(tiles.dtype).reshape(-1, *tiles.shape[2:])
    return total[:part].reshape(-1, rows.shape[-1]), total[part:], moved


def shared_back(rows, chunk, axis):
    everything = from_everyone(jnp.concatenate([rows.ravel(), chunk]), axis)
    whole_rows = everything[:, : rows.size].reshape(-1, rows.shape[-1])
    return whole_rows, everything[:, rows.size :].reshape(-1)


def cheb_tables(points):
    order = points - 1
    node_index = np.arange(points)
    nodes = -np.cos(np.pi * node_index / order)
    end_weight = np.where((node_index == 0) | (node_index == order), 2.0, 1.0)
    parity = (-1.0) ** (node_index[:, None] + node_index[None, :])
    offdiag = 1.0 - np.eye(points)
    spread = nodes[:, None] - nodes[None, :] + np.eye(points)
    deriv = end_weight[:, None] / end_weight[None, :] * parity / spread * offdiag
    deriv = deriv - np.eye(points) * deriv.sum(axis=1)[:, None]
    highpass = parity / (order * end_weight[None, :])
    return (deriv, highpass, 0.5 * order * order)


def axis_matrices(count, periodic):
    deriv, highpass, lift_half = cheb_tables(P_SIZE)
    length = count * P_SIZE
    slope = np.kron(np.eye(count), deriv)
    upper = np.kron(np.eye(count), highpass)
    faces = count if periodic else count - 1
    for element in range(faces):
        last_node = element * P_SIZE + P_SIZE - 1
        next_node = (element + 1) % count * P_SIZE
        slope[last_node, next_node] += lift_half
        slope[last_node, last_node] -= lift_half
        slope[next_node, last_node] -= lift_half
        slope[next_node, next_node] += lift_half
    if not periodic:
        slope[0, 0] += lift_half
        slope[length - 1, length - 1] -= lift_half
    paired = jnp.asarray(np.concatenate([slope, upper], axis=0), jnp.float32)
    return (paired, lift_half)


def slot_matrix(members, member_count):
    member_hot = (members[..., None] == jnp.arange(member_count, dtype=jnp.int32)).astype(jnp.int32)
    before = jnp.cumsum(member_hot, axis=-2) - member_hot
    ranks = jnp.sum(before * member_hot, axis=-1)
    slots = members * CAP + ranks
    return (slots[..., None, :] == jnp.arange(member_count * CAP, dtype=jnp.int32)[:, None]).astype(
        jnp.float32
    )


DIMS = ("NDHWC", "DHWIO", "NDHWC")
FILTER_DIMS = ("CDHWN", "IDHWO", "NDHWC")
SAME = ((1, 1), (1, 1), (1, 1))


def silu_slope(value):
    gate = jax.nn.sigmoid(value)
    return gate * (1.0 + value * (1.0 - gate))


def conv_taps(grid, kernel):
    return lax.conv_general_dilated(
        grid, kernel, (1, 1, 1), SAME, dimension_numbers=DIMS,
        preferred_element_type=jnp.float32,
    )


def conv_filter(grid, delta):
    taps = lax.conv_general_dilated(
        grid, delta, (1, 1, 1), SAME, dimension_numbers=FILTER_DIMS,
        preferred_element_type=jnp.float32,
    )
    return jnp.moveaxis(taps, 0, 3)


def forward_back(patches, aim_rows, valid, k_first, k_second, w_hidden, w_out, early):
    batch = patches.shape[0]
    channels = k_second.shape[-1]
    inputs = patches.reshape(batch, 2, PY, PX, PZ).transpose(0, 2, 3, 4, 1)
    first_taps = k_first.reshape(3, 3, 3, 2, channels)
    second_taps = k_second.reshape(3, 3, 3, channels, channels)
    scale_one = 1.0 / math.sqrt(54.0)
    scale_two = 1.0 / math.sqrt(27.0 * channels)
    scale_three = 1.0 / math.sqrt(1.0 * w_hidden.shape[0])
    scale_four = 1.0 / math.sqrt(1.0 * w_hidden.shape[1])
    pre_one = conv_taps(inputs, first_taps) * scale_one
    hidden_one = jax.nn.silu(pre_one).astype(jnp.bfloat16)
    pre_two = conv_taps(hidden_one, second_taps) * scale_two
    pooled = jax.nn.silu(pre_two).reshape(batch, PY // 2, 2, PX // 2, 2, PZ, channels).mean(axis=(2, 4))
    features = pooled.reshape(batch, -1).astype(jnp.bfloat16)
    pre_three = jnp.dot(features, w_hidden, preferred_element_type=jnp.float32) * scale_three
    hidden_three = jax.nn.silu(pre_three).astype(jnp.bfloat16)
    pred = jnp.dot(hidden_three, w_out, preferred_element_type=jnp.float32) * scale_four
    error = valid.astype(jnp.float32)[:, None] * (pred - aim_rows.astype(jnp.float32))
    grad_out = jnp.dot(hidden_three.astype(jnp.float32).T, error, precision=highest) * scale_four
    delta_three = (
        jnp.dot(error, w_out.astype(jnp.float32).T, precision=highest) * scale_four * silu_slope(pre_three)
    ).astype(jnp.bfloat16)
    delta_three, started = lax.optimization_barrier((delta_three, early(delta_three)))
    back_feat = jnp.dot(delta_three, w_hidden.T, preferred_element_type=jnp.float32) * scale_three
    back_grid = back_feat.reshape(batch, PY // 2, 1, PX // 2, 1, PZ, channels)
    spread_back = jnp.broadcast_to(back_grid, (batch, PY // 2, 2, PX // 2, 2, PZ, channels)).reshape(pre_two.shape) * 0.25
    delta_two = (spread_back * silu_slope(pre_two)).astype(jnp.bfloat16)
    grad_two = (conv_filter(hidden_one, delta_two) * scale_two).reshape(27, channels, channels)
    mirrored = jnp.flip(second_taps, axis=(0, 1, 2)).swapaxes(3, 4)
    back_one = conv_taps(delta_two, mirrored)
    delta_one = (back_one * scale_two * silu_slope(pre_one)).astype(jnp.bfloat16)
    grad_one = (conv_filter(inputs, delta_one) * scale_one).reshape(54, channels)
    return (pred, grad_one, grad_two, grad_out, features, delta_three, started)


def row_update(weight, grad):
    scale = jnp.sqrt(jnp.mean(grad * grad, axis=-1, keepdims=True) + rms_eps)
    return weight.astype(jnp.float32) - learn_rate * grad / scale


def whole_update(weight, grad):
    scale = jnp.sqrt(jnp.mean(grad * grad) + rms_eps)
    return weight.astype(jnp.float32) - learn_rate * grad / scale


def body(velocity, sample_block, sample_member, k_first, k_second, w_hidden, w_out):
    wall_count = lax.axis_size("wall")
    wall_place = lax.axis_index("wall")
    flow_count = lax.axis_size(STREAM)
    flow_place = lax.axis_index(STREAM)
    padded = extended(velocity, (("wall", 1), (STREAM, 2)), 1)
    keep_low = (wall_place > 0).astype(jnp.float32)
    keep_high = (wall_place < wall_count - 1).astype(jnp.float32)
    below = padded[:, 0, 1:-1, :] * keep_low
    above = padded[:, -1, 1:-1, :] * keep_high
    left_face = padded[:, 1:-1, 0, :]
    right_face = padded[:, 1:-1, -1, :]
    size_y, size_x, size_z = (velocity.shape[1], velocity.shape[2], velocity.shape[3])
    pair_y, lift_half = axis_matrices(size_y // P_SIZE, False)
    pair_x, lift_same = axis_matrices(size_x // P_SIZE, False)
    pair_z, lift_again = axis_matrices(size_z // P_SIZE, True)
    along_y = jnp.einsum("cyxz,wy->cwxz", velocity, pair_y, precision=highest)
    grad_y = (
        along_y[:, :size_y]
        .at[:, 0]
        .add(-lift_half * below)
        .at[:, size_y - 1]
        .add(lift_half * above)
    )
    high_y = along_y[:, size_y:]
    along_x = jnp.einsum("cyxz,wx->cywz", velocity, pair_x, precision=highest)
    grad_x = (
        along_x[:, :, :size_x]
        .at[:, :, 0]
        .add(-lift_half * left_face)
        .at[:, :, size_x - 1]
        .add(lift_half * right_face)
    )
    high_x = along_x[:, :, size_x:]
    along_z = jnp.einsum("cyxz,wz->cyxw", velocity, pair_z, precision=highest)
    grad_z = along_z[..., :size_z]
    high_z = along_z[..., size_z:]
    advect = velocity[0][None] * grad_x + velocity[1][None] * grad_y + velocity[2][None] * grad_z
    new_field = velocity + time_step * (-advect - relax_rate * (high_x + high_y + high_z))
    rows_y, rows_x, rows_z = (size_y // PY, size_x // PX, size_z // PZ)
    tangent = jnp.stack([velocity[0], velocity[2]]).reshape(2, rows_y, PY, rows_x, PX, rows_z, PZ)
    blocks = tangent.transpose(1, 3, 5, 0, 2, 4, 6).reshape(-1, 2 * PY * PX * PZ)
    slope_wall = jnp.stack([grad_y[0], grad_y[2]]).reshape(2, rows_y, PY, rows_x, PX, rows_z, PZ)
    stress_true = (
        (viscosity * jnp.mean(slope_wall, axis=(2, 4, 6))).transpose(1, 2, 3, 0).reshape(-1, 2)
    )
    picked = sample_block.reshape(-1)
    members = sample_member.reshape(-1)
    patch_rows = jnp.take(blocks, picked, axis=0).astype(jnp.bfloat16)
    aim_rows = jnp.take(stress_true, picked, axis=0).astype(jnp.bfloat16)
    select = slot_matrix(members, wall_count)
    select_half = select.astype(jnp.bfloat16)
    send_rows = jnp.dot(select_half, patch_rows, preferred_element_type=jnp.float32).astype(
        jnp.bfloat16
    )
    send_aims = jnp.dot(select_half, aim_rows, preferred_element_type=jnp.float32).astype(
        jnp.bfloat16
    )
    send_valid = jnp.sum(select, axis=1).astype(jnp.bfloat16)
    new_field, send_rows, send_aims, send_valid = lax.optimization_barrier(
        (new_field, send_rows, send_aims, send_valid)
    )
    recv_rows, recv_aims, recv_valid = in_one_piece(
        (send_rows, send_aims, send_valid), "wall", 0, 0, 1
    )
    gather_order = (1, 0, 2)
    pred, grad_one, grad_two, grad_out, features, delta_three, started = forward_back(
        recv_rows, recv_aims, recv_valid, k_first[0], k_second[0], w_hidden[0], w_out[0],
        lambda delta: lax.all_gather(delta, STREAM[gather_order[0]]),
    )
    back = lax.all_to_all(pred, "wall", split_axis=0, concat_axis=0, tiled=True)
    stress_local = jnp.dot(select.T, back, precision=highest)
    stress = stress_local.T[:, None, :]
    share_rows = FEATS // flow_count
    dense_scale = 1.0 / math.sqrt(1.0 * FEATS)
    small = jnp.concatenate([grad_one.ravel(), grad_out.ravel()])
    tiles = features.reshape(features.shape[0], flow_count, -1).transpose(1, 0, 2)
    started = lax.all_gather(started, STREAM[gather_order[1]])
    started, grad_two, small, tiles = lax.optimization_barrier((started, grad_two, small, tiles))
    grad_share, small_part, columns_here = owner_sums(grad_two.reshape(-1, CH), small, tiles, STREAM)
    grad_hidden = (
        jnp.dot(
            columns_here.T,
            gathered_by_axis(delta_three, STREAM, gather_order, 0, started, 2),
            preferred_element_type=jnp.float32,
        )
        * dense_scale
    )
    own_rows = lax.dynamic_slice_in_dim(w_hidden[0], flow_place * share_rows, share_rows, 0)
    new_w_hidden = row_update(own_rows, grad_hidden)[None]
    share_count = grad_share.shape[0]
    kernel_own = lax.dynamic_slice_in_dim(
        k_second[0].reshape(-1, CH), flow_place * share_count, share_count, 0
    )
    updated_rows = row_update(kernel_own, grad_share)
    kernel_rows, small = shared_back(updated_rows, small_part, STREAM)
    new_k_second = kernel_rows.reshape(k_second.shape[1:])
    grad_one = small[: grad_one.size].reshape(grad_one.shape)
    grad_out = small[grad_one.size : grad_one.size + grad_out.size].reshape(grad_out.shape)
    new_k_first = row_update(k_first[0], grad_one)
    new_w_out = whole_update(w_out[0], grad_out)
    return (new_field, stress, new_k_first[None], new_k_second[None], new_w_hidden, new_w_out[None])


def solution(mesh):
    torus = Mesh(
        mesh.devices.reshape(mesh.shape["wall"], 8, 2, 2),
        ("wall", "stream_0", "stream_1", "stream_2"),
    )
    in_specs = (
        P(None, "wall", STREAM, None),
        P("wall", STREAM),
        P("wall", STREAM, None),
        P("wall", None, None),
        P("wall", None, None, None),
        P("wall", None, None),
        P("wall", None, None),
    )
    out_specs = (
        P(None, "wall", STREAM, None),
        P(None, "wall", STREAM),
        P("wall", None, None),
        P("wall", None, None, None),
        P("wall", STREAM, None),
        P("wall", None, None),
    )
    return jax.shard_map(body, mesh=torus, in_specs=in_specs, out_specs=out_specs, check_vma=False)
```

```python
import math

import jax
import jax.numpy as jnp
import numpy as np
from jax import lax
from jax.sharding import Mesh
from jax.sharding import PartitionSpec as P

P_SIZE = 8
PY = 4
PX = 4
PZ = 8
CH = 64
CAP = 2
FEATS = 2048
STREAM = ("stream_0", "stream_1", "stream_2")


highest = lax.Precision.HIGHEST
time_step = 0.005
relax_rate = 20.0
viscosity = 0.3
learn_rate = 0.5
rms_eps = 1e-06
def extended(shard, sides, width):
    edges = {}
    for axis, dim in sides:
        size, length = (lax.axis_size(axis), shard.shape[dim])
        up = [(i, (i + 1) % size) for i in range(size)]
        last = lax.slice_in_dim(shard, length - width, length, axis=dim)
        first = lax.slice_in_dim(shard, 0, width, axis=dim)
        edges[dim] = (
            lax.ppermute(last, axis, up),
            lax.ppermute(first, axis, [(b, a) for a, b in up]),
        )
    done = []
    for _, dim in sides:
        low, high = edges[dim]
        around = [(width, width) if d in done else (0, 0) for d in range(shard.ndim)]
        shard = jnp.concatenate([jnp.pad(low, around), shard, jnp.pad(high, around)], axis=dim)
        done.append(dim)
    return shard


def in_one_piece(arrays, axis, split_dim, concat_dim, along):
    widths = [math.prod(a.shape[along:]) for a in arrays]
    both = jnp.concatenate(
        [a.reshape(*a.shape[:along], w) for a, w in zip(arrays, widths)], axis=along
    )
    whole = lax.all_to_all(both, axis, split_axis=split_dim, concat_axis=concat_dim, tiled=True)
    tiles = jnp.split(whole, [sum(widths[:k]) for k in range(1, len(widths))], axis=along)
    return tuple((b.reshape(*whole.shape[:along], *a.shape[along:]) for a, b in zip(arrays, tiles)))


def joined_along(tiles, dim):
    lengths = list(tiles.shape[1:])
    lengths[dim] *= tiles.shape[0]
    return jnp.moveaxis(tiles, 0, dim).reshape(lengths)


def gather_in_order(shard, axes, order):
    tiles = shard
    for k in order:
        tiles = lax.all_gather(tiles, axes[k])
    done = order[::-1]
    back = [done.index(k) for k in range(len(axes))]
    tiles = tiles.transpose(*back, *range(len(axes), tiles.ndim))
    return tiles.reshape(-1, *shard.shape)


def gathered_by_axis(shard, axes, order, dim):
    return joined_along(gather_in_order(shard, axes, order), dim)


def from_everyone(shard, axis):
    copies = jnp.broadcast_to(shard, (lax.axis_size(axis), *shard.shape))
    return lax.all_to_all(copies, axis, split_axis=0, concat_axis=0, tiled=True)


def owner_sums(rows, small, tiles, axis):
    count = lax.axis_size(axis)
    spare = -small.size % count
    small = jnp.pad(small, (0, spare))
    summed = [rows.reshape(count, -1), small.reshape(count, -1)]
    width = sum(part.shape[1] for part in summed)
    both = jnp.concatenate(summed + [tiles.reshape(count, -1).astype(jnp.float32)], axis=1)
    arrived = lax.all_to_all(both, axis, split_axis=0, concat_axis=0, tiled=True)
    total = arrived[:, :width].sum(axis=0)
    part = rows.size // count
    moved = arrived[:, width:].astype(tiles.dtype).reshape(-1, *tiles.shape[2:])
    return total[:part].reshape(-1, rows.shape[-1]), total[part:], moved


def shared_back(rows, chunk, axis):
    everything = from_everyone(jnp.concatenate([rows.ravel(), chunk]), axis)
    whole_rows = everything[:, : rows.size].reshape(-1, rows.shape[-1])
    return whole_rows, everything[:, rows.size :].reshape(-1)


def cheb_tables(points):
    order = points - 1
    node_index = np.arange(points)
    nodes = -np.cos(np.pi * node_index / order)
    end_weight = np.where((node_index == 0) | (node_index == order), 2.0, 1.0)
    parity = (-1.0) ** (node_index[:, None] + node_index[None, :])
    offdiag = 1.0 - np.eye(points)
    spread = nodes[:, None] - nodes[None, :] + np.eye(points)
    deriv = end_weight[:, None] / end_weight[None, :] * parity / spread * offdiag
    deriv = deriv - np.eye(points) * deriv.sum(axis=1)[:, None]
    highpass = parity / (order * end_weight[None, :])
    return (deriv, highpass, 0.5 * order * order)


def axis_matrices(count, periodic):
    deriv, highpass, lift_half = cheb_tables(P_SIZE)
    length = count * P_SIZE
    slope = np.kron(np.eye(count), deriv)
    upper = np.kron(np.eye(count), highpass)
    faces = count if periodic else count - 1
    for element in range(faces):
        last_node = element * P_SIZE + P_SIZE - 1
        next_node = (element + 1) % count * P_SIZE
        slope[last_node, next_node] += lift_half
        slope[last_node, last_node] -= lift_half
        slope[next_node, last_node] -= lift_half
        slope[next_node, next_node] += lift_half
    if not periodic:
        slope[0, 0] += lift_half
        slope[length - 1, length - 1] -= lift_half
    paired = jnp.asarray(np.concatenate([slope, upper], axis=0), jnp.float32)
    return (paired, lift_half)


def slot_matrix(members, member_count):
    member_hot = (members[..., None] == jnp.arange(member_count, dtype=jnp.int32)).astype(jnp.int32)
    before = jnp.cumsum(member_hot, axis=-2) - member_hot
    ranks = jnp.sum(before * member_hot, axis=-1)
    slots = members * CAP + ranks
    return (slots[..., None, :] == jnp.arange(member_count * CAP, dtype=jnp.int32)[:, None]).astype(
        jnp.float32
    )


DIMS = ("NDHWC", "DHWIO", "NDHWC")
FILTER_DIMS = ("CDHWN", "IDHWO", "NDHWC")
SAME = ((1, 1), (1, 1), (1, 1))


def silu_slope(value):
    gate = jax.nn.sigmoid(value)
    return gate * (1.0 + value * (1.0 - gate))


def conv_taps(grid, kernel):
    return lax.conv_general_dilated(
        grid, kernel, (1, 1, 1), SAME, dimension_numbers=DIMS,
        preferred_element_type=jnp.float32,
    )


def conv_filter(grid, delta):
    taps = lax.conv_general_dilated(
        grid, delta, (1, 1, 1), SAME, dimension_numbers=FILTER_DIMS,
        preferred_element_type=jnp.float32,
    )
    return jnp.moveaxis(taps, 0, 3)


def forward_back(patches, aim_rows, valid, k_first, k_second, w_hidden, w_out):
    batch = patches.shape[0]
    channels = k_second.shape[-1]
    inputs = patches.reshape(batch, 2, PY, PX, PZ).transpose(0, 2, 3, 4, 1)
    first_taps = k_first.reshape(3, 3, 3, 2, channels)
    second_taps = k_second.reshape(3, 3, 3, channels, channels)
    scale_one = 1.0 / math.sqrt(54.0)
    scale_two = 1.0 / math.sqrt(27.0 * channels)
    scale_three = 1.0 / math.sqrt(1.0 * w_hidden.shape[0])
    scale_four = 1.0 / math.sqrt(1.0 * w_hidden.shape[1])
    pre_one = conv_taps(inputs, first_taps) * scale_one
    hidden_one = jax.nn.silu(pre_one).astype(jnp.bfloat16)
    pre_two = conv_taps(hidden_one, second_taps) * scale_two
    pooled = jax.nn.silu(pre_two).reshape(batch, PY // 2, 2, PX // 2, 2, PZ, channels).mean(axis=(2, 4))
    features = pooled.reshape(batch, -1).astype(jnp.bfloat16)
    pre_three = jnp.dot(features, w_hidden, preferred_element_type=jnp.float32) * scale_three
    hidden_three = jax.nn.silu(pre_three).astype(jnp.bfloat16)
    pred = jnp.dot(hidden_three, w_out, preferred_element_type=jnp.float32) * scale_four
    error = valid.astype(jnp.float32)[:, None] * (pred - aim_rows.astype(jnp.float32))
    grad_out = jnp.dot(hidden_three.astype(jnp.float32).T, error, precision=highest) * scale_four
    delta_three = (
        jnp.dot(error, w_out.astype(jnp.float32).T, precision=highest) * scale_four * silu_slope(pre_three)
    ).astype(jnp.bfloat16)
    back_feat = jnp.dot(delta_three, w_hidden.T, preferred_element_type=jnp.float32) * scale_three
    back_grid = back_feat.reshape(batch, PY // 2, 1, PX // 2, 1, PZ, channels)
    spread_back = jnp.broadcast_to(back_grid, (batch, PY // 2, 2, PX // 2, 2, PZ, channels)).reshape(pre_two.shape) * 0.25
    delta_two = (spread_back * silu_slope(pre_two)).astype(jnp.bfloat16)
    grad_two = (conv_filter(hidden_one, delta_two) * scale_two).reshape(27, channels, channels)
    mirrored = jnp.flip(second_taps, axis=(0, 1, 2)).swapaxes(3, 4)
    back_one = conv_taps(delta_two, mirrored)
    delta_one = (back_one * scale_two * silu_slope(pre_one)).astype(jnp.bfloat16)
    grad_one = (conv_filter(inputs, delta_one) * scale_one).reshape(54, channels)
    return (pred, grad_one, grad_two, grad_out, features, delta_three)


def row_update(weight, grad):
    scale = jnp.sqrt(jnp.mean(grad * grad, axis=-1, keepdims=True) + rms_eps)
    return weight.astype(jnp.float32) - learn_rate * grad / scale


def whole_update(weight, grad):
    scale = jnp.sqrt(jnp.mean(grad * grad) + rms_eps)
    return weight.astype(jnp.float32) - learn_rate * grad / scale


def body(velocity, sample_block, sample_member, k_first, k_second, w_hidden, w_out):
    wall_count = lax.axis_size("wall")
    wall_place = lax.axis_index("wall")
    flow_count = lax.axis_size(STREAM)
    flow_place = lax.axis_index(STREAM)
    padded = extended(velocity, (("wall", 1), (STREAM, 2)), 1)
    keep_low = (wall_place > 0).astype(jnp.float32)
    keep_high = (wall_place < wall_count - 1).astype(jnp.float32)
    below = padded[:, 0, 1:-1, :] * keep_low
    above = padded[:, -1, 1:-1, :] * keep_high
    left_face = padded[:, 1:-1, 0, :]
    right_face = padded[:, 1:-1, -1, :]
    size_y, size_x, size_z = (velocity.shape[1], velocity.shape[2], velocity.shape[3])
    pair_y, lift_half = axis_matrices(size_y // P_SIZE, False)
    pair_x, lift_same = axis_matrices(size_x // P_SIZE, False)
    pair_z, lift_again = axis_matrices(size_z // P_SIZE, True)
    along_y = jnp.einsum("cyxz,wy->cwxz", velocity, pair_y, precision=highest)
    grad_y = (
        along_y[:, :size_y]
        .at[:, 0]
        .add(-lift_half * below)
        .at[:, size_y - 1]
        .add(lift_half * above)
    )
    high_y = along_y[:, size_y:]
    rows_y, rows_x, rows_z = (size_y // PY, size_x // PX, size_z // PZ)
    tangent = jnp.stack([velocity[0], velocity[2]]).reshape(2, rows_y, PY, rows_x, PX, rows_z, PZ)
    blocks = tangent.transpose(1, 3, 5, 0, 2, 4, 6).reshape(-1, 2 * PY * PX * PZ)
    slope_wall = jnp.stack([grad_y[0], grad_y[2]]).reshape(2, rows_y, PY, rows_x, PX, rows_z, PZ)
    stress_true = (
        (viscosity * jnp.mean(slope_wall, axis=(2, 4, 6))).transpose(1, 2, 3, 0).reshape(-1, 2)
    )
    picked = sample_block.reshape(-1)
    members = sample_member.reshape(-1)
    patch_rows = jnp.take(blocks, picked, axis=0).astype(jnp.bfloat16)
    aim_rows = jnp.take(stress_true, picked, axis=0).astype(jnp.bfloat16)
    select = slot_matrix(members, wall_count)
    select_half = select.astype(jnp.bfloat16)
    send_rows = jnp.dot(select_half, patch_rows, preferred_element_type=jnp.float32).astype(
        jnp.bfloat16
    )
    send_aims = jnp.dot(select_half, aim_rows, preferred_element_type=jnp.float32).astype(
        jnp.bfloat16
    )
    send_valid = jnp.sum(select, axis=1).astype(jnp.bfloat16)
    left_face, right_face, send_rows, send_aims, send_valid = lax.optimization_barrier(
        (left_face, right_face, send_rows, send_aims, send_valid)
    )
    along_x = jnp.einsum("cyxz,wx->cywz", velocity, pair_x, precision=highest)
    grad_x = (
        along_x[:, :, :size_x]
        .at[:, :, 0]
        .add(-lift_half * left_face)
        .at[:, :, size_x - 1]
        .add(lift_half * right_face)
    )
    high_x = along_x[:, :, size_x:]
    along_z = jnp.einsum("cyxz,wz->cyxw", velocity, pair_z, precision=highest)
    grad_z = along_z[..., :size_z]
    high_z = along_z[..., size_z:]
    advect = velocity[0][None] * grad_x + velocity[1][None] * grad_y + velocity[2][None] * grad_z
    new_field = velocity + time_step * (-advect - relax_rate * (high_x + high_y + high_z))
    recv_rows, recv_aims, recv_valid = in_one_piece(
        (send_rows, send_aims, send_valid), "wall", 0, 0, 1
    )
    pred, grad_one, grad_two, grad_out, features, delta_three = forward_back(
        recv_rows, recv_aims, recv_valid, k_first[0], k_second[0], w_hidden[0], w_out[0]
    )
    back = lax.all_to_all(pred, "wall", split_axis=0, concat_axis=0, tiled=True)
    stress_local = jnp.dot(select.T, back, precision=highest)
    stress = stress_local.T[:, None, :]
    share_rows = FEATS // flow_count
    dense_scale = 1.0 / math.sqrt(1.0 * FEATS)
    small = jnp.concatenate([grad_one.ravel(), grad_out.ravel()])
    tiles = features.reshape(features.shape[0], flow_count, -1).transpose(1, 0, 2)
    grad_share, small_part, columns_here = owner_sums(grad_two.reshape(-1, CH), small, tiles, STREAM)
    grad_hidden = (
        jnp.dot(
            columns_here.T,
            gathered_by_axis(delta_three, STREAM, (1, 0, 2), 0),
            preferred_element_type=jnp.float32,
        )
        * dense_scale
    )
    own_rows = lax.dynamic_slice_in_dim(w_hidden[0], flow_place * share_rows, share_rows, 0)
    new_w_hidden = row_update(own_rows, grad_hidden)[None]
    share_count = grad_share.shape[0]
    kernel_own = lax.dynamic_slice_in_dim(
        k_second[0].reshape(-1, CH), flow_place * share_count, share_count, 0
    )
    updated_rows = row_update(kernel_own, grad_share)
    kernel_rows, small = shared_back(updated_rows, small_part, STREAM)
    new_k_second = kernel_rows.reshape(k_second.shape[1:])
    grad_one = small[: grad_one.size].reshape(grad_one.shape)
    grad_out = small[grad_one.size : grad_one.size + grad_out.size].reshape(grad_out.shape)
    new_k_first = row_update(k_first[0], grad_one)
    new_w_out = whole_update(w_out[0], grad_out)
    return (new_field, stress, new_k_first[None], new_k_second[None], new_w_hidden, new_w_out[None])


def solution(mesh):
    torus = Mesh(
        mesh.devices.reshape(mesh.shape["wall"], 8, 2, 2),
        ("wall", "stream_0", "stream_1", "stream_2"),
    )
    in_specs = (
        P(None, "wall", STREAM, None),
        P("wall", STREAM),
        P("wall", STREAM, None),
        P("wall", None, None),
        P("wall", None, None, None),
        P("wall", None, None),
        P("wall", None, None),
    )
    out_specs = (
        P(None, "wall", STREAM, None),
        P(None, "wall", STREAM),
        P("wall", None, None),
        P("wall", None, None, None),
        P("wall", STREAM, None),
        P("wall", None, None),
    )
    return jax.shard_map(body, mesh=torus, in_specs=in_specs, out_specs=out_specs, check_vma=False)
```

```python
import math

import jax
import jax.numpy as jnp
import numpy as np
from jax import lax
from jax.sharding import Mesh
from jax.sharding import PartitionSpec as P

P_SIZE = 8
PY = 4
PX = 4
PZ = 8
CH = 64
CAP = 2
FEATS = 2048
STREAM = ("stream_0", "stream_1", "stream_2")


highest = lax.Precision.HIGHEST
time_step = 0.005
relax_rate = 20.0
viscosity = 0.3
learn_rate = 0.5
rms_eps = 1e-06
def extended(shard, sides, width):
    edges = {}
    for axis, dim in sides:
        size, length = (lax.axis_size(axis), shard.shape[dim])
        up = [(i, (i + 1) % size) for i in range(size)]
        last = lax.slice_in_dim(shard, length - width, length, axis=dim)
        first = lax.slice_in_dim(shard, 0, width, axis=dim)
        edges[dim] = (
            lax.ppermute(last, axis, up),
            lax.ppermute(first, axis, [(b, a) for a, b in up]),
        )
    done = []
    for _, dim in sides:
        low, high = edges[dim]
        around = [(width, width) if d in done else (0, 0) for d in range(shard.ndim)]
        shard = jnp.concatenate([jnp.pad(low, around), shard, jnp.pad(high, around)], axis=dim)
        done.append(dim)
    return shard


def in_one_piece(arrays, axis, split_dim, concat_dim, along):
    widths = [math.prod(a.shape[along:]) for a in arrays]
    both = jnp.concatenate(
        [a.reshape(*a.shape[:along], w) for a, w in zip(arrays, widths)], axis=along
    )
    whole = lax.all_to_all(both, axis, split_axis=split_dim, concat_axis=concat_dim, tiled=True)
    tiles = jnp.split(whole, [sum(widths[:k]) for k in range(1, len(widths))], axis=along)
    return tuple((b.reshape(*whole.shape[:along], *a.shape[along:]) for a, b in zip(arrays, tiles)))


def joined_along(tiles, dim):
    lengths = list(tiles.shape[1:])
    lengths[dim] *= tiles.shape[0]
    return jnp.moveaxis(tiles, 0, dim).reshape(lengths)


def gather_in_order(shard, axes, order):
    tiles = shard
    for k in order:
        tiles = lax.all_gather(tiles, axes[k])
    done = order[::-1]
    back = [done.index(k) for k in range(len(axes))]
    tiles = tiles.transpose(*back, *range(len(axes), tiles.ndim))
    return tiles.reshape(-1, *shard.shape)


def gathered_by_axis(shard, axes, order, dim):
    return joined_along(gather_in_order(shard, axes, order), dim)


def from_everyone(shard, axis):
    copies = jnp.broadcast_to(shard, (lax.axis_size(axis), *shard.shape))
    return lax.all_to_all(copies, axis, split_axis=0, concat_axis=0, tiled=True)


def owner_sums(rows, small, tiles, axis):
    count = lax.axis_size(axis)
    spare = -small.size % count
    small = jnp.pad(small, (0, spare))
    summed = [rows.reshape(count, -1), small.reshape(count, -1)]
    width = sum(part.shape[1] for part in summed)
    both = jnp.concatenate(summed + [tiles.reshape(count, -1).astype(jnp.float32)], axis=1)
    arrived = lax.all_to_all(both, axis, split_axis=0, concat_axis=0, tiled=True)
    total = arrived[:, :width].sum(axis=0)
    part = rows.size // count
    moved = arrived[:, width:].astype(tiles.dtype).reshape(-1, *tiles.shape[2:])
    return total[:part].reshape(-1, rows.shape[-1]), total[part:], moved


def shared_back(rows, chunk, axis):
    everything = from_everyone(jnp.concatenate([rows.ravel(), chunk]), axis)
    whole_rows = everything[:, : rows.size].reshape(-1, rows.shape[-1])
    return whole_rows, everything[:, rows.size :].reshape(-1)


def cheb_tables(points):
    order = points - 1
    node_index = np.arange(points)
    nodes = -np.cos(np.pi * node_index / order)
    end_weight = np.where((node_index == 0) | (node_index == order), 2.0, 1.0)
    parity = (-1.0) ** (node_index[:, None] + node_index[None, :])
    offdiag = 1.0 - np.eye(points)
    spread = nodes[:, None] - nodes[None, :] + np.eye(points)
    deriv = end_weight[:, None] / end_weight[None, :] * parity / spread * offdiag
    deriv = deriv - np.eye(points) * deriv.sum(axis=1)[:, None]
    highpass = parity / (order * end_weight[None, :])
    return (deriv, highpass, 0.5 * order * order)


def axis_matrices(count, periodic):
    deriv, highpass, lift_half = cheb_tables(P_SIZE)
    length = count * P_SIZE
    slope = np.kron(np.eye(count), deriv)
    upper = np.kron(np.eye(count), highpass)
    faces = count if periodic else count - 1
    for element in range(faces):
        last_node = element * P_SIZE + P_SIZE - 1
        next_node = (element + 1) % count * P_SIZE
        slope[last_node, next_node] += lift_half
        slope[last_node, last_node] -= lift_half
        slope[next_node, last_node] -= lift_half
        slope[next_node, next_node] += lift_half
    if not periodic:
        slope[0, 0] += lift_half
        slope[length - 1, length - 1] -= lift_half
    paired = jnp.asarray(np.concatenate([slope, upper], axis=0), jnp.float32)
    return (paired, lift_half)


def slot_matrix(members, member_count):
    member_hot = (members[..., None] == jnp.arange(member_count, dtype=jnp.int32)).astype(jnp.int32)
    before = jnp.cumsum(member_hot, axis=-2) - member_hot
    ranks = jnp.sum(before * member_hot, axis=-1)
    slots = members * CAP + ranks
    return (slots[..., None, :] == jnp.arange(member_count * CAP, dtype=jnp.int32)[:, None]).astype(
        jnp.float32
    )


DIMS = ("NDHWC", "DHWIO", "NDHWC")
FILTER_DIMS = ("CDHWN", "IDHWO", "NDHWC")
SAME = ((1, 1), (1, 1), (1, 1))


def silu_slope(value):
    gate = jax.nn.sigmoid(value)
    return gate * (1.0 + value * (1.0 - gate))


def conv_taps(grid, kernel):
    return lax.conv_general_dilated(
        grid, kernel, (1, 1, 1), SAME, dimension_numbers=DIMS,
        preferred_element_type=jnp.float32,
    )


def conv_filter(grid, delta):
    taps = lax.conv_general_dilated(
        grid, delta, (1, 1, 1), SAME, dimension_numbers=FILTER_DIMS,
        preferred_element_type=jnp.float32,
    )
    return jnp.moveaxis(taps, 0, 3)


def forward_back(patches, aim_rows, valid, k_first, k_second, w_hidden, w_out):
    batch = patches.shape[0]
    channels = k_second.shape[-1]
    inputs = patches.reshape(batch, 2, PY, PX, PZ).transpose(0, 2, 3, 4, 1)
    first_taps = k_first.reshape(3, 3, 3, 2, channels)
    second_taps = k_second.reshape(3, 3, 3, channels, channels)
    scale_one = 1.0 / math.sqrt(54.0)
    scale_two = 1.0 / math.sqrt(27.0 * channels)
    scale_three = 1.0 / math.sqrt(1.0 * w_hidden.shape[0])
    scale_four = 1.0 / math.sqrt(1.0 * w_hidden.shape[1])
    pre_one = conv_taps(inputs, first_taps) * scale_one
    hidden_one = jax.nn.silu(pre_one).astype(jnp.bfloat16)
    pre_two = conv_taps(hidden_one, second_taps) * scale_two
    pooled = jax.nn.silu(pre_two).reshape(batch, PY // 2, 2, PX // 2, 2, PZ, channels).mean(axis=(2, 4))
    features = pooled.reshape(batch, -1).astype(jnp.bfloat16)
    pre_three = jnp.dot(features, w_hidden, preferred_element_type=jnp.float32) * scale_three
    hidden_three = jax.nn.silu(pre_three).astype(jnp.bfloat16)
    pred = jnp.dot(hidden_three, w_out, preferred_element_type=jnp.float32) * scale_four
    error = valid.astype(jnp.float32)[:, None] * (pred - aim_rows.astype(jnp.float32))
    grad_out = jnp.dot(hidden_three.astype(jnp.float32).T, error, precision=highest) * scale_four
    delta_three = (
        jnp.dot(error, w_out.astype(jnp.float32).T, precision=highest) * scale_four * silu_slope(pre_three)
    ).astype(jnp.bfloat16)
    back_feat = jnp.dot(delta_three, w_hidden.T, preferred_element_type=jnp.float32) * scale_three
    back_grid = back_feat.reshape(batch, PY // 2, 1, PX // 2, 1, PZ, channels)
    spread_back = jnp.broadcast_to(back_grid, (batch, PY // 2, 2, PX // 2, 2, PZ, channels)).reshape(pre_two.shape) * 0.25
    delta_two = (spread_back * silu_slope(pre_two)).astype(jnp.bfloat16)
    grad_two = (conv_filter(hidden_one, delta_two) * scale_two).reshape(27, channels, channels)
    mirrored = jnp.flip(second_taps, axis=(0, 1, 2)).swapaxes(3, 4)
    back_one = conv_taps(delta_two, mirrored)
    delta_one = (back_one * scale_two * silu_slope(pre_one)).astype(jnp.bfloat16)
    grad_one = (conv_filter(inputs, delta_one) * scale_one).reshape(54, channels)
    return (pred, grad_one, grad_two, grad_out, features, delta_three)


def row_update(weight, grad):
    scale = jnp.sqrt(jnp.mean(grad * grad, axis=-1, keepdims=True) + rms_eps)
    return weight.astype(jnp.float32) - learn_rate * grad / scale


def whole_update(weight, grad):
    scale = jnp.sqrt(jnp.mean(grad * grad) + rms_eps)
    return weight.astype(jnp.float32) - learn_rate * grad / scale


def body(velocity, sample_block, sample_member, k_first, k_second, w_hidden, w_out):
    wall_count = lax.axis_size("wall")
    wall_place = lax.axis_index("wall")
    flow_count = lax.axis_size(STREAM)
    flow_place = lax.axis_index(STREAM)
    padded = extended(velocity, (("wall", 1), (STREAM, 2)), 1)
    keep_low = (wall_place > 0).astype(jnp.float32)
    keep_high = (wall_place < wall_count - 1).astype(jnp.float32)
    below = padded[:, 0, 1:-1, :] * keep_low
    above = padded[:, -1, 1:-1, :] * keep_high
    left_face = padded[:, 1:-1, 0, :]
    right_face = padded[:, 1:-1, -1, :]
    size_y, size_x, size_z = (velocity.shape[1], velocity.shape[2], velocity.shape[3])
    pair_y, lift_half = axis_matrices(size_y // P_SIZE, False)
    pair_x, lift_same = axis_matrices(size_x // P_SIZE, False)
    pair_z, lift_again = axis_matrices(size_z // P_SIZE, True)
    along_y = jnp.einsum("cyxz,wy->cwxz", velocity, pair_y, precision=highest)
    grad_y = (
        along_y[:, :size_y]
        .at[:, 0]
        .add(-lift_half * below)
        .at[:, size_y - 1]
        .add(lift_half * above)
    )
    high_y = along_y[:, size_y:]
    rows_y, rows_x, rows_z = (size_y // PY, size_x // PX, size_z // PZ)
    tangent = jnp.stack([velocity[0], velocity[2]]).reshape(2, rows_y, PY, rows_x, PX, rows_z, PZ)
    blocks = tangent.transpose(1, 3, 5, 0, 2, 4, 6).reshape(-1, 2 * PY * PX * PZ)
    slope_wall = jnp.stack([grad_y[0], grad_y[2]]).reshape(2, rows_y, PY, rows_x, PX, rows_z, PZ)
    stress_true = (
        (viscosity * jnp.mean(slope_wall, axis=(2, 4, 6))).transpose(1, 2, 3, 0).reshape(-1, 2)
    )
    picked = sample_block.reshape(-1)
    members = sample_member.reshape(-1)
    patch_rows = jnp.take(blocks, picked, axis=0).astype(jnp.bfloat16)
    aim_rows = jnp.take(stress_true, picked, axis=0).astype(jnp.bfloat16)
    select = slot_matrix(members, wall_count)
    select_half = select.astype(jnp.bfloat16)
    send_rows = jnp.dot(select_half, patch_rows, preferred_element_type=jnp.float32).astype(
        jnp.bfloat16
    )
    send_aims = jnp.dot(select_half, aim_rows, preferred_element_type=jnp.float32).astype(
        jnp.bfloat16
    )
    send_valid = jnp.sum(select, axis=1).astype(jnp.bfloat16)
    left_face, right_face, send_rows, send_aims, send_valid = lax.optimization_barrier(
        (left_face, right_face, send_rows, send_aims, send_valid)
    )
    along_x = jnp.einsum("cyxz,wx->cywz", velocity, pair_x, precision=highest)
    grad_x = (
        along_x[:, :, :size_x]
        .at[:, :, 0]
        .add(-lift_half * left_face)
        .at[:, :, size_x - 1]
        .add(lift_half * right_face)
    )
    high_x = along_x[:, :, size_x:]
    along_z = jnp.einsum("cyxz,wz->cyxw", velocity, pair_z, precision=highest)
    grad_z = along_z[..., :size_z]
    high_z = along_z[..., size_z:]
    advect = velocity[0][None] * grad_x + velocity[1][None] * grad_y + velocity[2][None] * grad_z
    new_field = velocity + time_step * (-advect - relax_rate * (high_x + high_y + high_z))
    recv_rows, recv_aims, recv_valid = in_one_piece(
        (send_rows, send_aims, send_valid), "wall", 0, 0, 1
    )
    pred, grad_one, grad_two, grad_out, features, delta_three = forward_back(
        recv_rows, recv_aims, recv_valid, k_first[0], k_second[0], w_hidden[0], w_out[0]
    )
    back = lax.all_to_all(pred, "wall", split_axis=0, concat_axis=0, tiled=True)
    stress_local = jnp.dot(select.T, back, precision=highest)
    stress = stress_local.T[:, None, :]
    share_rows = FEATS // flow_count
    dense_scale = 1.0 / math.sqrt(1.0 * FEATS)
    small = jnp.concatenate([grad_one.ravel(), grad_out.ravel()])
    tiles = features.reshape(features.shape[0], flow_count, -1).transpose(1, 0, 2)
    grad_share, small_part, columns_here = owner_sums(grad_two.reshape(-1, CH), small, tiles, STREAM)
    grad_hidden = (
        jnp.dot(
            columns_here.T,
            gathered_by_axis(delta_three, STREAM, (0, 1, 2), 0),
            preferred_element_type=jnp.float32,
        )
        * dense_scale
    )
    own_rows = lax.dynamic_slice_in_dim(w_hidden[0], flow_place * share_rows, share_rows, 0)
    new_w_hidden = row_update(own_rows, grad_hidden)[None]
    share_count = grad_share.shape[0]
    kernel_own = lax.dynamic_slice_in_dim(
        k_second[0].reshape(-1, CH), flow_place * share_count, share_count, 0
    )
    updated_rows = row_update(kernel_own, grad_share)
    kernel_rows, small = shared_back(updated_rows, small_part, STREAM)
    new_k_second = kernel_rows.reshape(k_second.shape[1:])
    grad_one = small[: grad_one.size].reshape(grad_one.shape)
    grad_out = small[grad_one.size : grad_one.size + grad_out.size].reshape(grad_out.shape)
    new_k_first = row_update(k_first[0], grad_one)
    new_w_out = whole_update(w_out[0], grad_out)
    return (new_field, stress, new_k_first[None], new_k_second[None], new_w_hidden, new_w_out[None])


def solution(mesh):
    torus = Mesh(
        mesh.devices.reshape(mesh.shape["wall"], 8, 2, 2),
        ("wall", "stream_0", "stream_1", "stream_2"),
    )
    in_specs = (
        P(None, "wall", STREAM, None),
        P("wall", STREAM),
        P("wall", STREAM, None),
        P("wall", None, None),
        P("wall", None, None, None),
        P("wall", None, None),
        P("wall", None, None),
    )
    out_specs = (
        P(None, "wall", STREAM, None),
        P(None, "wall", STREAM),
        P("wall", None, None),
        P("wall", None, None, None),
        P("wall", STREAM, None),
        P("wall", None, None),
    )
    return jax.shard_map(body, mesh=torus, in_specs=in_specs, out_specs=out_specs, check_vma=False)
```

```python
import math

import jax
import jax.numpy as jnp
import numpy as np
from jax import lax
from jax.sharding import Mesh
from jax.sharding import PartitionSpec as P

P_SIZE = 8
PY = 4
PX = 4
PZ = 8
CH = 64
CAP = 2
FEATS = 2048
STREAM = ("stream_0", "stream_1", "stream_2")


highest = lax.Precision.HIGHEST
time_step = 0.005
relax_rate = 20.0
viscosity = 0.3
learn_rate = 0.5
rms_eps = 1e-06
def extended(shard, sides, width):
    edges = {}
    for axis, dim in sides:
        size, length = (lax.axis_size(axis), shard.shape[dim])
        up = [(i, (i + 1) % size) for i in range(size)]
        last = lax.slice_in_dim(shard, length - width, length, axis=dim)
        first = lax.slice_in_dim(shard, 0, width, axis=dim)
        edges[dim] = (
            lax.ppermute(last, axis, up),
            lax.ppermute(first, axis, [(b, a) for a, b in up]),
        )
    done = []
    for _, dim in sides:
        low, high = edges[dim]
        around = [(width, width) if d in done else (0, 0) for d in range(shard.ndim)]
        shard = jnp.concatenate([jnp.pad(low, around), shard, jnp.pad(high, around)], axis=dim)
        done.append(dim)
    return shard


def in_one_piece(arrays, axis, split_dim, concat_dim, along):
    widths = [math.prod(a.shape[along:]) for a in arrays]
    both = jnp.concatenate(
        [a.reshape(*a.shape[:along], w) for a, w in zip(arrays, widths)], axis=along
    )
    whole = lax.all_to_all(both, axis, split_axis=split_dim, concat_axis=concat_dim, tiled=True)
    tiles = jnp.split(whole, [sum(widths[:k]) for k in range(1, len(widths))], axis=along)
    return tuple((b.reshape(*whole.shape[:along], *a.shape[along:]) for a, b in zip(arrays, tiles)))


def joined_along(tiles, dim):
    lengths = list(tiles.shape[1:])
    lengths[dim] *= tiles.shape[0]
    return jnp.moveaxis(tiles, 0, dim).reshape(lengths)


def gather_in_order(shard, axes, order):
    tiles = shard
    for k in order:
        tiles = lax.all_gather(tiles, axes[k])
    done = order[::-1]
    back = [done.index(k) for k in range(len(axes))]
    tiles = tiles.transpose(*back, *range(len(axes), tiles.ndim))
    return tiles.reshape(-1, *shard.shape)


def gathered_by_axis(shard, axes, order, dim):
    return joined_along(gather_in_order(shard, axes, order), dim)


def from_everyone(shard, axis):
    copies = jnp.broadcast_to(shard, (lax.axis_size(axis), *shard.shape))
    return lax.all_to_all(copies, axis, split_axis=0, concat_axis=0, tiled=True)


def owner_sums(rows, small, tiles, axis):
    count = lax.axis_size(axis)
    spare = -small.size % count
    small = jnp.pad(small, (0, spare))
    summed = [rows.reshape(count, -1), small.reshape(count, -1)]
    width = sum(part.shape[1] for part in summed)
    summed = [part.astype(tiles.dtype) for part in summed]
    both = jnp.concatenate(summed + [tiles.reshape(count, -1)], axis=1)
    arrived = lax.all_to_all(both, axis, split_axis=0, concat_axis=0, tiled=True)
    total = arrived[:, :width].astype(jnp.float32).sum(axis=0)
    part = rows.size // count
    moved = arrived[:, width:].astype(tiles.dtype).reshape(-1, *tiles.shape[2:])
    return total[:part].reshape(-1, rows.shape[-1]), total[part:], moved


def shared_back(rows, chunk, axis):
    everything = from_everyone(jnp.concatenate([rows.ravel(), chunk]), axis)
    whole_rows = everything[:, : rows.size].reshape(-1, rows.shape[-1])
    return whole_rows, everything[:, rows.size :].reshape(-1)


def cheb_tables(points):
    order = points - 1
    node_index = np.arange(points)
    nodes = -np.cos(np.pi * node_index / order)
    end_weight = np.where((node_index == 0) | (node_index == order), 2.0, 1.0)
    parity = (-1.0) ** (node_index[:, None] + node_index[None, :])
    offdiag = 1.0 - np.eye(points)
    spread = nodes[:, None] - nodes[None, :] + np.eye(points)
    deriv = end_weight[:, None] / end_weight[None, :] * parity / spread * offdiag
    deriv = deriv - np.eye(points) * deriv.sum(axis=1)[:, None]
    highpass = parity / (order * end_weight[None, :])
    return (deriv, highpass, 0.5 * order * order)


def axis_matrices(count, periodic):
    deriv, highpass, lift_half = cheb_tables(P_SIZE)
    length = count * P_SIZE
    slope = np.kron(np.eye(count), deriv)
    upper = np.kron(np.eye(count), highpass)
    faces = count if periodic else count - 1
    for element in range(faces):
        last_node = element * P_SIZE + P_SIZE - 1
        next_node = (element + 1) % count * P_SIZE
        slope[last_node, next_node] += lift_half
        slope[last_node, last_node] -= lift_half
        slope[next_node, last_node] -= lift_half
        slope[next_node, next_node] += lift_half
    if not periodic:
        slope[0, 0] += lift_half
        slope[length - 1, length - 1] -= lift_half
    paired = jnp.asarray(np.concatenate([slope, upper], axis=0), jnp.float32)
    return (paired, lift_half)


def slot_matrix(members, member_count):
    member_hot = (members[..., None] == jnp.arange(member_count, dtype=jnp.int32)).astype(jnp.int32)
    before = jnp.cumsum(member_hot, axis=-2) - member_hot
    ranks = jnp.sum(before * member_hot, axis=-1)
    slots = members * CAP + ranks
    return (slots[..., None, :] == jnp.arange(member_count * CAP, dtype=jnp.int32)[:, None]).astype(
        jnp.float32
    )


DIMS = ("NDHWC", "DHWIO", "NDHWC")
FILTER_DIMS = ("CDHWN", "IDHWO", "NDHWC")
SAME = ((1, 1), (1, 1), (1, 1))


def silu_slope(value):
    gate = jax.nn.sigmoid(value)
    return gate * (1.0 + value * (1.0 - gate))


def conv_taps(grid, kernel):
    return lax.conv_general_dilated(
        grid, kernel, (1, 1, 1), SAME, dimension_numbers=DIMS,
        preferred_element_type=jnp.float32,
    )


def conv_filter(grid, delta):
    taps = lax.conv_general_dilated(
        grid, delta, (1, 1, 1), SAME, dimension_numbers=FILTER_DIMS,
        preferred_element_type=jnp.float32,
    )
    return jnp.moveaxis(taps, 0, 3)


def forward_back(patches, aim_rows, valid, k_first, k_second, w_hidden, w_out):
    batch = patches.shape[0]
    channels = k_second.shape[-1]
    inputs = patches.reshape(batch, 2, PY, PX, PZ).transpose(0, 2, 3, 4, 1)
    first_taps = k_first.reshape(3, 3, 3, 2, channels)
    second_taps = k_second.reshape(3, 3, 3, channels, channels)
    scale_one = 1.0 / math.sqrt(54.0)
    scale_two = 1.0 / math.sqrt(27.0 * channels)
    scale_three = 1.0 / math.sqrt(1.0 * w_hidden.shape[0])
    scale_four = 1.0 / math.sqrt(1.0 * w_hidden.shape[1])
    pre_one = conv_taps(inputs, first_taps) * scale_one
    hidden_one = jax.nn.silu(pre_one).astype(jnp.bfloat16)
    pre_two = conv_taps(hidden_one, second_taps) * scale_two
    pooled = jax.nn.silu(pre_two).reshape(batch, PY // 2, 2, PX // 2, 2, PZ, channels).mean(axis=(2, 4))
    features = pooled.reshape(batch, -1).astype(jnp.bfloat16)
    pre_three = jnp.dot(features, w_hidden, preferred_element_type=jnp.float32) * scale_three
    hidden_three = jax.nn.silu(pre_three).astype(jnp.bfloat16)
    pred = jnp.dot(hidden_three, w_out, preferred_element_type=jnp.float32) * scale_four
    error = valid.astype(jnp.float32)[:, None] * (pred - aim_rows.astype(jnp.float32))
    grad_out = jnp.dot(hidden_three.astype(jnp.float32).T, error, precision=highest) * scale_four
    delta_three = (
        jnp.dot(error, w_out.astype(jnp.float32).T, precision=highest) * scale_four * silu_slope(pre_three)
    ).astype(jnp.bfloat16)
    back_feat = jnp.dot(delta_three, w_hidden.T, preferred_element_type=jnp.float32) * scale_three
    back_grid = back_feat.reshape(batch, PY // 2, 1, PX // 2, 1, PZ, channels)
    spread_back = jnp.broadcast_to(back_grid, (batch, PY // 2, 2, PX // 2, 2, PZ, channels)).reshape(pre_two.shape) * 0.25
    delta_two = (spread_back * silu_slope(pre_two)).astype(jnp.bfloat16)
    grad_two = (conv_filter(hidden_one, delta_two) * scale_two).reshape(27, channels, channels)
    mirrored = jnp.flip(second_taps, axis=(0, 1, 2)).swapaxes(3, 4)
    back_one = conv_taps(delta_two, mirrored)
    delta_one = (back_one * scale_two * silu_slope(pre_one)).astype(jnp.bfloat16)
    grad_one = (conv_filter(inputs, delta_one) * scale_one).reshape(54, channels)
    return (pred, grad_one, grad_two, grad_out, features, delta_three)


def row_update(weight, grad):
    scale = jnp.sqrt(jnp.mean(grad * grad, axis=-1, keepdims=True) + rms_eps)
    return weight.astype(jnp.float32) - learn_rate * grad / scale


def whole_update(weight, grad):
    scale = jnp.sqrt(jnp.mean(grad * grad) + rms_eps)
    return weight.astype(jnp.float32) - learn_rate * grad / scale


def body(velocity, sample_block, sample_member, k_first, k_second, w_hidden, w_out):
    wall_count = lax.axis_size("wall")
    wall_place = lax.axis_index("wall")
    flow_count = lax.axis_size(STREAM)
    flow_place = lax.axis_index(STREAM)
    padded = extended(velocity, (("wall", 1), (STREAM, 2)), 1)
    keep_low = (wall_place > 0).astype(jnp.float32)
    keep_high = (wall_place < wall_count - 1).astype(jnp.float32)
    below = padded[:, 0, 1:-1, :] * keep_low
    above = padded[:, -1, 1:-1, :] * keep_high
    left_face = padded[:, 1:-1, 0, :]
    right_face = padded[:, 1:-1, -1, :]
    size_y, size_x, size_z = (velocity.shape[1], velocity.shape[2], velocity.shape[3])
    pair_y, lift_half = axis_matrices(size_y // P_SIZE, False)
    pair_x, lift_same = axis_matrices(size_x // P_SIZE, False)
    pair_z, lift_again = axis_matrices(size_z // P_SIZE, True)
    along_y = jnp.einsum("cyxz,wy->cwxz", velocity, pair_y, precision=highest)
    grad_y = (
        along_y[:, :size_y]
        .at[:, 0]
        .add(-lift_half * below)
        .at[:, size_y - 1]
        .add(lift_half * above)
    )
    high_y = along_y[:, size_y:]
    rows_y, rows_x, rows_z = (size_y // PY, size_x // PX, size_z // PZ)
    tangent = jnp.stack([velocity[0], velocity[2]]).reshape(2, rows_y, PY, rows_x, PX, rows_z, PZ)
    blocks = tangent.transpose(1, 3, 5, 0, 2, 4, 6).reshape(-1, 2 * PY * PX * PZ)
    slope_wall = jnp.stack([grad_y[0], grad_y[2]]).reshape(2, rows_y, PY, rows_x, PX, rows_z, PZ)
    stress_true = (
        (viscosity * jnp.mean(slope_wall, axis=(2, 4, 6))).transpose(1, 2, 3, 0).reshape(-1, 2)
    )
    picked = sample_block.reshape(-1)
    members = sample_member.reshape(-1)
    patch_rows = jnp.take(blocks, picked, axis=0).astype(jnp.bfloat16)
    aim_rows = jnp.take(stress_true, picked, axis=0).astype(jnp.bfloat16)
    select = slot_matrix(members, wall_count)
    select_half = select.astype(jnp.bfloat16)
    send_rows = jnp.dot(select_half, patch_rows, preferred_element_type=jnp.float32).astype(
        jnp.bfloat16
    )
    send_aims = jnp.dot(select_half, aim_rows, preferred_element_type=jnp.float32).astype(
        jnp.bfloat16
    )
    send_valid = jnp.sum(select, axis=1).astype(jnp.bfloat16)
    left_face, right_face, send_rows, send_aims, send_valid = lax.optimization_barrier(
        (left_face, right_face, send_rows, send_aims, send_valid)
    )
    along_x = jnp.einsum("cyxz,wx->cywz", velocity, pair_x, precision=highest)
    grad_x = (
        along_x[:, :, :size_x]
        .at[:, :, 0]
        .add(-lift_half * left_face)
        .at[:, :, size_x - 1]
        .add(lift_half * right_face)
    )
    high_x = along_x[:, :, size_x:]
    along_z = jnp.einsum("cyxz,wz->cyxw", velocity, pair_z, precision=highest)
    grad_z = along_z[..., :size_z]
    high_z = along_z[..., size_z:]
    advect = velocity[0][None] * grad_x + velocity[1][None] * grad_y + velocity[2][None] * grad_z
    new_field = velocity + time_step * (-advect - relax_rate * (high_x + high_y + high_z))
    recv_rows, recv_aims, recv_valid = in_one_piece(
        (send_rows, send_aims, send_valid), "wall", 0, 0, 1
    )
    pred, grad_one, grad_two, grad_out, features, delta_three = forward_back(
        recv_rows, recv_aims, recv_valid, k_first[0], k_second[0], w_hidden[0], w_out[0]
    )
    back = lax.all_to_all(pred, "wall", split_axis=0, concat_axis=0, tiled=True)
    stress_local = jnp.dot(select.T, back, precision=highest)
    stress = stress_local.T[:, None, :]
    share_rows = FEATS // flow_count
    dense_scale = 1.0 / math.sqrt(1.0 * FEATS)
    small = jnp.concatenate([grad_one.ravel(), grad_out.ravel()])
    tiles = features.reshape(features.shape[0], flow_count, -1).transpose(1, 0, 2)
    grad_share, small_part, columns_here = owner_sums(grad_two.reshape(-1, CH), small, tiles, STREAM)
    grad_hidden = (
        jnp.dot(
            columns_here.T,
            gathered_by_axis(delta_three, STREAM, (1, 0, 2), 0),
            preferred_element_type=jnp.float32,
        )
        * dense_scale
    )
    own_rows = lax.dynamic_slice_in_dim(w_hidden[0], flow_place * share_rows, share_rows, 0)
    new_w_hidden = row_update(own_rows, grad_hidden)[None]
    share_count = grad_share.shape[0]
    kernel_own = lax.dynamic_slice_in_dim(
        k_second[0].reshape(-1, CH), flow_place * share_count, share_count, 0
    )
    updated_rows = row_update(kernel_own, grad_share)
    kernel_rows, small = shared_back(updated_rows, small_part, STREAM)
    new_k_second = kernel_rows.reshape(k_second.shape[1:])
    grad_one = small[: grad_one.size].reshape(grad_one.shape)
    grad_out = small[grad_one.size : grad_one.size + grad_out.size].reshape(grad_out.shape)
    new_k_first = row_update(k_first[0], grad_one)
    new_w_out = whole_update(w_out[0], grad_out)
    return (new_field, stress, new_k_first[None], new_k_second[None], new_w_hidden, new_w_out[None])


def solution(mesh):
    torus = Mesh(
        mesh.devices.reshape(mesh.shape["wall"], 8, 2, 2),
        ("wall", "stream_0", "stream_1", "stream_2"),
    )
    in_specs = (
        P(None, "wall", STREAM, None),
        P("wall", STREAM),
        P("wall", STREAM, None),
        P("wall", None, None),
        P("wall", None, None, None),
        P("wall", None, None),
        P("wall", None, None),
    )
    out_specs = (
        P(None, "wall", STREAM, None),
        P(None, "wall", STREAM),
        P("wall", None, None),
        P("wall", None, None, None),
        P("wall", STREAM, None),
        P("wall", None, None),
    )
    return jax.shard_map(body, mesh=torus, in_specs=in_specs, out_specs=out_specs, check_vma=False)
```

```python
import math

import jax
import jax.numpy as jnp
import numpy as np
from jax import lax
from jax.sharding import Mesh
from jax.sharding import PartitionSpec as P

P_SIZE = 8
PY = 4
PX = 4
PZ = 8
CH = 64
CAP = 2
FEATS = 2048
STREAM = ("stream_0", "stream_1", "stream_2")


highest = lax.Precision.HIGHEST
time_step = 0.005
relax_rate = 20.0
viscosity = 0.3
learn_rate = 0.5
rms_eps = 1e-06
def extended(shard, sides, width):
    edges = {}
    for axis, dim in sides:
        size, length = (lax.axis_size(axis), shard.shape[dim])
        up = [(i, (i + 1) % size) for i in range(size)]
        last = lax.slice_in_dim(shard, length - width, length, axis=dim)
        first = lax.slice_in_dim(shard, 0, width, axis=dim)
        edges[dim] = (
            lax.ppermute(last, axis, up),
            lax.ppermute(first, axis, [(b, a) for a, b in up]),
        )
    done = []
    for _, dim in sides:
        low, high = edges[dim]
        around = [(width, width) if d in done else (0, 0) for d in range(shard.ndim)]
        shard = jnp.concatenate([jnp.pad(low, around), shard, jnp.pad(high, around)], axis=dim)
        done.append(dim)
    return shard


def in_one_piece(arrays, axis, split_dim, concat_dim, along):
    widths = [math.prod(a.shape[along:]) for a in arrays]
    both = jnp.concatenate(
        [a.reshape(*a.shape[:along], w) for a, w in zip(arrays, widths)], axis=along
    )
    whole = lax.all_to_all(both, axis, split_axis=split_dim, concat_axis=concat_dim, tiled=True)
    tiles = jnp.split(whole, [sum(widths[:k]) for k in range(1, len(widths))], axis=along)
    return tuple((b.reshape(*whole.shape[:along], *a.shape[along:]) for a, b in zip(arrays, tiles)))


def joined_along(tiles, dim):
    lengths = list(tiles.shape[1:])
    lengths[dim] *= tiles.shape[0]
    return jnp.moveaxis(tiles, 0, dim).reshape(lengths)


def gather_in_order(shard, axes, order):
    tiles = shard
    for k in order:
        tiles = lax.all_gather(tiles, axes[k])
    done = order[::-1]
    back = [done.index(k) for k in range(len(axes))]
    tiles = tiles.transpose(*back, *range(len(axes), tiles.ndim))
    return tiles.reshape(-1, *shard.shape)


def gathered_by_axis(shard, axes, order, dim):
    return joined_along(gather_in_order(shard, axes, order), dim)


def from_everyone(shard, axis):
    copies = jnp.broadcast_to(shard, (lax.axis_size(axis), *shard.shape))
    return lax.all_to_all(copies, axis, split_axis=0, concat_axis=0, tiled=True)


def owner_sums(rows, small, tiles, axis):
    count = lax.axis_size(axis)
    spare = -small.size % count
    small = jnp.pad(small, (0, spare))
    summed = [rows.reshape(count, -1), small.reshape(count, -1)]
    width = sum(part.shape[1] for part in summed)
    summed = [part.astype(tiles.dtype) for part in summed]
    both = jnp.concatenate(summed + [tiles.reshape(count, -1)], axis=1)
    arrived = lax.all_to_all(both, axis, split_axis=0, concat_axis=0, tiled=True)
    total = arrived[:, :width].astype(jnp.float32).sum(axis=0)
    part = rows.size // count
    moved = arrived[:, width:].astype(tiles.dtype).reshape(-1, *tiles.shape[2:])
    return total[:part].reshape(-1, rows.shape[-1]), total[part:], moved


def shared_back(rows, chunk, axis):
    everything = from_everyone(jnp.concatenate([rows.ravel(), chunk]), axis)
    whole_rows = everything[:, : rows.size].reshape(-1, rows.shape[-1])
    return whole_rows, everything[:, rows.size :].reshape(-1)


def cheb_tables(points):
    order = points - 1
    node_index = np.arange(points)
    nodes = -np.cos(np.pi * node_index / order)
    end_weight = np.where((node_index == 0) | (node_index == order), 2.0, 1.0)
    parity = (-1.0) ** (node_index[:, None] + node_index[None, :])
    offdiag = 1.0 - np.eye(points)
    spread = nodes[:, None] - nodes[None, :] + np.eye(points)
    deriv = end_weight[:, None] / end_weight[None, :] * parity / spread * offdiag
    deriv = deriv - np.eye(points) * deriv.sum(axis=1)[:, None]
    highpass = parity / (order * end_weight[None, :])
    return (deriv, highpass, 0.5 * order * order)


def axis_matrices(count, periodic):
    deriv, highpass, lift_half = cheb_tables(P_SIZE)
    length = count * P_SIZE
    slope = np.kron(np.eye(count), deriv)
    upper = np.kron(np.eye(count), highpass)
    faces = count if periodic else count - 1
    for element in range(faces):
        last_node = element * P_SIZE + P_SIZE - 1
        next_node = (element + 1) % count * P_SIZE
        slope[last_node, next_node] += lift_half
        slope[last_node, last_node] -= lift_half
        slope[next_node, last_node] -= lift_half
        slope[next_node, next_node] += lift_half
    if not periodic:
        slope[0, 0] += lift_half
        slope[length - 1, length - 1] -= lift_half
    paired = jnp.asarray(np.concatenate([slope, upper], axis=0), jnp.float32)
    return (paired, lift_half)


def slot_matrix(members, member_count):
    member_hot = (members[..., None] == jnp.arange(member_count, dtype=jnp.int32)).astype(jnp.int32)
    before = jnp.cumsum(member_hot, axis=-2) - member_hot
    ranks = jnp.sum(before * member_hot, axis=-1)
    slots = members * CAP + ranks
    return (slots[..., None, :] == jnp.arange(member_count * CAP, dtype=jnp.int32)[:, None]).astype(
        jnp.float32
    )


DIMS = ("NDHWC", "DHWIO", "NDHWC")
FILTER_DIMS = ("CDHWN", "IDHWO", "NDHWC")
SAME = ((1, 1), (1, 1), (1, 1))


def silu_slope(value):
    gate = jax.nn.sigmoid(value)
    return gate * (1.0 + value * (1.0 - gate))


def conv_taps(grid, kernel):
    return lax.conv_general_dilated(
        grid, kernel, (1, 1, 1), SAME, dimension_numbers=DIMS,
        preferred_element_type=jnp.float32,
    )


def conv_filter(grid, delta):
    taps = lax.conv_general_dilated(
        grid, delta, (1, 1, 1), SAME, dimension_numbers=FILTER_DIMS,
        preferred_element_type=jnp.float32,
    )
    return jnp.moveaxis(taps, 0, 3)


def forward_back(patches, aim_rows, valid, k_first, k_second, w_hidden, w_out):
    batch = patches.shape[0]
    channels = k_second.shape[-1]
    inputs = patches.reshape(batch, 2, PY, PX, PZ).transpose(0, 2, 3, 4, 1)
    first_taps = k_first.reshape(3, 3, 3, 2, channels)
    second_taps = k_second.reshape(3, 3, 3, channels, channels)
    scale_one = 1.0 / math.sqrt(54.0)
    scale_two = 1.0 / math.sqrt(27.0 * channels)
    scale_three = 1.0 / math.sqrt(1.0 * w_hidden.shape[0])
    scale_four = 1.0 / math.sqrt(1.0 * w_hidden.shape[1])
    pre_one = conv_taps(inputs, first_taps) * scale_one
    hidden_one = jax.nn.silu(pre_one).astype(jnp.bfloat16)
    pre_two = conv_taps(hidden_one, second_taps) * scale_two
    pooled = jax.nn.silu(pre_two).reshape(batch, PY // 2, 2, PX // 2, 2, PZ, channels).mean(axis=(2, 4))
    features = pooled.reshape(batch, -1).astype(jnp.bfloat16)
    pre_three = jnp.dot(features, w_hidden, preferred_element_type=jnp.float32) * scale_three
    hidden_three = jax.nn.silu(pre_three).astype(jnp.bfloat16)
    pred = jnp.dot(hidden_three, w_out, preferred_element_type=jnp.float32) * scale_four
    error = valid.astype(jnp.float32)[:, None] * (pred - aim_rows.astype(jnp.float32))
    grad_out = jnp.dot(hidden_three.astype(jnp.float32).T, error, precision=highest) * scale_four
    delta_three = (
        jnp.dot(error, w_out.astype(jnp.float32).T, precision=highest) * scale_four * silu_slope(pre_three)
    ).astype(jnp.bfloat16)
    back_feat = jnp.dot(delta_three, w_hidden.T, preferred_element_type=jnp.float32) * scale_three
    back_grid = back_feat.reshape(batch, PY // 2, 1, PX // 2, 1, PZ, channels)
    spread_back = jnp.broadcast_to(back_grid, (batch, PY // 2, 2, PX // 2, 2, PZ, channels)).reshape(pre_two.shape) * 0.25
    delta_two = (spread_back * silu_slope(pre_two)).astype(jnp.bfloat16)
    grad_two = (conv_filter(hidden_one, delta_two) * scale_two).reshape(27, channels, channels)
    mirrored = jnp.flip(second_taps, axis=(0, 1, 2)).swapaxes(3, 4)
    back_one = conv_taps(delta_two, mirrored)
    delta_one = (back_one * scale_two * silu_slope(pre_one)).astype(jnp.bfloat16)
    grad_one = (conv_filter(inputs, delta_one) * scale_one).reshape(54, channels)
    return (pred, grad_one, grad_two, grad_out, features, delta_three)


def row_update(weight, grad):
    scale = jnp.sqrt(jnp.mean(grad * grad, axis=-1, keepdims=True) + rms_eps)
    return weight.astype(jnp.float32) - learn_rate * grad / scale


def whole_update(weight, grad):
    scale = jnp.sqrt(jnp.mean(grad * grad) + rms_eps)
    return weight.astype(jnp.float32) - learn_rate * grad / scale


def body(velocity, sample_block, sample_member, k_first, k_second, w_hidden, w_out):
    wall_count = lax.axis_size("wall")
    wall_place = lax.axis_index("wall")
    flow_count = lax.axis_size(STREAM)
    flow_place = lax.axis_index(STREAM)
    padded = extended(velocity, (("wall", 1), (STREAM, 2)), 1)
    keep_low = (wall_place > 0).astype(jnp.float32)
    keep_high = (wall_place < wall_count - 1).astype(jnp.float32)
    below = padded[:, 0, 1:-1, :] * keep_low
    above = padded[:, -1, 1:-1, :] * keep_high
    left_face = padded[:, 1:-1, 0, :]
    right_face = padded[:, 1:-1, -1, :]
    size_y, size_x, size_z = (velocity.shape[1], velocity.shape[2], velocity.shape[3])
    pair_y, lift_half = axis_matrices(size_y // P_SIZE, False)
    pair_x, lift_same = axis_matrices(size_x // P_SIZE, False)
    pair_z, lift_again = axis_matrices(size_z // P_SIZE, True)
    along_y = jnp.einsum("cyxz,wy->cwxz", velocity, pair_y, precision=highest)
    grad_y = (
        along_y[:, :size_y]
        .at[:, 0]
        .add(-lift_half * below)
        .at[:, size_y - 1]
        .add(lift_half * above)
    )
    high_y = along_y[:, size_y:]
    rows_y, rows_x, rows_z = (size_y // PY, size_x // PX, size_z // PZ)
    tangent = jnp.stack([velocity[0], velocity[2]]).reshape(2, rows_y, PY, rows_x, PX, rows_z, PZ)
    blocks = tangent.transpose(1, 3, 5, 0, 2, 4, 6).reshape(-1, 2 * PY * PX * PZ)
    slope_wall = jnp.stack([grad_y[0], grad_y[2]]).reshape(2, rows_y, PY, rows_x, PX, rows_z, PZ)
    stress_true = (
        (viscosity * jnp.mean(slope_wall, axis=(2, 4, 6))).transpose(1, 2, 3, 0).reshape(-1, 2)
    )
    picked = sample_block.reshape(-1)
    members = sample_member.reshape(-1)
    patch_rows = jnp.take(blocks, picked, axis=0).astype(jnp.bfloat16)
    aim_rows = jnp.take(stress_true, picked, axis=0).astype(jnp.bfloat16)
    select = slot_matrix(members, wall_count)
    select_half = select.astype(jnp.bfloat16)
    send_rows = jnp.dot(select_half, patch_rows, preferred_element_type=jnp.float32).astype(
        jnp.bfloat16
    )
    send_aims = jnp.dot(select_half, aim_rows, preferred_element_type=jnp.float32).astype(
        jnp.bfloat16
    )
    send_valid = jnp.sum(select, axis=1).astype(jnp.bfloat16)
    left_face, right_face, send_rows, send_aims, send_valid = lax.optimization_barrier(
        (left_face, right_face, send_rows, send_aims, send_valid)
    )
    along_x = jnp.einsum("cyxz,wx->cywz", velocity, pair_x, precision=highest)
    grad_x = (
        along_x[:, :, :size_x]
        .at[:, :, 0]
        .add(-lift_half * left_face)
        .at[:, :, size_x - 1]
        .add(lift_half * right_face)
    )
    high_x = along_x[:, :, size_x:]
    along_z = jnp.einsum("cyxz,wz->cyxw", velocity, pair_z, precision=highest)
    grad_z = along_z[..., :size_z]
    high_z = along_z[..., size_z:]
    advect = velocity[0][None] * grad_x + velocity[1][None] * grad_y + velocity[2][None] * grad_z
    new_field = velocity + time_step * (-advect - relax_rate * (high_x + high_y + high_z))
    recv_rows, recv_aims, recv_valid = in_one_piece(
        (send_rows, send_aims, send_valid), "wall", 0, 0, 1
    )
    pred, grad_one, grad_two, grad_out, features, delta_three = forward_back(
        recv_rows, recv_aims, recv_valid, k_first[0], k_second[0], w_hidden[0], w_out[0]
    )
    back = lax.all_to_all(pred, "wall", split_axis=0, concat_axis=0, tiled=True)
    stress_local = jnp.dot(select.T, back, precision=highest)
    stress = stress_local.T[:, None, :]
    share_rows = FEATS // flow_count
    dense_scale = 1.0 / math.sqrt(1.0 * FEATS)
    small = jnp.concatenate([grad_one.ravel(), grad_out.ravel()])
    tiles = features.reshape(features.shape[0], flow_count, -1).transpose(1, 0, 2)
    grad_share, small_part, columns_here = owner_sums(grad_two.reshape(-1, CH), small, tiles, STREAM)
    grad_hidden = (
        jnp.dot(
            columns_here.T,
            gathered_by_axis(delta_three, STREAM, (1, 0, 2), 0),
            preferred_element_type=jnp.float32,
        )
        * dense_scale
    )
    own_rows = lax.dynamic_slice_in_dim(w_hidden[0], flow_place * share_rows, share_rows, 0)
    new_w_hidden = row_update(own_rows, grad_hidden)[None]
    kernel_rows, small = shared_back(
        grad_share.astype(jnp.bfloat16), small_part.astype(jnp.bfloat16), STREAM
    )
    kernel_grad = kernel_rows.astype(jnp.float32).reshape(k_second.shape[1:])
    new_k_second = row_update(k_second[0], kernel_grad)
    small = small.astype(jnp.float32)
    grad_one = small[: grad_one.size].reshape(grad_one.shape)
    grad_out = small[grad_one.size : grad_one.size + grad_out.size].reshape(grad_out.shape)
    new_k_first = row_update(k_first[0], grad_one)
    new_w_out = whole_update(w_out[0], grad_out)
    return (new_field, stress, new_k_first[None], new_k_second[None], new_w_hidden, new_w_out[None])


def solution(mesh):
    torus = Mesh(
        mesh.devices.reshape(mesh.shape["wall"], 8, 2, 2),
        ("wall", "stream_0", "stream_1", "stream_2"),
    )
    in_specs = (
        P(None, "wall", STREAM, None),
        P("wall", STREAM),
        P("wall", STREAM, None),
        P("wall", None, None),
        P("wall", None, None, None),
        P("wall", None, None),
        P("wall", None, None),
    )
    out_specs = (
        P(None, "wall", STREAM, None),
        P(None, "wall", STREAM),
        P("wall", None, None),
        P("wall", None, None, None),
        P("wall", STREAM, None),
        P("wall", None, None),
    )
    return jax.shard_map(body, mesh=torus, in_specs=in_specs, out_specs=out_specs, check_vma=False)
```

```python
import math

import jax
import jax.numpy as jnp
import numpy as np
from jax import lax
from jax.sharding import Mesh
from jax.sharding import PartitionSpec as P

P_SIZE = 8
PY = 4
PX = 4
PZ = 8
CH = 64
CAP = 2
FEATS = 2048
STREAM = ("stream_0", "stream_1", "stream_2")


highest = lax.Precision.HIGHEST
time_step = 0.005
relax_rate = 20.0
viscosity = 0.3
learn_rate = 0.5
rms_eps = 1e-06
def extended(shard, sides, width):
    edges = {}
    for axis, dim in sides:
        size, length = (lax.axis_size(axis), shard.shape[dim])
        up = [(i, (i + 1) % size) for i in range(size)]
        last = lax.slice_in_dim(shard, length - width, length, axis=dim)
        first = lax.slice_in_dim(shard, 0, width, axis=dim)
        edges[dim] = (
            lax.ppermute(last, axis, up),
            lax.ppermute(first, axis, [(b, a) for a, b in up]),
        )
    done = []
    for _, dim in sides:
        low, high = edges[dim]
        around = [(width, width) if d in done else (0, 0) for d in range(shard.ndim)]
        shard = jnp.concatenate([jnp.pad(low, around), shard, jnp.pad(high, around)], axis=dim)
        done.append(dim)
    return shard


def in_one_piece(arrays, axis, split_dim, concat_dim, along):
    widths = [math.prod(a.shape[along:]) for a in arrays]
    both = jnp.concatenate(
        [a.reshape(*a.shape[:along], w) for a, w in zip(arrays, widths)], axis=along
    )
    whole = lax.all_to_all(both, axis, split_axis=split_dim, concat_axis=concat_dim, tiled=True)
    tiles = jnp.split(whole, [sum(widths[:k]) for k in range(1, len(widths))], axis=along)
    return tuple((b.reshape(*whole.shape[:along], *a.shape[along:]) for a, b in zip(arrays, tiles)))


def from_everyone(shard, axis):
    copies = jnp.broadcast_to(shard, (lax.axis_size(axis), *shard.shape))
    return lax.all_to_all(copies, axis, split_axis=0, concat_axis=0, tiled=True)


def owner_sums(rows, small, tiles, axis):
    count = lax.axis_size(axis)
    spare = -small.size % count
    small = jnp.pad(small, (0, spare))
    summed = [rows.reshape(count, -1), small.reshape(count, -1)]
    width = sum(part.shape[1] for part in summed)
    summed = [part.astype(tiles.dtype) for part in summed]
    both = jnp.concatenate(summed + [tiles.reshape(count, -1)], axis=1)
    arrived = lax.all_to_all(both, axis, split_axis=0, concat_axis=0, tiled=True)
    total = arrived[:, :width].astype(jnp.float32).sum(axis=0)
    part = rows.size // count
    moved = arrived[:, width:].astype(tiles.dtype).reshape(-1, *tiles.shape[2:])
    return total[:part].reshape(-1, rows.shape[-1]), total[part:], moved


def shared_back(rows, chunk, axis):
    everything = from_everyone(jnp.concatenate([rows.ravel(), chunk]), axis)
    whole_rows = everything[:, : rows.size].reshape(-1, rows.shape[-1])
    return whole_rows, everything[:, rows.size :].reshape(-1)


def cheb_tables(points):
    order = points - 1
    node_index = np.arange(points)
    nodes = -np.cos(np.pi * node_index / order)
    end_weight = np.where((node_index == 0) | (node_index == order), 2.0, 1.0)
    parity = (-1.0) ** (node_index[:, None] + node_index[None, :])
    offdiag = 1.0 - np.eye(points)
    spread = nodes[:, None] - nodes[None, :] + np.eye(points)
    deriv = end_weight[:, None] / end_weight[None, :] * parity / spread * offdiag
    deriv = deriv - np.eye(points) * deriv.sum(axis=1)[:, None]
    highpass = parity / (order * end_weight[None, :])
    return (deriv, highpass, 0.5 * order * order)


def axis_matrices(count, periodic):
    deriv, highpass, lift_half = cheb_tables(P_SIZE)
    length = count * P_SIZE
    slope = np.kron(np.eye(count), deriv)
    upper = np.kron(np.eye(count), highpass)
    faces = count if periodic else count - 1
    for element in range(faces):
        last_node = element * P_SIZE + P_SIZE - 1
        next_node = (element + 1) % count * P_SIZE
        slope[last_node, next_node] += lift_half
        slope[last_node, last_node] -= lift_half
        slope[next_node, last_node] -= lift_half
        slope[next_node, next_node] += lift_half
    if not periodic:
        slope[0, 0] += lift_half
        slope[length - 1, length - 1] -= lift_half
    paired = jnp.asarray(np.concatenate([slope, upper], axis=0), jnp.float32)
    return (paired, lift_half)


def slot_matrix(members, member_count):
    member_hot = (members[..., None] == jnp.arange(member_count, dtype=jnp.int32)).astype(jnp.int32)
    before = jnp.cumsum(member_hot, axis=-2) - member_hot
    ranks = jnp.sum(before * member_hot, axis=-1)
    slots = members * CAP + ranks
    return (slots[..., None, :] == jnp.arange(member_count * CAP, dtype=jnp.int32)[:, None]).astype(
        jnp.float32
    )


DIMS = ("NDHWC", "DHWIO", "NDHWC")
FILTER_DIMS = ("CDHWN", "IDHWO", "NDHWC")
SAME = ((1, 1), (1, 1), (1, 1))


def silu_slope(value):
    gate = jax.nn.sigmoid(value)
    return gate * (1.0 + value * (1.0 - gate))


def conv_taps(grid, kernel):
    return lax.conv_general_dilated(
        grid, kernel, (1, 1, 1), SAME, dimension_numbers=DIMS,
        preferred_element_type=jnp.float32,
    )


def conv_filter(grid, delta):
    taps = lax.conv_general_dilated(
        grid, delta, (1, 1, 1), SAME, dimension_numbers=FILTER_DIMS,
        preferred_element_type=jnp.float32,
    )
    return jnp.moveaxis(taps, 0, 3)


def forward_back(patches, aim_rows, valid, k_first, k_second, w_hidden, w_out):
    batch = patches.shape[0]
    channels = k_second.shape[-1]
    inputs = patches.reshape(batch, 2, PY, PX, PZ).transpose(0, 2, 3, 4, 1)
    first_taps = k_first.reshape(3, 3, 3, 2, channels)
    second_taps = k_second.reshape(3, 3, 3, channels, channels)
    scale_one = 1.0 / math.sqrt(54.0)
    scale_two = 1.0 / math.sqrt(27.0 * channels)
    scale_three = 1.0 / math.sqrt(1.0 * w_hidden.shape[0])
    scale_four = 1.0 / math.sqrt(1.0 * w_hidden.shape[1])
    pre_one = conv_taps(inputs, first_taps) * scale_one
    hidden_one = jax.nn.silu(pre_one).astype(jnp.bfloat16)
    pre_two = conv_taps(hidden_one, second_taps) * scale_two
    pooled = jax.nn.silu(pre_two).reshape(batch, PY // 2, 2, PX // 2, 2, PZ, channels).mean(axis=(2, 4))
    features = pooled.reshape(batch, -1).astype(jnp.bfloat16)
    pre_three = jnp.dot(features, w_hidden, preferred_element_type=jnp.float32) * scale_three
    hidden_three = jax.nn.silu(pre_three).astype(jnp.bfloat16)
    pred = jnp.dot(hidden_three, w_out, preferred_element_type=jnp.float32) * scale_four
    error = valid.astype(jnp.float32)[:, None] * (pred - aim_rows.astype(jnp.float32))
    grad_out = jnp.dot(hidden_three.astype(jnp.float32).T, error, precision=highest) * scale_four
    delta_three = (
        jnp.dot(error, w_out.astype(jnp.float32).T, precision=highest) * scale_four * silu_slope(pre_three)
    ).astype(jnp.bfloat16)
    back_feat = jnp.dot(delta_three, w_hidden.T, preferred_element_type=jnp.float32) * scale_three
    back_grid = back_feat.reshape(batch, PY // 2, 1, PX // 2, 1, PZ, channels)
    spread_back = jnp.broadcast_to(back_grid, (batch, PY // 2, 2, PX // 2, 2, PZ, channels)).reshape(pre_two.shape) * 0.25
    delta_two = (spread_back * silu_slope(pre_two)).astype(jnp.bfloat16)
    grad_two = (conv_filter(hidden_one, delta_two) * scale_two).reshape(27, channels, channels)
    mirrored = jnp.flip(second_taps, axis=(0, 1, 2)).swapaxes(3, 4)
    back_one = conv_taps(delta_two, mirrored)
    delta_one = (back_one * scale_two * silu_slope(pre_one)).astype(jnp.bfloat16)
    grad_one = (conv_filter(inputs, delta_one) * scale_one).reshape(54, channels)
    return (pred, grad_one, grad_two, grad_out, features, delta_three)


def row_update(weight, grad):
    scale = jnp.sqrt(jnp.mean(grad * grad, axis=-1, keepdims=True) + rms_eps)
    return weight.astype(jnp.float32) - learn_rate * grad / scale


def whole_update(weight, grad):
    scale = jnp.sqrt(jnp.mean(grad * grad) + rms_eps)
    return weight.astype(jnp.float32) - learn_rate * grad / scale


def body(velocity, sample_block, sample_member, k_first, k_second, w_hidden, w_out):
    wall_count = lax.axis_size("wall")
    wall_place = lax.axis_index("wall")
    flow_count = lax.axis_size(STREAM)
    flow_place = lax.axis_index(STREAM)
    padded = extended(velocity, (("wall", 1), (STREAM, 2)), 1)
    keep_low = (wall_place > 0).astype(jnp.float32)
    keep_high = (wall_place < wall_count - 1).astype(jnp.float32)
    below = padded[:, 0, 1:-1, :] * keep_low
    above = padded[:, -1, 1:-1, :] * keep_high
    left_face = padded[:, 1:-1, 0, :]
    right_face = padded[:, 1:-1, -1, :]
    size_y, size_x, size_z = (velocity.shape[1], velocity.shape[2], velocity.shape[3])
    pair_y, lift_half = axis_matrices(size_y // P_SIZE, False)
    pair_x, lift_same = axis_matrices(size_x // P_SIZE, False)
    pair_z, lift_again = axis_matrices(size_z // P_SIZE, True)
    along_y = jnp.einsum("cyxz,wy->cwxz", velocity, pair_y, precision=highest)
    grad_y = (
        along_y[:, :size_y]
        .at[:, 0]
        .add(-lift_half * below)
        .at[:, size_y - 1]
        .add(lift_half * above)
    )
    high_y = along_y[:, size_y:]
    rows_y, rows_x, rows_z = (size_y // PY, size_x // PX, size_z // PZ)
    tangent = jnp.stack([velocity[0], velocity[2]]).reshape(2, rows_y, PY, rows_x, PX, rows_z, PZ)
    blocks = tangent.transpose(1, 3, 5, 0, 2, 4, 6).reshape(-1, 2 * PY * PX * PZ)
    slope_wall = jnp.stack([grad_y[0], grad_y[2]]).reshape(2, rows_y, PY, rows_x, PX, rows_z, PZ)
    stress_true = (
        (viscosity * jnp.mean(slope_wall, axis=(2, 4, 6))).transpose(1, 2, 3, 0).reshape(-1, 2)
    )
    picked = sample_block.reshape(-1)
    members = sample_member.reshape(-1)
    patch_rows = jnp.take(blocks, picked, axis=0).astype(jnp.bfloat16)
    aim_rows = jnp.take(stress_true, picked, axis=0).astype(jnp.bfloat16)
    select = slot_matrix(members, wall_count)
    select_half = select.astype(jnp.bfloat16)
    send_rows = jnp.dot(select_half, patch_rows, preferred_element_type=jnp.float32).astype(
        jnp.bfloat16
    )
    send_aims = jnp.dot(select_half, aim_rows, preferred_element_type=jnp.float32).astype(
        jnp.bfloat16
    )
    send_valid = jnp.sum(select, axis=1).astype(jnp.bfloat16)
    left_face, right_face, send_rows, send_aims, send_valid = lax.optimization_barrier(
        (left_face, right_face, send_rows, send_aims, send_valid)
    )
    along_x = jnp.einsum("cyxz,wx->cywz", velocity, pair_x, precision=highest)
    grad_x = (
        along_x[:, :, :size_x]
        .at[:, :, 0]
        .add(-lift_half * left_face)
        .at[:, :, size_x - 1]
        .add(lift_half * right_face)
    )
    high_x = along_x[:, :, size_x:]
    along_z = jnp.einsum("cyxz,wz->cyxw", velocity, pair_z, precision=highest)
    grad_z = along_z[..., :size_z]
    high_z = along_z[..., size_z:]
    advect = velocity[0][None] * grad_x + velocity[1][None] * grad_y + velocity[2][None] * grad_z
    new_field = velocity + time_step * (-advect - relax_rate * (high_x + high_y + high_z))
    recv_rows, recv_aims, recv_valid = in_one_piece(
        (send_rows, send_aims, send_valid), "wall", 0, 0, 1
    )
    pred, grad_one, grad_two, grad_out, features, delta_three = forward_back(
        recv_rows, recv_aims, recv_valid, k_first[0], k_second[0], w_hidden[0], w_out[0]
    )
    back = lax.all_to_all(pred, "wall", split_axis=0, concat_axis=0, tiled=True)
    stress_local = jnp.dot(select.T, back, precision=highest)
    stress = stress_local.T[:, None, :]
    share_rows = FEATS // flow_count
    dense_scale = 1.0 / math.sqrt(1.0 * FEATS)
    small = jnp.concatenate([grad_one.ravel(), grad_out.ravel()])
    tiles = features.reshape(features.shape[0], flow_count, -1).transpose(1, 0, 2)
    grad_share, small_part, columns_here = owner_sums(grad_two.reshape(-1, CH), small, tiles, STREAM)
    gather_order = (1, 0, 2)
    stacked = delta_three
    for k in gather_order:
        stacked = lax.all_gather(stacked, STREAM[k])
    sizes = [lax.axis_size(name) for name in STREAM]
    columns_here = columns_here.reshape(*sizes, delta_three.shape[0], -1)
    columns_here = columns_here.transpose(*gather_order[::-1], 3, 4).reshape(stacked.size // FEATS, -1)
    grad_hidden = (
        jnp.dot(
            columns_here.T,
            stacked.reshape(-1, FEATS),
            preferred_element_type=jnp.float32,
        )
        * dense_scale
    )
    own_rows = lax.dynamic_slice_in_dim(w_hidden[0], flow_place * share_rows, share_rows, 0)
    new_w_hidden = row_update(own_rows, grad_hidden)[None]
    share_count = grad_share.shape[0]
    kernel_own = lax.dynamic_slice_in_dim(
        k_second[0].reshape(-1, CH), flow_place * share_count, share_count, 0
    )
    updated_rows = row_update(kernel_own, grad_share)
    kernel_rows, small = shared_back(updated_rows, small_part, STREAM)
    new_k_second = kernel_rows.reshape(k_second.shape[1:])
    grad_one = small[: grad_one.size].reshape(grad_one.shape)
    grad_out = small[grad_one.size : grad_one.size + grad_out.size].reshape(grad_out.shape)
    new_k_first = row_update(k_first[0], grad_one)
    new_w_out = whole_update(w_out[0], grad_out)
    return (new_field, stress, new_k_first[None], new_k_second[None], new_w_hidden, new_w_out[None])


def solution(mesh):
    torus = Mesh(
        mesh.devices.reshape(mesh.shape["wall"], 8, 2, 2),
        ("wall", "stream_0", "stream_1", "stream_2"),
    )
    in_specs = (
        P(None, "wall", STREAM, None),
        P("wall", STREAM),
        P("wall", STREAM, None),
        P("wall", None, None),
        P("wall", None, None, None),
        P("wall", None, None),
        P("wall", None, None),
    )
    out_specs = (
        P(None, "wall", STREAM, None),
        P(None, "wall", STREAM),
        P("wall", None, None),
        P("wall", None, None, None),
        P("wall", STREAM, None),
        P("wall", None, None),
    )
    return jax.shard_map(body, mesh=torus, in_specs=in_specs, out_specs=out_specs, check_vma=False)
```

```python
import math

import jax
import jax.numpy as jnp
import numpy as np
from jax import lax
from jax.sharding import Mesh
from jax.sharding import PartitionSpec as P

P_SIZE = 8
PY = 4
PX = 4
PZ = 8
CH = 64
CAP = 2
FEATS = 2048
STREAM = ("stream_0", "stream_1", "stream_2")


highest = lax.Precision.HIGHEST
time_step = 0.005
relax_rate = 20.0
viscosity = 0.3
learn_rate = 0.5
rms_eps = 1e-06
def extended(shard, sides, width):
    edges = {}
    for axis, dim in sides:
        size, length = (lax.axis_size(axis), shard.shape[dim])
        up = [(i, (i + 1) % size) for i in range(size)]
        last = lax.slice_in_dim(shard, length - width, length, axis=dim)
        first = lax.slice_in_dim(shard, 0, width, axis=dim)
        edges[dim] = (
            lax.ppermute(last, axis, up),
            lax.ppermute(first, axis, [(b, a) for a, b in up]),
        )
    done = []
    for _, dim in sides:
        low, high = edges[dim]
        around = [(width, width) if d in done else (0, 0) for d in range(shard.ndim)]
        shard = jnp.concatenate([jnp.pad(low, around), shard, jnp.pad(high, around)], axis=dim)
        done.append(dim)
    return shard


def in_one_piece(arrays, axis, split_dim, concat_dim, along):
    widths = [math.prod(a.shape[along:]) for a in arrays]
    both = jnp.concatenate(
        [a.reshape(*a.shape[:along], w) for a, w in zip(arrays, widths)], axis=along
    )
    whole = lax.all_to_all(both, axis, split_axis=split_dim, concat_axis=concat_dim, tiled=True)
    tiles = jnp.split(whole, [sum(widths[:k]) for k in range(1, len(widths))], axis=along)
    return tuple((b.reshape(*whole.shape[:along], *a.shape[along:]) for a, b in zip(arrays, tiles)))


def joined_along(tiles, dim):
    lengths = list(tiles.shape[1:])
    lengths[dim] *= tiles.shape[0]
    return jnp.moveaxis(tiles, 0, dim).reshape(lengths)


def gather_in_order(shard, axes, order):
    tiles = shard
    for k in order:
        tiles = lax.all_gather(tiles, axes[k])
    done = order[::-1]
    back = [done.index(k) for k in range(len(axes))]
    tiles = tiles.transpose(*back, *range(len(axes), tiles.ndim))
    return tiles.reshape(-1, *shard.shape)


def gathered_by_axis(shard, axes, order, dim):
    return joined_along(gather_in_order(shard, axes, order), dim)


def from_everyone(shard, axis):
    copies = jnp.broadcast_to(shard, (lax.axis_size(axis), *shard.shape))
    return lax.all_to_all(copies, axis, split_axis=0, concat_axis=0, tiled=True)


def owner_sums(rows, small, tiles, axis):
    count = lax.axis_size(axis)
    spare = -small.size % count
    small = jnp.pad(small, (0, spare))
    summed = [rows.reshape(count, -1), small.reshape(count, -1)]
    width = sum(part.shape[1] for part in summed)
    summed = [part.astype(tiles.dtype) for part in summed]
    both = jnp.concatenate(summed + [tiles.reshape(count, -1)], axis=1)
    arrived = lax.all_to_all(both, axis, split_axis=0, concat_axis=0, tiled=True)
    total = arrived[:, :width].astype(jnp.float32).sum(axis=0)
    part = rows.size // count
    moved = arrived[:, width:].astype(tiles.dtype).reshape(-1, *tiles.shape[2:])
    return total[:part].reshape(-1, rows.shape[-1]), total[part:], moved


def shared_back(rows, chunk, axis):
    everything = from_everyone(jnp.concatenate([rows.ravel(), chunk]), axis)
    whole_rows = everything[:, : rows.size].reshape(-1, rows.shape[-1])
    return whole_rows, everything[:, rows.size :].reshape(-1)


def cheb_tables(points):
    order = points - 1
    node_index = np.arange(points)
    nodes = -np.cos(np.pi * node_index / order)
    end_weight = np.where((node_index == 0) | (node_index == order), 2.0, 1.0)
    parity = (-1.0) ** (node_index[:, None] + node_index[None, :])
    offdiag = 1.0 - np.eye(points)
    spread = nodes[:, None] - nodes[None, :] + np.eye(points)
    deriv = end_weight[:, None] / end_weight[None, :] * parity / spread * offdiag
    deriv = deriv - np.eye(points) * deriv.sum(axis=1)[:, None]
    highpass = parity / (order * end_weight[None, :])
    return (deriv, highpass, 0.5 * order * order)


def axis_matrices(count, periodic):
    deriv, highpass, lift_half = cheb_tables(P_SIZE)
    length = count * P_SIZE
    slope = np.kron(np.eye(count), deriv)
    upper = np.kron(np.eye(count), highpass)
    faces = count if periodic else count - 1
    for element in range(faces):
        last_node = element * P_SIZE + P_SIZE - 1
        next_node = (element + 1) % count * P_SIZE
        slope[last_node, next_node] += lift_half
        slope[last_node, last_node] -= lift_half
        slope[next_node, last_node] -= lift_half
        slope[next_node, next_node] += lift_half
    if not periodic:
        slope[0, 0] += lift_half
        slope[length - 1, length - 1] -= lift_half
    paired = jnp.asarray(np.concatenate([slope, upper], axis=0), jnp.float32)
    return (paired, lift_half)


def slot_matrix(members, member_count):
    member_hot = (members[..., None] == jnp.arange(member_count, dtype=jnp.int32)).astype(jnp.int32)
    before = jnp.cumsum(member_hot, axis=-2) - member_hot
    ranks = jnp.sum(before * member_hot, axis=-1)
    slots = members * CAP + ranks
    return (slots[..., None, :] == jnp.arange(member_count * CAP, dtype=jnp.int32)[:, None]).astype(
        jnp.float32
    )


DIMS = ("NDHWC", "DHWIO", "NDHWC")
FILTER_DIMS = ("CDHWN", "IDHWO", "NDHWC")
SAME = ((1, 1), (1, 1), (1, 1))


def silu_slope(value):
    gate = jax.nn.sigmoid(value)
    return gate * (1.0 + value * (1.0 - gate))


def conv_taps(grid, kernel):
    return lax.conv_general_dilated(
        grid, kernel, (1, 1, 1), SAME, dimension_numbers=DIMS,
        preferred_element_type=jnp.float32,
    )


def conv_filter(grid, delta):
    taps = lax.conv_general_dilated(
        grid, delta, (1, 1, 1), SAME, dimension_numbers=FILTER_DIMS,
        preferred_element_type=jnp.float32,
    )
    return jnp.moveaxis(taps, 0, 3)


def forward_back(patches, aim_rows, valid, k_first, k_second, w_hidden, w_out):
    batch = patches.shape[0]
    channels = k_second.shape[-1]
    inputs = patches.reshape(batch, 2, PY, PX, PZ).transpose(0, 2, 3, 4, 1)
    first_taps = k_first.reshape(3, 3, 3, 2, channels)
    second_taps = k_second.reshape(3, 3, 3, channels, channels)
    scale_one = 1.0 / math.sqrt(54.0)
    scale_two = 1.0 / math.sqrt(27.0 * channels)
    scale_three = 1.0 / math.sqrt(1.0 * w_hidden.shape[0])
    scale_four = 1.0 / math.sqrt(1.0 * w_hidden.shape[1])
    pre_one = conv_taps(inputs, first_taps) * scale_one
    hidden_one = jax.nn.silu(pre_one).astype(jnp.bfloat16)
    pre_two = conv_taps(hidden_one, second_taps) * scale_two
    pooled = jax.nn.silu(pre_two).reshape(batch, PY // 2, 2, PX // 2, 2, PZ, channels).mean(axis=(2, 4))
    features = pooled.reshape(batch, -1).astype(jnp.bfloat16)
    pre_three = jnp.dot(features, w_hidden, preferred_element_type=jnp.float32) * scale_three
    hidden_three = jax.nn.silu(pre_three).astype(jnp.bfloat16)
    pred = jnp.dot(hidden_three, w_out, preferred_element_type=jnp.float32) * scale_four
    error = valid.astype(jnp.float32)[:, None] * (pred - aim_rows.astype(jnp.float32))
    grad_out = jnp.dot(hidden_three.astype(jnp.float32).T, error, precision=highest) * scale_four
    delta_three = (
        jnp.dot(error, w_out.astype(jnp.float32).T, precision=highest) * scale_four * silu_slope(pre_three)
    ).astype(jnp.bfloat16)
    back_feat = jnp.dot(delta_three, w_hidden.T, preferred_element_type=jnp.float32) * scale_three
    back_grid = back_feat.reshape(batch, PY // 2, 1, PX // 2, 1, PZ, channels)
    spread_back = jnp.broadcast_to(back_grid, (batch, PY // 2, 2, PX // 2, 2, PZ, channels)).reshape(pre_two.shape) * 0.25
    delta_two = (spread_back * silu_slope(pre_two)).astype(jnp.bfloat16)
    grad_two = (conv_filter(hidden_one, delta_two) * scale_two).reshape(27, channels, channels)
    mirrored = jnp.flip(second_taps, axis=(0, 1, 2)).swapaxes(3, 4)
    back_one = conv_taps(delta_two, mirrored)
    delta_one = (back_one * scale_two * silu_slope(pre_one)).astype(jnp.bfloat16)
    grad_one = (conv_filter(inputs, delta_one) * scale_one).reshape(54, channels)
    return (pred, grad_one, grad_two, grad_out, features, delta_three)


def row_update(weight, grad):
    scale = jnp.sqrt(jnp.mean(grad * grad, axis=-1, keepdims=True) + rms_eps)
    return weight.astype(jnp.float32) - learn_rate * grad / scale


def whole_update(weight, grad):
    scale = jnp.sqrt(jnp.mean(grad * grad) + rms_eps)
    return weight.astype(jnp.float32) - learn_rate * grad / scale


def body(velocity, sample_block, sample_member, k_first, k_second, w_hidden, w_out):
    wall_count = lax.axis_size("wall")
    wall_place = lax.axis_index("wall")
    flow_count = lax.axis_size(STREAM)
    flow_place = lax.axis_index(STREAM)
    padded = extended(velocity, (("wall", 1), (STREAM, 2)), 1)
    keep_low = (wall_place > 0).astype(jnp.float32)
    keep_high = (wall_place < wall_count - 1).astype(jnp.float32)
    below = padded[:, 0, 1:-1, :] * keep_low
    above = padded[:, -1, 1:-1, :] * keep_high
    left_face = padded[:, 1:-1, 0, :]
    right_face = padded[:, 1:-1, -1, :]
    size_y, size_x, size_z = (velocity.shape[1], velocity.shape[2], velocity.shape[3])
    pair_y, lift_half = axis_matrices(size_y // P_SIZE, False)
    pair_x, lift_same = axis_matrices(size_x // P_SIZE, False)
    pair_z, lift_again = axis_matrices(size_z // P_SIZE, True)
    along_y = jnp.einsum("cyxz,wy->cwxz", velocity, pair_y, precision=highest)
    grad_y = (
        along_y[:, :size_y]
        .at[:, 0]
        .add(-lift_half * below)
        .at[:, size_y - 1]
        .add(lift_half * above)
    )
    high_y = along_y[:, size_y:]
    rows_y, rows_x, rows_z = (size_y // PY, size_x // PX, size_z // PZ)
    tangent = jnp.stack([velocity[0], velocity[2]]).reshape(2, rows_y, PY, rows_x, PX, rows_z, PZ)
    blocks = tangent.transpose(1, 3, 5, 0, 2, 4, 6).reshape(-1, 2 * PY * PX * PZ)
    slope_wall = jnp.stack([grad_y[0], grad_y[2]]).reshape(2, rows_y, PY, rows_x, PX, rows_z, PZ)
    stress_true = (
        (viscosity * jnp.mean(slope_wall, axis=(2, 4, 6))).transpose(1, 2, 3, 0).reshape(-1, 2)
    )
    picked = sample_block.reshape(-1)
    members = sample_member.reshape(-1)
    patch_rows = jnp.take(blocks, picked, axis=0).astype(jnp.bfloat16)
    aim_rows = jnp.take(stress_true, picked, axis=0).astype(jnp.bfloat16)
    select = slot_matrix(members, wall_count)
    select_half = select.astype(jnp.bfloat16)
    send_rows = jnp.dot(select_half, patch_rows, preferred_element_type=jnp.float32).astype(
        jnp.bfloat16
    )
    send_aims = jnp.dot(select_half, aim_rows, preferred_element_type=jnp.float32).astype(
        jnp.bfloat16
    )
    send_valid = jnp.sum(select, axis=1).astype(jnp.bfloat16)
    left_face, right_face, send_rows, send_aims, send_valid = lax.optimization_barrier(
        (left_face, right_face, send_rows, send_aims, send_valid)
    )
    along_x = jnp.einsum("cyxz,wx->cywz", velocity, pair_x, precision=highest)
    grad_x = (
        along_x[:, :, :size_x]
        .at[:, :, 0]
        .add(-lift_half * left_face)
        .at[:, :, size_x - 1]
        .add(lift_half * right_face)
    )
    high_x = along_x[:, :, size_x:]
    along_z = jnp.einsum("cyxz,wz->cyxw", velocity, pair_z, precision=highest)
    grad_z = along_z[..., :size_z]
    high_z = along_z[..., size_z:]
    advect = velocity[0][None] * grad_x + velocity[1][None] * grad_y + velocity[2][None] * grad_z
    new_field = velocity + time_step * (-advect - relax_rate * (high_x + high_y + high_z))
    recv_rows, recv_aims, recv_valid = in_one_piece(
        (send_rows, send_aims, send_valid), "wall", 0, 0, 1
    )
    pred, grad_one, grad_two, grad_out, features, delta_three = forward_back(
        recv_rows, recv_aims, recv_valid, k_first[0], k_second[0], w_hidden[0], w_out[0]
    )
    back = lax.all_to_all(pred, "wall", split_axis=0, concat_axis=0, tiled=True)
    stress_local = jnp.dot(select.T, back, precision=highest)
    stress = stress_local.T[:, None, :]
    share_rows = FEATS // flow_count
    dense_scale = 1.0 / math.sqrt(1.0 * FEATS)
    small = jnp.concatenate([grad_one.ravel(), grad_out.ravel()])
    tiles = features.reshape(features.shape[0], flow_count, -1).transpose(1, 0, 2)
    grad_share, small_part, columns_here = owner_sums(grad_two.reshape(-1, CH), small, tiles, STREAM)
    grad_hidden = (
        jnp.dot(
            columns_here.T,
            gathered_by_axis(delta_three, STREAM, (2, 0, 1), 0),
            preferred_element_type=jnp.float32,
        )
        * dense_scale
    )
    own_rows = lax.dynamic_slice_in_dim(w_hidden[0], flow_place * share_rows, share_rows, 0)
    new_w_hidden = row_update(own_rows, grad_hidden)[None]
    share_count = grad_share.shape[0]
    kernel_own = lax.dynamic_slice_in_dim(
        k_second[0].reshape(-1, CH), flow_place * share_count, share_count, 0
    )
    updated_rows = row_update(kernel_own, grad_share)
    kernel_rows, small = shared_back(updated_rows, small_part, STREAM)
    new_k_second = kernel_rows.reshape(k_second.shape[1:])
    grad_one = small[: grad_one.size].reshape(grad_one.shape)
    grad_out = small[grad_one.size : grad_one.size + grad_out.size].reshape(grad_out.shape)
    new_k_first = row_update(k_first[0], grad_one)
    new_w_out = whole_update(w_out[0], grad_out)
    return (new_field, stress, new_k_first[None], new_k_second[None], new_w_hidden, new_w_out[None])


def solution(mesh):
    torus = Mesh(
        mesh.devices.reshape(mesh.shape["wall"], 8, 2, 2),
        ("wall", "stream_0", "stream_1", "stream_2"),
    )
    in_specs = (
        P(None, "wall", STREAM, None),
        P("wall", STREAM),
        P("wall", STREAM, None),
        P("wall", None, None),
        P("wall", None, None, None),
        P("wall", None, None),
        P("wall", None, None),
    )
    out_specs = (
        P(None, "wall", STREAM, None),
        P(None, "wall", STREAM),
        P("wall", None, None),
        P("wall", None, None, None),
        P("wall", STREAM, None),
        P("wall", None, None),
    )
    return jax.shard_map(body, mesh=torus, in_specs=in_specs, out_specs=out_specs, check_vma=False)
```

```python
import math

import jax
import jax.numpy as jnp
import numpy as np
from jax import lax
from jax.sharding import Mesh
from jax.sharding import PartitionSpec as P

P_SIZE = 8
PY = 4
PX = 4
PZ = 8
CH = 64
CAP = 2
FEATS = 2048
STREAM = ("stream_0", "stream_1", "stream_2")


highest = lax.Precision.HIGHEST
time_step = 0.005
relax_rate = 20.0
viscosity = 0.3
learn_rate = 0.5
rms_eps = 1e-06
def extended(shard, sides, width):
    edges = {}
    for axis, dim in sides:
        size, length = (lax.axis_size(axis), shard.shape[dim])
        up = [(i, (i + 1) % size) for i in range(size)]
        last = lax.slice_in_dim(shard, length - width, length, axis=dim)
        first = lax.slice_in_dim(shard, 0, width, axis=dim)
        edges[dim] = (
            lax.ppermute(last, axis, up),
            lax.ppermute(first, axis, [(b, a) for a, b in up]),
        )
    done = []
    for _, dim in sides:
        low, high = edges[dim]
        around = [(width, width) if d in done else (0, 0) for d in range(shard.ndim)]
        shard = jnp.concatenate([jnp.pad(low, around), shard, jnp.pad(high, around)], axis=dim)
        done.append(dim)
    return shard


def in_one_piece(arrays, axis, split_dim, concat_dim, along):
    widths = [math.prod(a.shape[along:]) for a in arrays]
    both = jnp.concatenate(
        [a.reshape(*a.shape[:along], w) for a, w in zip(arrays, widths)], axis=along
    )
    whole = lax.all_to_all(both, axis, split_axis=split_dim, concat_axis=concat_dim, tiled=True)
    tiles = jnp.split(whole, [sum(widths[:k]) for k in range(1, len(widths))], axis=along)
    return tuple((b.reshape(*whole.shape[:along], *a.shape[along:]) for a, b in zip(arrays, tiles)))


def joined_along(tiles, dim):
    lengths = list(tiles.shape[1:])
    lengths[dim] *= tiles.shape[0]
    return jnp.moveaxis(tiles, 0, dim).reshape(lengths)


def gather_in_order(shard, axes, order):
    tiles = shard
    for k in order:
        tiles = lax.all_gather(tiles, axes[k])
    done = order[::-1]
    back = [done.index(k) for k in range(len(axes))]
    tiles = tiles.transpose(*back, *range(len(axes), tiles.ndim))
    return tiles.reshape(-1, *shard.shape)


def gathered_by_axis(shard, axes, order, dim):
    return joined_along(gather_in_order(shard, axes, order), dim)


def from_everyone(shard, axis):
    copies = jnp.broadcast_to(shard, (lax.axis_size(axis), *shard.shape))
    return lax.all_to_all(copies, axis, split_axis=0, concat_axis=0, tiled=True)


def owner_sums(rows, small, tiles, axis):
    count = lax.axis_size(axis)
    spare = -small.size % count
    small = jnp.pad(small, (0, spare))
    summed = [rows.reshape(count, -1), small.reshape(count, -1)]
    width = sum(part.shape[1] for part in summed)
    summed = [part.astype(tiles.dtype) for part in summed]
    both = jnp.concatenate(summed + [tiles.reshape(count, -1)], axis=1)
    arrived = lax.all_to_all(both, axis, split_axis=0, concat_axis=0, tiled=True)
    total = arrived[:, :width].astype(jnp.float32).sum(axis=0)
    part = rows.size // count
    moved = arrived[:, width:].astype(tiles.dtype).reshape(-1, *tiles.shape[2:])
    return total[:part].reshape(-1, rows.shape[-1]), total[part:], moved


def shared_back(rows, chunk, axis):
    everything = from_everyone(jnp.concatenate([rows.ravel(), chunk]), axis)
    whole_rows = everything[:, : rows.size].reshape(-1, rows.shape[-1])
    return whole_rows, everything[:, rows.size :].reshape(-1)


def cheb_tables(points):
    order = points - 1
    node_index = np.arange(points)
    nodes = -np.cos(np.pi * node_index / order)
    end_weight = np.where((node_index == 0) | (node_index == order), 2.0, 1.0)
    parity = (-1.0) ** (node_index[:, None] + node_index[None, :])
    offdiag = 1.0 - np.eye(points)
    spread = nodes[:, None] - nodes[None, :] + np.eye(points)
    deriv = end_weight[:, None] / end_weight[None, :] * parity / spread * offdiag
    deriv = deriv - np.eye(points) * deriv.sum(axis=1)[:, None]
    highpass = parity / (order * end_weight[None, :])
    return (deriv, highpass, 0.5 * order * order)


def axis_matrices(count, periodic):
    deriv, highpass, lift_half = cheb_tables(P_SIZE)
    length = count * P_SIZE
    slope = np.kron(np.eye(count), deriv)
    upper = np.kron(np.eye(count), highpass)
    faces = count if periodic else count - 1
    for element in range(faces):
        last_node = element * P_SIZE + P_SIZE - 1
        next_node = (element + 1) % count * P_SIZE
        slope[last_node, next_node] += lift_half
        slope[last_node, last_node] -= lift_half
        slope[next_node, last_node] -= lift_half
        slope[next_node, next_node] += lift_half
    if not periodic:
        slope[0, 0] += lift_half
        slope[length - 1, length - 1] -= lift_half
    paired = jnp.asarray(np.concatenate([slope, upper], axis=0), jnp.float32)
    return (paired, lift_half)


def slot_matrix(members, member_count):
    member_hot = (members[..., None] == jnp.arange(member_count, dtype=jnp.int32)).astype(jnp.int32)
    before = jnp.cumsum(member_hot, axis=-2) - member_hot
    ranks = jnp.sum(before * member_hot, axis=-1)
    slots = members * CAP + ranks
    return (slots[..., None, :] == jnp.arange(member_count * CAP, dtype=jnp.int32)[:, None]).astype(
        jnp.float32
    )


DIMS = ("NDHWC", "DHWIO", "NDHWC")
FILTER_DIMS = ("CDHWN", "IDHWO", "NDHWC")
SAME = ((1, 1), (1, 1), (1, 1))


def silu_slope(value):
    gate = jax.nn.sigmoid(value)
    return gate * (1.0 + value * (1.0 - gate))


def conv_taps(grid, kernel):
    return lax.conv_general_dilated(
        grid, kernel, (1, 1, 1), SAME, dimension_numbers=DIMS,
        preferred_element_type=jnp.float32,
    )


def conv_filter(grid, delta):
    taps = lax.conv_general_dilated(
        grid, delta, (1, 1, 1), SAME, dimension_numbers=FILTER_DIMS,
        preferred_element_type=jnp.float32,
    )
    return jnp.moveaxis(taps, 0, 3)


def forward_back(patches, aim_rows, valid, k_first, k_second, w_hidden, w_out):
    batch = patches.shape[0]
    channels = k_second.shape[-1]
    inputs = patches.reshape(batch, 2, PY, PX, PZ).transpose(0, 2, 3, 4, 1)
    first_taps = k_first.reshape(3, 3, 3, 2, channels)
    second_taps = k_second.reshape(3, 3, 3, channels, channels)
    scale_one = 1.0 / math.sqrt(54.0)
    scale_two = 1.0 / math.sqrt(27.0 * channels)
    scale_three = 1.0 / math.sqrt(1.0 * w_hidden.shape[0])
    scale_four = 1.0 / math.sqrt(1.0 * w_hidden.shape[1])
    pre_one = conv_taps(inputs, first_taps) * scale_one
    hidden_one = jax.nn.silu(pre_one).astype(jnp.bfloat16)
    pre_two = conv_taps(hidden_one, second_taps) * scale_two
    pooled = jax.nn.silu(pre_two).reshape(batch, PY // 2, 2, PX // 2, 2, PZ, channels).mean(axis=(2, 4))
    features = pooled.reshape(batch, -1).astype(jnp.bfloat16)
    pre_three = jnp.dot(features, w_hidden, preferred_element_type=jnp.float32) * scale_three
    hidden_three = jax.nn.silu(pre_three).astype(jnp.bfloat16)
    pred = jnp.dot(hidden_three, w_out, preferred_element_type=jnp.float32) * scale_four
    error = valid.astype(jnp.float32)[:, None] * (pred - aim_rows.astype(jnp.float32))
    grad_out = jnp.dot(hidden_three.astype(jnp.float32).T, error, precision=highest) * scale_four
    delta_three = (
        jnp.dot(error, w_out.astype(jnp.float32).T, precision=highest) * scale_four * silu_slope(pre_three)
    ).astype(jnp.bfloat16)
    back_feat = jnp.dot(delta_three, w_hidden.T, preferred_element_type=jnp.float32) * scale_three
    back_grid = back_feat.reshape(batch, PY // 2, 1, PX // 2, 1, PZ, channels)
    spread_back = jnp.broadcast_to(back_grid, (batch, PY // 2, 2, PX // 2, 2, PZ, channels)).reshape(pre_two.shape) * 0.25
    delta_two = (spread_back * silu_slope(pre_two)).astype(jnp.bfloat16)
    grad_two = (conv_filter(hidden_one, delta_two) * scale_two).reshape(27, channels, channels)
    mirrored = jnp.flip(second_taps, axis=(0, 1, 2)).swapaxes(3, 4)
    back_one = conv_taps(delta_two, mirrored)
    delta_one = (back_one * scale_two * silu_slope(pre_one)).astype(jnp.bfloat16)
    grad_one = (conv_filter(inputs, delta_one) * scale_one).reshape(54, channels)
    return (pred, grad_one, grad_two, grad_out, features, delta_three)


def row_update(weight, grad):
    scale = jnp.sqrt(jnp.mean(grad * grad, axis=-1, keepdims=True) + rms_eps)
    return weight.astype(jnp.float32) - learn_rate * grad / scale


def whole_update(weight, grad):
    scale = jnp.sqrt(jnp.mean(grad * grad) + rms_eps)
    return weight.astype(jnp.float32) - learn_rate * grad / scale


def body(velocity, sample_block, sample_member, k_first, k_second, w_hidden, w_out):
    wall_count = lax.axis_size("wall")
    wall_place = lax.axis_index("wall")
    flow_count = lax.axis_size(STREAM)
    flow_place = lax.axis_index(STREAM)
    padded = extended(velocity, (("wall", 1), (STREAM, 2)), 1)
    keep_low = (wall_place > 0).astype(jnp.float32)
    keep_high = (wall_place < wall_count - 1).astype(jnp.float32)
    below = padded[:, 0, 1:-1, :] * keep_low
    above = padded[:, -1, 1:-1, :] * keep_high
    left_face = padded[:, 1:-1, 0, :]
    right_face = padded[:, 1:-1, -1, :]
    size_y, size_x, size_z = (velocity.shape[1], velocity.shape[2], velocity.shape[3])
    pair_y, lift_half = axis_matrices(size_y // P_SIZE, False)
    pair_x, lift_same = axis_matrices(size_x // P_SIZE, False)
    pair_z, lift_again = axis_matrices(size_z // P_SIZE, True)
    along_y = jnp.einsum("cyxz,wy->cwxz", velocity, pair_y, precision=highest)
    grad_y = (
        along_y[:, :size_y]
        .at[:, 0]
        .add(-lift_half * below)
        .at[:, size_y - 1]
        .add(lift_half * above)
    )
    high_y = along_y[:, size_y:]
    rows_y, rows_x, rows_z = (size_y // PY, size_x // PX, size_z // PZ)
    tangent = jnp.stack([velocity[0], velocity[2]]).reshape(2, rows_y, PY, rows_x, PX, rows_z, PZ)
    blocks = tangent.transpose(1, 3, 5, 0, 2, 4, 6).reshape(-1, 2 * PY * PX * PZ)
    slope_wall = jnp.stack([grad_y[0], grad_y[2]]).reshape(2, rows_y, PY, rows_x, PX, rows_z, PZ)
    stress_true = (
        (viscosity * jnp.mean(slope_wall, axis=(2, 4, 6))).transpose(1, 2, 3, 0).reshape(-1, 2)
    )
    picked = sample_block.reshape(-1)
    members = sample_member.reshape(-1)
    patch_rows = jnp.take(blocks, picked, axis=0).astype(jnp.bfloat16)
    aim_rows = jnp.take(stress_true, picked, axis=0).astype(jnp.bfloat16)
    select = slot_matrix(members, wall_count)
    select_half = select.astype(jnp.bfloat16)
    send_rows = jnp.dot(select_half, patch_rows, preferred_element_type=jnp.float32).astype(
        jnp.bfloat16
    )
    send_aims = jnp.dot(select_half, aim_rows, preferred_element_type=jnp.float32).astype(
        jnp.bfloat16
    )
    send_valid = jnp.sum(select, axis=1).astype(jnp.bfloat16)
    left_face, right_face, send_rows, send_aims, send_valid = lax.optimization_barrier(
        (left_face, right_face, send_rows, send_aims, send_valid)
    )
    along_x = jnp.einsum("cyxz,wx->cywz", velocity, pair_x, precision=highest)
    grad_x = (
        along_x[:, :, :size_x]
        .at[:, :, 0]
        .add(-lift_half * left_face)
        .at[:, :, size_x - 1]
        .add(lift_half * right_face)
    )
    high_x = along_x[:, :, size_x:]
    along_z = jnp.einsum("cyxz,wz->cyxw", velocity, pair_z, precision=highest)
    grad_z = along_z[..., :size_z]
    high_z = along_z[..., size_z:]
    advect = velocity[0][None] * grad_x + velocity[1][None] * grad_y + velocity[2][None] * grad_z
    new_field = velocity + time_step * (-advect - relax_rate * (high_x + high_y + high_z))
    recv_rows, recv_aims, recv_valid = in_one_piece(
        (send_rows, send_aims, send_valid), "wall", 0, 0, 1
    )
    pred, grad_one, grad_two, grad_out, features, delta_three = forward_back(
        recv_rows, recv_aims, recv_valid, k_first[0], k_second[0], w_hidden[0], w_out[0]
    )
    back = lax.all_to_all(pred, "wall", split_axis=0, concat_axis=0, tiled=True)
    back, grad_one, grad_two, grad_out = lax.optimization_barrier((back, grad_one, grad_two, grad_out))
    stress_local = jnp.dot(select.T, back, precision=highest)
    stress = stress_local.T[:, None, :]
    share_rows = FEATS // flow_count
    dense_scale = 1.0 / math.sqrt(1.0 * FEATS)
    small = jnp.concatenate([grad_one.ravel(), grad_out.ravel()])
    tiles = features.reshape(features.shape[0], flow_count, -1).transpose(1, 0, 2)
    grad_share, small_part, columns_here = owner_sums(grad_two.reshape(-1, CH), small, tiles, STREAM)
    grad_hidden = (
        jnp.dot(
            columns_here.T,
            gathered_by_axis(delta_three, STREAM, (1, 0, 2), 0),
            preferred_element_type=jnp.float32,
        )
        * dense_scale
    )
    own_rows = lax.dynamic_slice_in_dim(w_hidden[0], flow_place * share_rows, share_rows, 0)
    new_w_hidden = row_update(own_rows, grad_hidden)[None]
    share_count = grad_share.shape[0]
    kernel_own = lax.dynamic_slice_in_dim(
        k_second[0].reshape(-1, CH), flow_place * share_count, share_count, 0
    )
    updated_rows = row_update(kernel_own, grad_share)
    kernel_rows, small = shared_back(updated_rows, small_part, STREAM)
    new_k_second = kernel_rows.reshape(k_second.shape[1:])
    grad_one = small[: grad_one.size].reshape(grad_one.shape)
    grad_out = small[grad_one.size : grad_one.size + grad_out.size].reshape(grad_out.shape)
    new_k_first = row_update(k_first[0], grad_one)
    new_w_out = whole_update(w_out[0], grad_out)
    return (new_field, stress, new_k_first[None], new_k_second[None], new_w_hidden, new_w_out[None])


def solution(mesh):
    torus = Mesh(
        mesh.devices.reshape(mesh.shape["wall"], 8, 2, 2),
        ("wall", "stream_0", "stream_1", "stream_2"),
    )
    in_specs = (
        P(None, "wall", STREAM, None),
        P("wall", STREAM),
        P("wall", STREAM, None),
        P("wall", None, None),
        P("wall", None, None, None),
        P("wall", None, None),
        P("wall", None, None),
    )
    out_specs = (
        P(None, "wall", STREAM, None),
        P(None, "wall", STREAM),
        P("wall", None, None),
        P("wall", None, None, None),
        P("wall", STREAM, None),
        P("wall", None, None),
    )
    return jax.shard_map(body, mesh=torus, in_specs=in_specs, out_specs=out_specs, check_vma=False)
```

```python
import math

import jax
import jax.numpy as jnp
import numpy as np
from jax import lax
from jax.sharding import Mesh
from jax.sharding import PartitionSpec as P

P_SIZE = 8
PY = 4
PX = 4
PZ = 8
CH = 64
CAP = 2
FEATS = 2048
STREAM = ("stream_0", "stream_1", "stream_2")


highest = lax.Precision.HIGHEST
time_step = 0.005
relax_rate = 20.0
viscosity = 0.3
learn_rate = 0.5
rms_eps = 1e-06
def extended(shard, sides, width):
    edges = {}
    for axis, dim in sides:
        size, length = (lax.axis_size(axis), shard.shape[dim])
        up = [(i, (i + 1) % size) for i in range(size)]
        last = lax.slice_in_dim(shard, length - width, length, axis=dim)
        first = lax.slice_in_dim(shard, 0, width, axis=dim)
        edges[dim] = (
            lax.ppermute(last, axis, up),
            lax.ppermute(first, axis, [(b, a) for a, b in up]),
        )
    done = []
    for _, dim in sides:
        low, high = edges[dim]
        around = [(width, width) if d in done else (0, 0) for d in range(shard.ndim)]
        shard = jnp.concatenate([jnp.pad(low, around), shard, jnp.pad(high, around)], axis=dim)
        done.append(dim)
    return shard


def in_one_piece(arrays, axis, split_dim, concat_dim, along):
    widths = [math.prod(a.shape[along:]) for a in arrays]
    both = jnp.concatenate(
        [a.reshape(*a.shape[:along], w) for a, w in zip(arrays, widths)], axis=along
    )
    whole = lax.all_to_all(both, axis, split_axis=split_dim, concat_axis=concat_dim, tiled=True)
    tiles = jnp.split(whole, [sum(widths[:k]) for k in range(1, len(widths))], axis=along)
    return tuple((b.reshape(*whole.shape[:along], *a.shape[along:]) for a, b in zip(arrays, tiles)))


def joined_along(tiles, dim):
    lengths = list(tiles.shape[1:])
    lengths[dim] *= tiles.shape[0]
    return jnp.moveaxis(tiles, 0, dim).reshape(lengths)


def gather_in_order(shard, axes, order):
    tiles = shard
    for k in order:
        tiles = lax.all_gather(tiles, axes[k])
    done = order[::-1]
    back = [done.index(k) for k in range(len(axes))]
    tiles = tiles.transpose(*back, *range(len(axes), tiles.ndim))
    return tiles.reshape(-1, *shard.shape)


def gathered_by_axis(shard, axes, order, dim):
    return joined_along(gather_in_order(shard, axes, order), dim)


def from_everyone(shard, axis):
    copies = jnp.broadcast_to(shard, (lax.axis_size(axis), *shard.shape))
    return lax.all_to_all(copies, axis, split_axis=0, concat_axis=0, tiled=True)


def owner_sums(rows, small, tiles, axis):
    count = lax.axis_size(axis)
    spare = -small.size % count
    small = jnp.pad(small, (0, spare))
    summed = [rows.reshape(count, -1), small.reshape(count, -1)]
    width = sum(part.shape[1] for part in summed)
    summed = [part.astype(tiles.dtype) for part in summed]
    both = jnp.concatenate(summed + [tiles.reshape(count, -1)], axis=1)
    arrived = lax.all_to_all(both, axis, split_axis=0, concat_axis=0, tiled=True)
    total = arrived[:, :width].astype(jnp.float32).sum(axis=0)
    part = rows.size // count
    moved = arrived[:, width:].astype(tiles.dtype).reshape(-1, *tiles.shape[2:])
    return total[:part].reshape(-1, rows.shape[-1]), total[part:], moved


def shared_back(rows, chunk, axis):
    everything = from_everyone(jnp.concatenate([rows.ravel(), chunk]), axis)
    whole_rows = everything[:, : rows.size].reshape(-1, rows.shape[-1])
    return whole_rows, everything[:, rows.size :].reshape(-1)


def cheb_tables(points):
    order = points - 1
    node_index = np.arange(points)
    nodes = -np.cos(np.pi * node_index / order)
    end_weight = np.where((node_index == 0) | (node_index == order), 2.0, 1.0)
    parity = (-1.0) ** (node_index[:, None] + node_index[None, :])
    offdiag = 1.0 - np.eye(points)
    spread = nodes[:, None] - nodes[None, :] + np.eye(points)
    deriv = end_weight[:, None] / end_weight[None, :] * parity / spread * offdiag
    deriv = deriv - np.eye(points) * deriv.sum(axis=1)[:, None]
    highpass = parity / (order * end_weight[None, :])
    return (deriv, highpass, 0.5 * order * order)


def axis_matrices(count, periodic):
    deriv, highpass, lift_half = cheb_tables(P_SIZE)
    length = count * P_SIZE
    slope = np.kron(np.eye(count), deriv)
    upper = np.kron(np.eye(count), highpass)
    faces = count if periodic else count - 1
    for element in range(faces):
        last_node = element * P_SIZE + P_SIZE - 1
        next_node = (element + 1) % count * P_SIZE
        slope[last_node, next_node] += lift_half
        slope[last_node, last_node] -= lift_half
        slope[next_node, last_node] -= lift_half
        slope[next_node, next_node] += lift_half
    if not periodic:
        slope[0, 0] += lift_half
        slope[length - 1, length - 1] -= lift_half
    paired = jnp.asarray(np.concatenate([slope, upper], axis=0), jnp.float32)
    return (paired, lift_half)


def slot_matrix(members, member_count):
    member_hot = (members[..., None] == jnp.arange(member_count, dtype=jnp.int32)).astype(jnp.int32)
    before = jnp.cumsum(member_hot, axis=-2) - member_hot
    ranks = jnp.sum(before * member_hot, axis=-1)
    slots = members * CAP + ranks
    return (slots[..., None, :] == jnp.arange(member_count * CAP, dtype=jnp.int32)[:, None]).astype(
        jnp.float32
    )


DIMS = ("NDHWC", "DHWIO", "NDHWC")
FILTER_DIMS = ("CDHWN", "IDHWO", "NDHWC")
SAME = ((1, 1), (1, 1), (1, 1))


def silu_slope(value):
    gate = jax.nn.sigmoid(value)
    return gate * (1.0 + value * (1.0 - gate))


def conv_taps(grid, kernel):
    return lax.conv_general_dilated(
        grid, kernel, (1, 1, 1), SAME, dimension_numbers=DIMS,
        preferred_element_type=jnp.float32,
    )


def conv_filter(grid, delta):
    taps = lax.conv_general_dilated(
        grid, delta, (1, 1, 1), SAME, dimension_numbers=FILTER_DIMS,
        preferred_element_type=jnp.float32,
    )
    return jnp.moveaxis(taps, 0, 3)


def forward_back(patches, aim_rows, valid, k_first, k_second, w_hidden, w_out, early):
    batch = patches.shape[0]
    channels = k_second.shape[-1]
    inputs = patches.reshape(batch, 2, PY, PX, PZ).transpose(0, 2, 3, 4, 1)
    first_taps = k_first.reshape(3, 3, 3, 2, channels)
    second_taps = k_second.reshape(3, 3, 3, channels, channels)
    scale_one = 1.0 / math.sqrt(54.0)
    scale_two = 1.0 / math.sqrt(27.0 * channels)
    scale_three = 1.0 / math.sqrt(1.0 * w_hidden.shape[0])
    scale_four = 1.0 / math.sqrt(1.0 * w_hidden.shape[1])
    pre_one = conv_taps(inputs, first_taps) * scale_one
    hidden_one = jax.nn.silu(pre_one).astype(jnp.bfloat16)
    pre_two = conv_taps(hidden_one, second_taps) * scale_two
    pooled = jax.nn.silu(pre_two).reshape(batch, PY // 2, 2, PX // 2, 2, PZ, channels).mean(axis=(2, 4))
    features = pooled.reshape(batch, -1).astype(jnp.bfloat16)
    pre_three = jnp.dot(features, w_hidden, preferred_element_type=jnp.float32) * scale_three
    hidden_three = jax.nn.silu(pre_three).astype(jnp.bfloat16)
    pred = jnp.dot(hidden_three, w_out, preferred_element_type=jnp.float32) * scale_four
    error = valid.astype(jnp.float32)[:, None] * (pred - aim_rows.astype(jnp.float32))
    grad_out = jnp.dot(hidden_three.astype(jnp.float32).T, error, precision=highest) * scale_four
    delta_three = (
        jnp.dot(error, w_out.astype(jnp.float32).T, precision=highest) * scale_four * silu_slope(pre_three)
    ).astype(jnp.bfloat16)
    delta_three, sent = lax.optimization_barrier((delta_three, early(pred)))
    back_feat = jnp.dot(delta_three, w_hidden.T, preferred_element_type=jnp.float32) * scale_three
    back_grid = back_feat.reshape(batch, PY // 2, 1, PX // 2, 1, PZ, channels)
    spread_back = jnp.broadcast_to(back_grid, (batch, PY // 2, 2, PX // 2, 2, PZ, channels)).reshape(pre_two.shape) * 0.25
    delta_two = (spread_back * silu_slope(pre_two)).astype(jnp.bfloat16)
    grad_two = (conv_filter(hidden_one, delta_two) * scale_two).reshape(27, channels, channels)
    mirrored = jnp.flip(second_taps, axis=(0, 1, 2)).swapaxes(3, 4)
    back_one = conv_taps(delta_two, mirrored)
    delta_one = (back_one * scale_two * silu_slope(pre_one)).astype(jnp.bfloat16)
    grad_one = (conv_filter(inputs, delta_one) * scale_one).reshape(54, channels)
    return (sent, grad_one, grad_two, grad_out, features, delta_three)


def row_update(weight, grad):
    scale = jnp.sqrt(jnp.mean(grad * grad, axis=-1, keepdims=True) + rms_eps)
    return weight.astype(jnp.float32) - learn_rate * grad / scale


def whole_update(weight, grad):
    scale = jnp.sqrt(jnp.mean(grad * grad) + rms_eps)
    return weight.astype(jnp.float32) - learn_rate * grad / scale


def body(velocity, sample_block, sample_member, k_first, k_second, w_hidden, w_out):
    wall_count = lax.axis_size("wall")
    wall_place = lax.axis_index("wall")
    flow_count = lax.axis_size(STREAM)
    flow_place = lax.axis_index(STREAM)
    padded = extended(velocity, (("wall", 1), (STREAM, 2)), 1)
    keep_low = (wall_place > 0).astype(jnp.float32)
    keep_high = (wall_place < wall_count - 1).astype(jnp.float32)
    below = padded[:, 0, 1:-1, :] * keep_low
    above = padded[:, -1, 1:-1, :] * keep_high
    left_face = padded[:, 1:-1, 0, :]
    right_face = padded[:, 1:-1, -1, :]
    size_y, size_x, size_z = (velocity.shape[1], velocity.shape[2], velocity.shape[3])
    pair_y, lift_half = axis_matrices(size_y // P_SIZE, False)
    pair_x, lift_same = axis_matrices(size_x // P_SIZE, False)
    pair_z, lift_again = axis_matrices(size_z // P_SIZE, True)
    along_y = jnp.einsum("cyxz,wy->cwxz", velocity, pair_y, precision=highest)
    grad_y = (
        along_y[:, :size_y]
        .at[:, 0]
        .add(-lift_half * below)
        .at[:, size_y - 1]
        .add(lift_half * above)
    )
    high_y = along_y[:, size_y:]
    rows_y, rows_x, rows_z = (size_y // PY, size_x // PX, size_z // PZ)
    tangent = jnp.stack([velocity[0], velocity[2]]).reshape(2, rows_y, PY, rows_x, PX, rows_z, PZ)
    blocks = tangent.transpose(1, 3, 5, 0, 2, 4, 6).reshape(-1, 2 * PY * PX * PZ)
    slope_wall = jnp.stack([grad_y[0], grad_y[2]]).reshape(2, rows_y, PY, rows_x, PX, rows_z, PZ)
    stress_true = (
        (viscosity * jnp.mean(slope_wall, axis=(2, 4, 6))).transpose(1, 2, 3, 0).reshape(-1, 2)
    )
    picked = sample_block.reshape(-1)
    members = sample_member.reshape(-1)
    patch_rows = jnp.take(blocks, picked, axis=0).astype(jnp.bfloat16)
    aim_rows = jnp.take(stress_true, picked, axis=0).astype(jnp.bfloat16)
    select = slot_matrix(members, wall_count)
    select_half = select.astype(jnp.bfloat16)
    send_rows = jnp.dot(select_half, patch_rows, preferred_element_type=jnp.float32).astype(
        jnp.bfloat16
    )
    send_aims = jnp.dot(select_half, aim_rows, preferred_element_type=jnp.float32).astype(
        jnp.bfloat16
    )
    send_valid = jnp.sum(select, axis=1).astype(jnp.bfloat16)
    left_face, right_face, send_rows, send_aims, send_valid = lax.optimization_barrier(
        (left_face, right_face, send_rows, send_aims, send_valid)
    )
    along_x = jnp.einsum("cyxz,wx->cywz", velocity, pair_x, precision=highest)
    grad_x = (
        along_x[:, :, :size_x]
        .at[:, :, 0]
        .add(-lift_half * left_face)
        .at[:, :, size_x - 1]
        .add(lift_half * right_face)
    )
    high_x = along_x[:, :, size_x:]
    along_z = jnp.einsum("cyxz,wz->cyxw", velocity, pair_z, precision=highest)
    grad_z = along_z[..., :size_z]
    high_z = along_z[..., size_z:]
    advect = velocity[0][None] * grad_x + velocity[1][None] * grad_y + velocity[2][None] * grad_z
    new_field = velocity + time_step * (-advect - relax_rate * (high_x + high_y + high_z))
    recv_rows, recv_aims, recv_valid = in_one_piece(
        (send_rows, send_aims, send_valid), "wall", 0, 0, 1
    )
    pred, grad_one, grad_two, grad_out, features, delta_three = forward_back(
        recv_rows, recv_aims, recv_valid, k_first[0], k_second[0], w_hidden[0], w_out[0],
        lambda pred: lax.all_to_all(pred, "wall", split_axis=0, concat_axis=0, tiled=True),
    )
    back = pred
    stress_local = jnp.dot(select.T, back, precision=highest)
    stress = stress_local.T[:, None, :]
    share_rows = FEATS // flow_count
    dense_scale = 1.0 / math.sqrt(1.0 * FEATS)
    small = jnp.concatenate([grad_one.ravel(), grad_out.ravel()])
    tiles = features.reshape(features.shape[0], flow_count, -1).transpose(1, 0, 2)
    grad_share, small_part, columns_here = owner_sums(grad_two.reshape(-1, CH), small, tiles, STREAM)
    grad_hidden = (
        jnp.dot(
            columns_here.T,
            gathered_by_axis(delta_three, STREAM, (1, 0, 2), 0),
            preferred_element_type=jnp.float32,
        )
        * dense_scale
    )
    own_rows = lax.dynamic_slice_in_dim(w_hidden[0], flow_place * share_rows, share_rows, 0)
    new_w_hidden = row_update(own_rows, grad_hidden)[None]
    share_count = grad_share.shape[0]
    kernel_own = lax.dynamic_slice_in_dim(
        k_second[0].reshape(-1, CH), flow_place * share_count, share_count, 0
    )
    updated_rows = row_update(kernel_own, grad_share)
    kernel_rows, small = shared_back(updated_rows, small_part, STREAM)
    new_k_second = kernel_rows.reshape(k_second.shape[1:])
    grad_one = small[: grad_one.size].reshape(grad_one.shape)
    grad_out = small[grad_one.size : grad_one.size + grad_out.size].reshape(grad_out.shape)
    new_k_first = row_update(k_first[0], grad_one)
    new_w_out = whole_update(w_out[0], grad_out)
    return (new_field, stress, new_k_first[None], new_k_second[None], new_w_hidden, new_w_out[None])


def solution(mesh):
    torus = Mesh(
        mesh.devices.reshape(mesh.shape["wall"], 8, 2, 2),
        ("wall", "stream_0", "stream_1", "stream_2"),
    )
    in_specs = (
        P(None, "wall", STREAM, None),
        P("wall", STREAM),
        P("wall", STREAM, None),
        P("wall", None, None),
        P("wall", None, None, None),
        P("wall", None, None),
        P("wall", None, None),
    )
    out_specs = (
        P(None, "wall", STREAM, None),
        P(None, "wall", STREAM),
        P("wall", None, None),
        P("wall", None, None, None),
        P("wall", STREAM, None),
        P("wall", None, None),
    )
    return jax.shard_map(body, mesh=torus, in_specs=in_specs, out_specs=out_specs, check_vma=False)
```
